32 devices in a mesh: row: 8 (over y, x, core), col: 4 (over z).
Axes of the slice: x: 2, y: 2, z: 4, core: 2. Of those that a mesh axis runs over, the one named last changes fastest.
Arguments:
- records: float32 [128, 6, 8192], P(('row', 'col')), may hold values from -6 to 6
- fir_taps: float32 [32], replicated, may hold values from -1 to 1
- lag_limit: int32 [128], P('row'), may hold values from 16 to 64
Outputs:
- corr: float32 [128, 4, 32, 128], P('row', 'col')
The draws below stay inside these ranges and needn't reach their ends.
Inputs may be any that keep to these rules, and one draw needn't show every extreme that they name: lag_limit[i] is the largest lag offset |l - 64| kept for reference station i.
All inputs are finite; a program needn't handle non-finite values.
Results may differ from the reference program's by a relative error of at most 0.0031.
Values may be sent and summed in bfloat16 or wider, within the bound.
No kernel may reach another device: no remote copies, remote signals or barrier semaphores. Data moves between devices by JAX's collectives and lax.ppermute only.
A program may use at most 64 MiB of HBM per device.

```python
import math
import jax
import jax.numpy as jnp
from jax import lax

BLK = 4
NWIN = 6
NS = 8192
DECIM = 2
TAPS = 32
LAGS = 128
BAND = 64
LH = 64
STATIONS = 128
N_ROW = 8
N_COL = 4


def with_ends(values, own_key, least, top_value):
    shape = values.shape
    index_at = [jax.random.randint(jax.random.fold_in(own_key, axis), (), 0, shape[axis]) for axis in range(len(shape))]
    values = values.at[tuple(index_at)].set(least)
    longest = shape.index(max(shape))
    index_at[longest] = (index_at[longest] + 1) % shape[longest]
    return values.at[tuple(index_at)].set(top_value)


def level_of(stream_key, extent, shards, low, high):
    def one(position, parts):
        heights = jax.random.uniform(jax.random.fold_in(jax.random.fold_in(stream_key, 6), position), (parts,), jnp.float32, low / len(shards), high / len(shards))
        return jnp.repeat(jnp.exp(heights), extent[position] // parts).reshape((-1,) + (1,) * (len(extent) - position - 1))

    factor_of = one(*shards[0])
    for cut in shards[1:]:
        factor_of = factor_of * one(*cut)
    return factor_of


def noise(own_key, extent, spread, bound, shards=(), kind=jnp.bfloat16):
    drawn = jax.random.normal(own_key, extent, jnp.float32) * spread
    if len(shards) > 0:
        drawn = level_of(own_key, extent, shards, -0.22, 0.18) * drawn
    return jnp.clip(drawn, min=-bound, max=bound).astype(kind)


def setup_inputs(seed: int = 0) -> dict:
    key_list = jax.random.split(jax.random.key(seed), 4)
    return {
        "records": noise(key_list[0], (STATIONS, NWIN, NS), 1.0, 6.0, ((0, 32),), jnp.float32),
        "fir_taps": noise(key_list[1], (TAPS,), TAPS ** -0.5, 1.0, (), jnp.float32),
        "lag_limit": with_ends(jax.random.randint(key_list[2], (STATIONS,), LH // 4, LH + 1), jax.random.fold_in(key_list[2], 1), LH // 4, LH).astype(jnp.int32),
    }


def angle_table(row_count, col_count, period, offset):
    row_ids = jnp.arange(row_count, dtype=jnp.int32)[:, None] + offset
    col_ids = jnp.arange(col_count, dtype=jnp.int32)[None, :]
    phase_int = jnp.mod(row_ids * col_ids, period)
    angles = phase_int.astype(jnp.float32) * (2.0 * math.pi / period)
    return (jnp.cos(angles), jnp.sin(angles))

def decimate(records, fir_taps):
    tap_count = fir_taps.shape[0]
    out_block = 128
    in_block = DECIM * out_block
    lead_dims = records.shape[:2]
    block_count = records.shape[2] // in_block
    blocks = records.reshape(lead_dims + (block_count, in_block))
    tails = blocks[:, :, :-1, in_block - tap_count:]
    tails = jnp.concatenate([jnp.zeros(lead_dims + (1, tap_count), records.dtype), tails], axis=2)
    windows = jnp.concatenate([tails, blocks], axis=3)
    tap_ids = jnp.arange(tap_count, dtype=jnp.int32)[:, None, None]
    in_ids = jnp.arange(in_block + tap_count, dtype=jnp.int32)[None, :, None]
    out_ids = jnp.arange(out_block, dtype=jnp.int32)[None, None, :]
    onehot = (in_ids == DECIM * out_ids + tap_count - tap_ids).astype(jnp.float32)
    band_matrix = jnp.einsum('k,kij->ij', fir_taps, onehot, precision=lax.Precision.HIGHEST)
    summed = jnp.einsum('swbi,ij->swbj', windows, band_matrix, precision=lax.Precision.HIGHEST)
    return summed.reshape(lead_dims + (block_count * out_block,))

def whiten(spec_real, spec_imag):
    lead_dims = spec_real.shape[:-1]
    bin_count = spec_real.shape[-1]
    banded = lead_dims + (bin_count // BAND, BAND)
    squares = (spec_real * spec_real + spec_imag * spec_imag).reshape(banded)
    band_power = lax.optimization_barrier(jnp.mean(squares, axis=-1, keepdims=True))
    inverse = 1.0 / jnp.sqrt(band_power + 1e-06)
    white_real = (spec_real.reshape(banded) * inverse).reshape(spec_real.shape)
    white_imag = (spec_imag.reshape(banded) * inverse).reshape(spec_imag.shape)
    return jnp.concatenate([white_real, white_imag], axis=-1).astype(jnp.bfloat16)

def reference(records, fir_taps, lag_limit):
    decimated = decimate(records, fir_taps)
    out_length = decimated.shape[-1]
    bin_count = out_length // 2
    spectra = jnp.fft.rfft(decimated, axis=-1)[..., :bin_count]
    white = whiten(jnp.real(spectra).astype(jnp.float32), jnp.imag(spectra).astype(jnp.float32))
    cos_lag, sin_lag = angle_table(LAGS, bin_count, out_length, -LH)
    lag_table = jnp.concatenate([cos_lag.T, sin_lag.T], axis=0).astype(jnp.bfloat16)
    norm_scale = 1.0 / math.sqrt(NWIN * bin_count)
    lag_offset = jnp.abs(jnp.arange(LAGS, dtype=jnp.int32) - LH)
    keep_mask = lag_offset[None, :] <= lag_limit[:, None]
    group_size = 16
    visiting = white.reshape(STATIONS // group_size, group_size, NWIN, 2 * bin_count)

    def one_group(sub_block):
        cross_real = jnp.zeros((STATIONS, group_size, bin_count), jnp.float32)
        cross_imag = jnp.zeros((STATIONS, group_size, bin_count), jnp.float32)
        for window in range(NWIN):
            left_c = white[:, window, :bin_count].astype(jnp.float32)[:, None, :]
            left_d = white[:, window, bin_count:].astype(jnp.float32)[:, None, :]
            vis_c = sub_block[:, window, :bin_count].astype(jnp.float32)[None]
            vis_d = sub_block[:, window, bin_count:].astype(jnp.float32)[None]
            cross_real = cross_real + (left_c * vis_c + left_d * vis_d)
            cross_imag = cross_imag + (left_c * vis_d - left_d * vis_c)
        cross = jnp.concatenate([cross_real, cross_imag], axis=-1).astype(jnp.bfloat16)
        pair_block = jnp.dot(cross.reshape(STATIONS * group_size, 2 * bin_count), lag_table, preferred_element_type=jnp.float32)
        pair_block = pair_block.reshape(STATIONS, group_size, LAGS) * norm_scale
        return jnp.where(keep_mask[:, None, :], pair_block, 0.0)
    stacked = lax.map(one_group, visiting)
    full_corr = jnp.moveaxis(stacked, 0, 1).reshape(STATIONS, STATIONS, LAGS)
    arranged = full_corr.reshape(STATIONS, N_ROW, N_COL, BLK, LAGS).transpose(0, 2, 1, 3, 4)
    return arranged.reshape(STATIONS, N_COL, N_ROW * BLK, LAGS)
```

```python
import math

import jax
import jax.numpy as jnp
from jax import lax
from jax.experimental import pallas as pl
from jax.experimental.pallas import tpu as pltpu
from jax.sharding import PartitionSpec as P

DECIM = 2
LAGS = 128
BAND = 64
LH = 64


def angle_table(row_count, col_count, period, offset):
    row_ids = jnp.arange(row_count, dtype=jnp.int32)[:, None] + offset
    col_ids = jnp.arange(col_count, dtype=jnp.int32)[None, :]
    phase_int = jnp.mod(row_ids * col_ids, period)
    angles = phase_int.astype(jnp.float32) * (2.0 * math.pi / period)
    return (jnp.cos(angles), jnp.sin(angles))


def decimate(records, fir_taps):
    tap_count = fir_taps.shape[0]
    out_block = 128
    in_block = DECIM * out_block
    lead_dims = records.shape[:2]
    block_count = records.shape[2] // in_block
    blocks = records.reshape(lead_dims + (block_count, in_block))
    tails = blocks[:, :, :-1, in_block - tap_count :]
    tails = jnp.concatenate([jnp.zeros(lead_dims + (1, tap_count), records.dtype), tails], axis=2)
    windows = jnp.concatenate([tails, blocks], axis=3)
    tap_ids = jnp.arange(tap_count, dtype=jnp.int32)[:, None, None]
    in_ids = jnp.arange(in_block + tap_count, dtype=jnp.int32)[None, :, None]
    out_ids = jnp.arange(out_block, dtype=jnp.int32)[None, None, :]
    onehot = (in_ids == DECIM * out_ids + tap_count - tap_ids).astype(jnp.float32)
    band_matrix = jnp.einsum("k,kij->ij", fir_taps, onehot, precision=lax.Precision.HIGHEST)
    summed = jnp.einsum("swbi,ij->swbj", windows, band_matrix, precision=lax.Precision.HIGHEST)
    return summed.reshape(lead_dims + (block_count * out_block,))


def spectrum(decimated):
    out_length = decimated.shape[-1]
    first_len = 64
    second_len = out_length // first_len
    lead_dims = decimated.shape[:-1]
    blocks = decimated.reshape(lead_dims + (first_len, second_len))
    cos_one, sin_one = angle_table(first_len, first_len, first_len, 0)
    real_z = jnp.einsum("bwnq,fn->bwfq", blocks, cos_one, precision=lax.Precision.HIGHEST)
    imag_z = -jnp.einsum("bwnq,fn->bwfq", blocks, sin_one, precision=lax.Precision.HIGHEST)
    cos_two, sin_two = angle_table(first_len, second_len, out_length, 0)
    real_t = real_z * cos_two + imag_z * sin_two
    imag_t = imag_z * cos_two - real_z * sin_two
    cos_three, sin_three = angle_table(second_len // 2, second_len, second_len, 0)
    real_x = jnp.einsum(
        "bwfq,gq->bwgf", real_t, cos_three, precision=lax.Precision.HIGHEST
    ) + jnp.einsum("bwfq,gq->bwgf", imag_t, sin_three, precision=lax.Precision.HIGHEST)
    imag_x = jnp.einsum(
        "bwfq,gq->bwgf", imag_t, cos_three, precision=lax.Precision.HIGHEST
    ) - jnp.einsum("bwfq,gq->bwgf", real_t, sin_three, precision=lax.Precision.HIGHEST)
    bin_count = out_length // 2
    return (real_x.reshape(lead_dims + (bin_count,)), imag_x.reshape(lead_dims + (bin_count,)))


def whiten(spec_real, spec_imag):
    lead_dims = spec_real.shape[:-1]
    bin_count = spec_real.shape[-1]
    banded = lead_dims + (bin_count // BAND, BAND)
    squares = (spec_real * spec_real + spec_imag * spec_imag).reshape(banded)
    band_power = jnp.mean(squares, axis=-1, keepdims=True)
    inverse = 1.0 / jnp.sqrt(band_power + 1e-06)
    white_real = (spec_real.reshape(banded) * inverse).reshape(spec_real.shape)
    white_imag = (spec_imag.reshape(banded) * inverse).reshape(spec_imag.shape)
    return jnp.concatenate([white_real, white_imag], axis=-1).astype(jnp.bfloat16)


def cross_kernel(left_ref, visit_ref, table_ref, out_ref, left_f32, visit_f32, cross_ref):
    window_count, left_count, width = left_ref.shape
    group = visit_ref.shape[1]
    bin_count = width // 2
    chunk = max(128, min(512, 8192 // left_count))
    chunks = bin_count // chunk

    @pl.when(pl.program_id(0) == 0)
    def _():
        left_f32[...] = left_ref[...].astype(jnp.float32)

    visit_f32[...] = visit_ref[...].astype(jnp.float32)

    def one_chunk(step, carry):
        partner = step // chunks
        off = pl.multiple_of((step % chunks) * chunk, chunk)
        acc_re = jnp.zeros((left_count, chunk), jnp.float32)
        acc_im = jnp.zeros((left_count, chunk), jnp.float32)
        for window in range(window_count):
            left_c = left_f32[window, :, pl.ds(off, chunk)]
            left_d = left_f32[window, :, pl.ds(off + bin_count, chunk)]
            vis_c = visit_f32[window, pl.ds(partner, 1), pl.ds(off, chunk)]
            vis_d = visit_f32[window, pl.ds(partner, 1), pl.ds(off + bin_count, chunk)]
            acc_re = acc_re + (left_c * vis_c + left_d * vis_d)
            acc_im = acc_im + (left_c * vis_d - left_d * vis_c)
        row = pl.multiple_of(partner * left_count, left_count)
        cross_ref[pl.ds(row, left_count), pl.ds(off, chunk)] = acc_re.astype(jnp.bfloat16)
        cross_ref[pl.ds(row, left_count), pl.ds(off + bin_count, chunk)] = acc_im.astype(jnp.bfloat16)
        return carry

    lax.fori_loop(0, group * chunks, one_chunk, 0)
    out_ref[...] = jnp.dot(cross_ref[...], table_ref[...], preferred_element_type=jnp.float32)


def pair_block(left_by_window, visiting, lag_table):
    window_count, left_count, width = left_by_window.shape
    visit_count = visiting.shape[1]
    lag_count = lag_table.shape[1]
    group = min(8, visit_count)
    while visit_count % group:
        group -= 1
    rows = group * left_count
    flops = visit_count * left_count * width * (4 * window_count + 2 * lag_count)
    return pl.pallas_call(
        cross_kernel,
        out_shape=jax.ShapeDtypeStruct((visit_count * left_count, lag_count), jnp.float32),
        grid=(visit_count // group,),
        in_specs=[
            pl.BlockSpec((window_count, left_count, width), lambda g: (0, 0, 0)),
            pl.BlockSpec((window_count, group, width), lambda g: (0, g, 0)),
            pl.BlockSpec((width, lag_count), lambda g: (0, 0)),
        ],
        out_specs=pl.BlockSpec((rows, lag_count), lambda g: (g, 0)),
        scratch_shapes=[
            pltpu.VMEM((window_count, left_count, width), jnp.float32),
            pltpu.VMEM((window_count, group, width), jnp.float32),
            pltpu.VMEM((rows, width), jnp.bfloat16),
        ],
        compiler_params=pltpu.CompilerParams(dimension_semantics=("arbitrary",)),
        cost_estimate=pl.CostEstimate(
            flops=flops,
            transcendentals=0,
            bytes_accessed=2 * width * (window_count * (left_count + visit_count) + lag_count)
            + 4 * visit_count * left_count * lag_count,
        ),
    )(left_by_window, visiting, lag_table)


def on_device(records, fir_taps, lag_limit):
    block_size = records.shape[0]
    decimated = decimate(records, fir_taps)
    out_length = decimated.shape[-1]
    bin_count = out_length // 2
    spec_real, spec_imag = spectrum(decimated)
    white = whiten(spec_real, spec_imag)
    white_by_window = jnp.moveaxis(white, 1, 0)
    left_by_window = lax.all_gather(white_by_window, "col", axis=1, tiled=True)
    cos_lag, sin_lag = angle_table(LAGS, bin_count, out_length, -LH)
    lag_table = jnp.concatenate([cos_lag.T, sin_lag.T], axis=0).astype(jnp.bfloat16)
    group_rows = left_by_window.shape[1]
    piece_rows = lax.all_gather(white_by_window, "row", axis=1, tiled=True)
    visit_count = piece_rows.shape[1]
    pair = pair_block(left_by_window, piece_rows, lag_table)
    pair = jnp.swapaxes(pair.reshape(visit_count, group_rows, LAGS), 0, 1)
    norm_scale = 1.0 / math.sqrt(white.shape[1] * bin_count)
    pair = pair * norm_scale
    lag_offset = jnp.abs(jnp.arange(LAGS, dtype=jnp.int32) - LH)
    keep_mask = lag_offset[None, :] <= lag_limit[:, None]
    tile_stack = jnp.where(keep_mask[:, None, :], pair, 0.0)
    return tile_stack[:, None]


def solution(mesh):
    placed = (P(("row", "col"), None, None), P(), P("row"))
    return jax.shard_map(
        on_device,
        mesh=mesh,
        in_specs=placed,
        out_specs=P("row", "col", None, None),
        check_vma=False,
    )
```

```python
import math

import jax
import jax.numpy as jnp
from jax import lax
from jax.experimental import pallas as pl
from jax.experimental.pallas import tpu as pltpu
from jax.sharding import PartitionSpec as P

DECIM = 2
LAGS = 128
BAND = 64
LH = 64


def angle_table(row_count, col_count, period, offset):
    row_ids = jnp.arange(row_count, dtype=jnp.int32)[:, None] + offset
    col_ids = jnp.arange(col_count, dtype=jnp.int32)[None, :]
    phase_int = jnp.mod(row_ids * col_ids, period)
    angles = phase_int.astype(jnp.float32) * (2.0 * math.pi / period)
    return (jnp.cos(angles), jnp.sin(angles))


def decimate(records, fir_taps):
    tap_count = fir_taps.shape[0]
    out_block = 128
    in_block = DECIM * out_block
    lead_dims = records.shape[:2]
    block_count = records.shape[2] // in_block
    blocks = records.reshape(lead_dims + (block_count, in_block))
    tails = blocks[:, :, :-1, in_block - tap_count :]
    tails = jnp.concatenate([jnp.zeros(lead_dims + (1, tap_count), records.dtype), tails], axis=2)
    windows = jnp.concatenate([tails, blocks], axis=3)
    tap_ids = jnp.arange(tap_count, dtype=jnp.int32)[:, None, None]
    in_ids = jnp.arange(in_block + tap_count, dtype=jnp.int32)[None, :, None]
    out_ids = jnp.arange(out_block, dtype=jnp.int32)[None, None, :]
    onehot = (in_ids == DECIM * out_ids + tap_count - tap_ids).astype(jnp.float32)
    band_matrix = jnp.einsum("k,kij->ij", fir_taps, onehot, precision=lax.Precision.HIGHEST)
    summed = jnp.einsum("swbi,ij->swbj", windows, band_matrix, precision=lax.Precision.HIGHEST)
    return summed.reshape(lead_dims + (block_count * out_block,))


def spectrum(decimated):
    out_length = decimated.shape[-1]
    first_len = 64
    second_len = out_length // first_len
    lead_dims = decimated.shape[:-1]
    blocks = decimated.reshape(lead_dims + (first_len, second_len))
    cos_one, sin_one = angle_table(first_len, first_len, first_len, 0)
    real_z = jnp.einsum("bwnq,fn->bwfq", blocks, cos_one, precision=lax.Precision.HIGHEST)
    imag_z = -jnp.einsum("bwnq,fn->bwfq", blocks, sin_one, precision=lax.Precision.HIGHEST)
    cos_two, sin_two = angle_table(first_len, second_len, out_length, 0)
    real_t = real_z * cos_two + imag_z * sin_two
    imag_t = imag_z * cos_two - real_z * sin_two
    cos_three, sin_three = angle_table(second_len // 2, second_len, second_len, 0)
    real_x = jnp.einsum(
        "bwfq,gq->bwgf", real_t, cos_three, precision=lax.Precision.HIGHEST
    ) + jnp.einsum("bwfq,gq->bwgf", imag_t, sin_three, precision=lax.Precision.HIGHEST)
    imag_x = jnp.einsum(
        "bwfq,gq->bwgf", imag_t, cos_three, precision=lax.Precision.HIGHEST
    ) - jnp.einsum("bwfq,gq->bwgf", real_t, sin_three, precision=lax.Precision.HIGHEST)
    bin_count = out_length // 2
    return (real_x.reshape(lead_dims + (bin_count,)), imag_x.reshape(lead_dims + (bin_count,)))


def whiten(spec_real, spec_imag):
    lead_dims = spec_real.shape[:-1]
    bin_count = spec_real.shape[-1]
    banded = lead_dims + (bin_count // BAND, BAND)
    squares = (spec_real * spec_real + spec_imag * spec_imag).reshape(banded)
    band_power = jnp.mean(squares, axis=-1, keepdims=True)
    inverse = 1.0 / jnp.sqrt(band_power + 1e-06)
    white_real = (spec_real.reshape(banded) * inverse).reshape(spec_real.shape)
    white_imag = (spec_imag.reshape(banded) * inverse).reshape(spec_imag.shape)
    return jnp.concatenate([white_real, white_imag], axis=-1).astype(jnp.bfloat16)


def cross_kernel(left_ref, visit_ref, table_ref, out_ref, left_f32, visit_f32, cross_ref):
    window_count, left_count, width = left_ref.shape
    group = visit_ref.shape[1]
    bin_count = width // 2
    chunk = max(128, min(512, 8192 // left_count))
    chunks = bin_count // chunk

    @pl.when(pl.program_id(0) == 0)
    def _():
        left_f32[...] = left_ref[...].astype(jnp.float32)

    visit_f32[...] = visit_ref[...].astype(jnp.float32)

    def one_chunk(step, carry):
        partner = step // chunks
        off = pl.multiple_of((step % chunks) * chunk, chunk)
        acc_re = jnp.zeros((left_count, chunk), jnp.float32)
        acc_im = jnp.zeros((left_count, chunk), jnp.float32)
        for window in range(window_count):
            left_c = left_f32[window, :, pl.ds(off, chunk)]
            left_d = left_f32[window, :, pl.ds(off + bin_count, chunk)]
            vis_c = visit_f32[window, pl.ds(partner, 1), pl.ds(off, chunk)]
            vis_d = visit_f32[window, pl.ds(partner, 1), pl.ds(off + bin_count, chunk)]
            acc_re = acc_re + (left_c * vis_c + left_d * vis_d)
            acc_im = acc_im + (left_c * vis_d - left_d * vis_c)
        row = pl.multiple_of(partner * left_count, left_count)
        cross_ref[pl.ds(row, left_count), pl.ds(off, chunk)] = acc_re.astype(jnp.bfloat16)
        cross_ref[pl.ds(row, left_count), pl.ds(off + bin_count, chunk)] = acc_im.astype(jnp.bfloat16)
        return carry

    lax.fori_loop(0, group * chunks, one_chunk, 0)
    out_ref[...] = jnp.dot(cross_ref[...], table_ref[...], preferred_element_type=jnp.float32)


def pair_block(left_by_window, visiting, lag_table):
    window_count, left_count, width = left_by_window.shape
    visit_count = visiting.shape[1]
    lag_count = lag_table.shape[1]
    group = min(8, visit_count)
    while visit_count % group:
        group -= 1
    rows = group * left_count
    flops = visit_count * left_count * width * (4 * window_count + 2 * lag_count)
    return pl.pallas_call(
        cross_kernel,
        out_shape=jax.ShapeDtypeStruct((visit_count * left_count, lag_count), jnp.float32),
        grid=(visit_count // group,),
        in_specs=[
            pl.BlockSpec((window_count, left_count, width), lambda g: (0, 0, 0)),
            pl.BlockSpec((window_count, group, width), lambda g: (0, g, 0)),
            pl.BlockSpec((width, lag_count), lambda g: (0, 0)),
        ],
        out_specs=pl.BlockSpec((rows, lag_count), lambda g: (g, 0)),
        scratch_shapes=[
            pltpu.VMEM((window_count, left_count, width), jnp.float32),
            pltpu.VMEM((window_count, group, width), jnp.float32),
            pltpu.VMEM((rows, width), jnp.bfloat16),
        ],
        compiler_params=pltpu.CompilerParams(dimension_semantics=("arbitrary",)),
        cost_estimate=pl.CostEstimate(
            flops=flops,
            transcendentals=0,
            bytes_accessed=2 * width * (window_count * (left_count + visit_count) + lag_count)
            + 4 * visit_count * left_count * lag_count,
        ),
    )(left_by_window, visiting, lag_table)


def xor_gather(block, axis_name, size):
    if size & (size - 1):
        return lax.all_gather(block, axis_name, axis=1, tiled=True), None
    pieces = [block]
    for step in range(1, size):
        pairs = [(source, source ^ step) for source in range(size)]
        pieces.append(lax.ppermute(block, axis_name, pairs))
    order = lax.axis_index(axis_name) ^ jnp.arange(size, dtype=jnp.int32)
    return jnp.concatenate(pieces, axis=1), order


def on_device(records, fir_taps, lag_limit):
    block_size = records.shape[0]
    decimated = decimate(records, fir_taps)
    out_length = decimated.shape[-1]
    bin_count = out_length // 2
    spec_real, spec_imag = spectrum(decimated)
    white = whiten(spec_real, spec_imag)
    white_by_window = jnp.moveaxis(white, 1, 0)
    col_size = lax.axis_size("col")
    row_size = lax.axis_size("row")
    left_by_window, left_order = xor_gather(white_by_window, "col", col_size)
    cos_lag, sin_lag = angle_table(LAGS, bin_count, out_length, -LH)
    lag_table = jnp.concatenate([cos_lag.T, sin_lag.T], axis=0).astype(jnp.bfloat16)
    group_rows = left_by_window.shape[1]
    piece_rows, visit_order = xor_gather(white_by_window, "row", row_size)
    visit_count = piece_rows.shape[1]
    pair = pair_block(left_by_window, piece_rows, lag_table)
    pair = jnp.swapaxes(pair.reshape(visit_count, group_rows, LAGS), 0, 1)
    if visit_order is not None:
        pair = pair.reshape(group_rows, row_size, block_size, LAGS)
        pair = jnp.take(pair, visit_order, axis=1).reshape(group_rows, visit_count, LAGS)
    if left_order is not None:
        pair = pair.reshape(col_size, block_size, visit_count, LAGS)
        pair = jnp.take(pair, left_order, axis=0).reshape(group_rows, visit_count, LAGS)
    norm_scale = 1.0 / math.sqrt(white.shape[1] * bin_count)
    pair = pair * norm_scale
    lag_offset = jnp.abs(jnp.arange(LAGS, dtype=jnp.int32) - LH)
    keep_mask = lag_offset[None, :] <= lag_limit[:, None]
    tile_stack = jnp.where(keep_mask[:, None, :], pair, 0.0)
    return tile_stack[:, None]


def solution(mesh):
    placed = (P(("row", "col"), None, None), P(), P("row"))
    return jax.shard_map(
        on_device,
        mesh=mesh,
        in_specs=placed,
        out_specs=P("row", "col", None, None),
        check_vma=False,
    )
```

```python
import functools
import math

import jax
import jax.numpy as jnp
from jax import lax
from jax.experimental import pallas as pl
from jax.experimental.pallas import tpu as pltpu
from jax.sharding import PartitionSpec as P

DECIM = 2
LAGS = 128
BAND = 64
LH = 64


def angle_table(row_count, col_count, period, offset):
    row_ids = jnp.arange(row_count, dtype=jnp.int32)[:, None] + offset
    col_ids = jnp.arange(col_count, dtype=jnp.int32)[None, :]
    phase_int = jnp.mod(row_ids * col_ids, period)
    angles = phase_int.astype(jnp.float32) * (2.0 * math.pi / period)
    return (jnp.cos(angles), jnp.sin(angles))


def decimate(records, fir_taps):
    tap_count = fir_taps.shape[0]
    out_block = 128
    in_block = DECIM * out_block
    lead_dims = records.shape[:2]
    block_count = records.shape[2] // in_block
    blocks = records.reshape(lead_dims + (block_count, in_block))
    tails = blocks[:, :, :-1, in_block - tap_count :]
    tails = jnp.concatenate([jnp.zeros(lead_dims + (1, tap_count), records.dtype), tails], axis=2)
    windows = jnp.concatenate([tails, blocks], axis=3)
    tap_ids = jnp.arange(tap_count, dtype=jnp.int32)[:, None, None]
    in_ids = jnp.arange(in_block + tap_count, dtype=jnp.int32)[None, :, None]
    out_ids = jnp.arange(out_block, dtype=jnp.int32)[None, None, :]
    onehot = (in_ids == DECIM * out_ids + tap_count - tap_ids).astype(jnp.float32)
    band_matrix = jnp.einsum("k,kij->ij", fir_taps, onehot, precision=lax.Precision.HIGHEST)
    summed = jnp.einsum("swbi,ij->swbj", windows, band_matrix, precision=lax.Precision.HIGHEST)
    return summed.reshape(lead_dims + (block_count * out_block,))


def spectrum(decimated):
    out_length = decimated.shape[-1]
    first_len = 64
    second_len = out_length // first_len
    lead_dims = decimated.shape[:-1]
    blocks = decimated.reshape(lead_dims + (first_len, second_len))
    cos_one, sin_one = angle_table(first_len, first_len, first_len, 0)
    real_z = jnp.einsum("bwnq,fn->bwfq", blocks, cos_one, precision=lax.Precision.HIGHEST)
    imag_z = -jnp.einsum("bwnq,fn->bwfq", blocks, sin_one, precision=lax.Precision.HIGHEST)
    cos_two, sin_two = angle_table(first_len, second_len, out_length, 0)
    real_t = real_z * cos_two + imag_z * sin_two
    imag_t = imag_z * cos_two - real_z * sin_two
    cos_three, sin_three = angle_table(second_len // 2, second_len, second_len, 0)
    real_x = jnp.einsum(
        "bwfq,gq->bwgf", real_t, cos_three, precision=lax.Precision.HIGHEST
    ) + jnp.einsum("bwfq,gq->bwgf", imag_t, sin_three, precision=lax.Precision.HIGHEST)
    imag_x = jnp.einsum(
        "bwfq,gq->bwgf", imag_t, cos_three, precision=lax.Precision.HIGHEST
    ) - jnp.einsum("bwfq,gq->bwgf", real_t, sin_three, precision=lax.Precision.HIGHEST)
    bin_count = out_length // 2
    return (real_x.reshape(lead_dims + (bin_count,)), imag_x.reshape(lead_dims + (bin_count,)))


def whiten(spec_real, spec_imag):
    lead_dims = spec_real.shape[:-1]
    bin_count = spec_real.shape[-1]
    banded = lead_dims + (bin_count // BAND, BAND)
    squares = (spec_real * spec_real + spec_imag * spec_imag).reshape(banded)
    band_power = jnp.mean(squares, axis=-1, keepdims=True)
    inverse = 1.0 / jnp.sqrt(band_power + 1e-06)
    white_real = (spec_real.reshape(banded) * inverse).reshape(spec_real.shape)
    white_imag = (spec_imag.reshape(banded) * inverse).reshape(spec_imag.shape)
    return jnp.concatenate([white_real, white_imag], axis=-1).astype(jnp.bfloat16)


def cross_kernel(left_count, visit_count, *refs):
    left_refs = refs[:left_count]
    visit_refs = refs[left_count:left_count + visit_count]
    table_ref, out_ref, left_f32, visit_f32, cross_ref = refs[left_count + visit_count:]
    window_count, piece, width = left_refs[0].shape
    rows_left = left_f32.shape[1]
    bin_count = width // 2
    chunk = max(128, min(512, 8192 // rows_left))
    chunks = bin_count // chunk
    group_rows = cross_ref.shape[0]
    group = group_rows // (piece * rows_left)

    for index, ref in enumerate(left_refs):
        left_f32[:, index * piece:(index + 1) * piece, :] = ref[...].astype(jnp.float32)
    for index, ref in enumerate(visit_refs):
        visit_f32[:, index * piece:(index + 1) * piece, :] = ref[...].astype(jnp.float32)

    for first in range(0, visit_count, group):
        base = first * piece

        def one_chunk(step, carry):
            local = step // chunks
            partner = base + local
            off = pl.multiple_of((step % chunks) * chunk, chunk)
            acc_re = jnp.zeros((rows_left, chunk), jnp.float32)
            acc_im = jnp.zeros((rows_left, chunk), jnp.float32)
            for window in range(window_count):
                left_c = left_f32[window, :, pl.ds(off, chunk)]
                left_d = left_f32[window, :, pl.ds(off + bin_count, chunk)]
                vis_c = visit_f32[window, pl.ds(partner, 1), pl.ds(off, chunk)]
                vis_d = visit_f32[window, pl.ds(partner, 1), pl.ds(off + bin_count, chunk)]
                acc_re = acc_re + (left_c * vis_c + left_d * vis_d)
                acc_im = acc_im + (left_c * vis_d - left_d * vis_c)
            row = pl.multiple_of(local * rows_left, rows_left)
            cross_ref[pl.ds(row, rows_left), pl.ds(off, chunk)] = acc_re.astype(jnp.bfloat16)
            cross_ref[pl.ds(row, rows_left), pl.ds(off + bin_count, chunk)] = acc_im.astype(jnp.bfloat16)
            return carry

        lax.fori_loop(0, group * piece * chunks, one_chunk, 0)
        out_ref[base * rows_left:base * rows_left + group_rows, :] = jnp.dot(
            cross_ref[...], table_ref[...], preferred_element_type=jnp.float32
        )


def pair_block(left_pieces, visit_pieces, lag_table):
    window_count, piece, width = left_pieces[0].shape
    left_count = len(left_pieces)
    visit_count = len(visit_pieces)
    rows_left = left_count * piece
    visit_rows = visit_count * piece
    lag_count = lag_table.shape[1]
    group = max(1, min(visit_count, 256 // (piece * rows_left)))
    while visit_count % group:
        group -= 1
    flops = visit_rows * rows_left * width * (4 * window_count + 2 * lag_count)
    vmem = pltpu.VMEM
    return pl.pallas_call(
        functools.partial(cross_kernel, left_count, visit_count),
        out_shape=jax.ShapeDtypeStruct((visit_rows * rows_left, lag_count), jnp.float32),
        in_specs=[pl.BlockSpec(memory_space=vmem)] * (left_count + visit_count + 1),
        out_specs=pl.BlockSpec(memory_space=vmem),
        scratch_shapes=[
            vmem((window_count, rows_left, width), jnp.float32),
            vmem((window_count, visit_rows, width), jnp.float32),
            vmem((group * piece * rows_left, width), jnp.bfloat16),
        ],
        compiler_params=pltpu.CompilerParams(vmem_limit_bytes=60 * 1024 * 1024),
        cost_estimate=pl.CostEstimate(
            flops=flops,
            transcendentals=0,
            bytes_accessed=2 * width * (window_count * (rows_left + visit_rows) + lag_count)
            + 4 * visit_rows * rows_left * lag_count,
        ),
    )(*left_pieces, *visit_pieces, lag_table)


def xor_gather(block, axis_name, size):
    if size & (size - 1):
        return [lax.all_gather(block, axis_name, axis=1, tiled=True)], None
    pieces = [block]
    for step in range(1, size):
        pairs = [(source, source ^ step) for source in range(size)]
        pieces.append(lax.ppermute(block, axis_name, pairs))
    order = lax.axis_index(axis_name) ^ jnp.arange(size, dtype=jnp.int32)
    return pieces, order


def on_device(records, fir_taps, lag_limit):
    block_size = records.shape[0]
    decimated = decimate(records, fir_taps)
    out_length = decimated.shape[-1]
    bin_count = out_length // 2
    spec_real, spec_imag = spectrum(decimated)
    white = whiten(spec_real, spec_imag)
    white_by_window = jnp.moveaxis(white, 1, 0)
    col_size = lax.axis_size("col")
    row_size = lax.axis_size("row")
    left_by_window, left_order = xor_gather(white_by_window, "col", col_size)
    cos_lag, sin_lag = angle_table(LAGS, bin_count, out_length, -LH)
    lag_table = jnp.concatenate([cos_lag.T, sin_lag.T], axis=0).astype(jnp.bfloat16)
    group_rows = sum(piece.shape[1] for piece in left_by_window)
    piece_rows, visit_order = xor_gather(white_by_window, "row", row_size)
    visit_count = sum(piece.shape[1] for piece in piece_rows)
    pair = pair_block(left_by_window, piece_rows, lag_table)
    pair = jnp.swapaxes(pair.reshape(visit_count, group_rows, LAGS), 0, 1)
    if visit_order is not None:
        pair = pair.reshape(group_rows, row_size, block_size, LAGS)
        pair = jnp.take(pair, visit_order, axis=1).reshape(group_rows, visit_count, LAGS)
    if left_order is not None:
        pair = pair.reshape(col_size, block_size, visit_count, LAGS)
        pair = jnp.take(pair, left_order, axis=0).reshape(group_rows, visit_count, LAGS)
    norm_scale = 1.0 / math.sqrt(white.shape[1] * bin_count)
    pair = pair * norm_scale
    lag_offset = jnp.abs(jnp.arange(LAGS, dtype=jnp.int32) - LH)
    keep_mask = lag_offset[None, :] <= lag_limit[:, None]
    tile_stack = jnp.where(keep_mask[:, None, :], pair, 0.0)
    return tile_stack[:, None]


def solution(mesh):
    placed = (P(("row", "col"), None, None), P(), P("row"))
    return jax.shard_map(
        on_device,
        mesh=mesh,
        in_specs=placed,
        out_specs=P("row", "col", None, None),
        check_vma=False,
    )
```

```python
import functools
import math

import jax
import jax.numpy as jnp
from jax import lax
from jax.experimental import pallas as pl
from jax.experimental.pallas import tpu as pltpu
from jax.sharding import PartitionSpec as P

DECIM = 2
LAGS = 128
BAND = 64
LH = 64


def angle_table(row_count, col_count, period, offset):
    row_ids = jnp.arange(row_count, dtype=jnp.int32)[:, None] + offset
    col_ids = jnp.arange(col_count, dtype=jnp.int32)[None, :]
    phase_int = jnp.mod(row_ids * col_ids, period)
    angles = phase_int.astype(jnp.float32) * (2.0 * math.pi / period)
    return (jnp.cos(angles), jnp.sin(angles))


def decimate(records, fir_taps):
    tap_count = fir_taps.shape[0]
    out_block = 128
    in_block = DECIM * out_block
    lead_dims = records.shape[:2]
    block_count = records.shape[2] // in_block
    blocks = records.reshape(lead_dims + (block_count, in_block))
    tails = blocks[:, :, :-1, in_block - tap_count :]
    tails = jnp.concatenate([jnp.zeros(lead_dims + (1, tap_count), records.dtype), tails], axis=2)
    windows = jnp.concatenate([tails, blocks], axis=3)
    tap_ids = jnp.arange(tap_count, dtype=jnp.int32)[:, None, None]
    in_ids = jnp.arange(in_block + tap_count, dtype=jnp.int32)[None, :, None]
    out_ids = jnp.arange(out_block, dtype=jnp.int32)[None, None, :]
    onehot = (in_ids == DECIM * out_ids + tap_count - tap_ids).astype(jnp.float32)
    band_matrix = jnp.einsum("k,kij->ij", fir_taps, onehot, precision=lax.Precision.HIGHEST)
    summed = jnp.einsum("swbi,ij->swbj", windows, band_matrix, precision=lax.Precision.HIGHEST)
    return summed.reshape(lead_dims + (block_count * out_block,))


def spectrum(decimated):
    out_length = decimated.shape[-1]
    first_len = 64
    second_len = out_length // first_len
    lead_dims = decimated.shape[:-1]
    blocks = decimated.reshape(lead_dims + (first_len, second_len))
    cos_one, sin_one = angle_table(first_len, first_len, first_len, 0)
    real_z = jnp.einsum("bwnq,fn->bwfq", blocks, cos_one, precision=lax.Precision.HIGHEST)
    imag_z = -jnp.einsum("bwnq,fn->bwfq", blocks, sin_one, precision=lax.Precision.HIGHEST)
    cos_two, sin_two = angle_table(first_len, second_len, out_length, 0)
    real_t = real_z * cos_two + imag_z * sin_two
    imag_t = imag_z * cos_two - real_z * sin_two
    cos_three, sin_three = angle_table(second_len // 2, second_len, second_len, 0)
    real_x = jnp.einsum(
        "bwfq,gq->bwgf", real_t, cos_three, precision=lax.Precision.HIGHEST
    ) + jnp.einsum("bwfq,gq->bwgf", imag_t, sin_three, precision=lax.Precision.HIGHEST)
    imag_x = jnp.einsum(
        "bwfq,gq->bwgf", imag_t, cos_three, precision=lax.Precision.HIGHEST
    ) - jnp.einsum("bwfq,gq->bwgf", real_t, sin_three, precision=lax.Precision.HIGHEST)
    bin_count = out_length // 2
    return (real_x.reshape(lead_dims + (bin_count,)), imag_x.reshape(lead_dims + (bin_count,)))


def whiten(spec_real, spec_imag):
    lead_dims = spec_real.shape[:-1]
    bin_count = spec_real.shape[-1]
    banded = lead_dims + (bin_count // BAND, BAND)
    squares = (spec_real * spec_real + spec_imag * spec_imag).reshape(banded)
    band_power = jnp.mean(squares, axis=-1, keepdims=True)
    inverse = 1.0 / jnp.sqrt(band_power + 1e-06)
    white_real = (spec_real.reshape(banded) * inverse).reshape(spec_real.shape)
    white_imag = (spec_imag.reshape(banded) * inverse).reshape(spec_imag.shape)
    return jnp.concatenate([white_real, white_imag], axis=-1).astype(jnp.bfloat16)


def cross_kernel(left_count, visit_count, *refs):
    left_refs = refs[:left_count]
    visit_refs = refs[left_count:left_count + visit_count]
    table_ref, out_ref, left_f32, visit_f32, cross_ref = refs[left_count + visit_count:]
    window_count, piece, width = left_refs[0].shape
    rows_left = left_f32.shape[1]
    bin_count = width // 2
    chunk = max(128, min(512, 8192 // rows_left))
    chunks = bin_count // chunk
    group_rows = cross_ref.shape[0]
    group = group_rows // (piece * rows_left)

    for index, ref in enumerate(left_refs):
        left_f32[:, index * piece:(index + 1) * piece, :] = ref[...].astype(jnp.float32)
    for index, ref in enumerate(visit_refs):
        visit_f32[:, index * piece:(index + 1) * piece, :] = ref[...].astype(jnp.float32)

    for first in range(0, visit_count, group):
        base = first * piece

        def one_chunk(step, carry):
            local = step // chunks
            partner = base + local
            off = pl.multiple_of((step % chunks) * chunk, chunk)
            acc_re = jnp.zeros((rows_left, chunk), jnp.float32)
            acc_im = jnp.zeros((rows_left, chunk), jnp.float32)
            for window in range(window_count):
                left_c = left_f32[window, :, pl.ds(off, chunk)]
                left_d = left_f32[window, :, pl.ds(off + bin_count, chunk)]
                vis_c = visit_f32[window, pl.ds(partner, 1), pl.ds(off, chunk)]
                vis_d = visit_f32[window, pl.ds(partner, 1), pl.ds(off + bin_count, chunk)]
                acc_re = acc_re + (left_c * vis_c + left_d * vis_d)
                acc_im = acc_im + (left_c * vis_d - left_d * vis_c)
            row = pl.multiple_of(local * rows_left, rows_left)
            cross_ref[pl.ds(row, rows_left), pl.ds(off, chunk)] = acc_re.astype(jnp.bfloat16)
            cross_ref[pl.ds(row, rows_left), pl.ds(off + bin_count, chunk)] = acc_im.astype(jnp.bfloat16)
            return carry

        lax.fori_loop(0, group * piece * chunks, one_chunk, 0)
        out_ref[base * rows_left:base * rows_left + group_rows, :] = jnp.dot(
            cross_ref[...], table_ref[...], preferred_element_type=jnp.float32
        )


def pair_block(left_pieces, visit_pieces, lag_table):
    window_count, piece, width = left_pieces[0].shape
    left_count = len(left_pieces)
    visit_count = len(visit_pieces)
    rows_left = left_count * piece
    visit_rows = visit_count * piece
    lag_count = lag_table.shape[1]
    group = max(1, min(visit_count, 256 // (piece * rows_left)))
    while visit_count % group:
        group -= 1
    flops = visit_rows * rows_left * width * (4 * window_count + 2 * lag_count)
    vmem = pltpu.VMEM
    return pl.pallas_call(
        functools.partial(cross_kernel, left_count, visit_count),
        out_shape=jax.ShapeDtypeStruct((visit_rows * rows_left, lag_count), jnp.float32),
        in_specs=[pl.BlockSpec(memory_space=vmem)] * (left_count + visit_count + 1),
        out_specs=pl.BlockSpec(memory_space=vmem),
        scratch_shapes=[
            vmem((window_count, rows_left, width), jnp.float32),
            vmem((window_count, visit_rows, width), jnp.float32),
            vmem((group * piece * rows_left, width), jnp.bfloat16),
        ],
        compiler_params=pltpu.CompilerParams(vmem_limit_bytes=60 * 1024 * 1024),
        cost_estimate=pl.CostEstimate(
            flops=flops,
            transcendentals=0,
            bytes_accessed=2 * width * (window_count * (rows_left + visit_rows) + lag_count)
            + 4 * visit_rows * rows_left * lag_count,
        ),
    )(*left_pieces, *visit_pieces, lag_table)


def xor_gather(block, axis_name, size):
    if size & (size - 1):
        return [lax.all_gather(block, axis_name, axis=1, tiled=True)], None
    pieces = [block]
    for step in range(1, size):
        pairs = [(source, source ^ step) for source in range(size)]
        pieces.append(lax.ppermute(block, axis_name, pairs))
    order = lax.axis_index(axis_name) ^ jnp.arange(size, dtype=jnp.int32)
    return pieces, order


def on_device(records, fir_taps, lag_limit):
    block_size = records.shape[0]
    decimated = decimate(records, fir_taps)
    out_length = decimated.shape[-1]
    bin_count = out_length // 2
    spec_real, spec_imag = spectrum(decimated)
    white = whiten(spec_real, spec_imag)
    white_by_window = jnp.moveaxis(white, 1, 0)
    col_size = lax.axis_size("col")
    row_size = lax.axis_size("row")
    left_by_window, left_order = xor_gather(white_by_window, "col", col_size)
    cos_lag, sin_lag = angle_table(LAGS, bin_count, out_length, -LH)
    lag_table = jnp.concatenate([cos_lag.T, sin_lag.T], axis=0).astype(jnp.bfloat16)
    group_rows = sum(piece.shape[1] for piece in left_by_window)
    row_block = white_by_window
    if len(left_by_window) > 1:
        row_block, ignored = lax.optimization_barrier((white_by_window, left_by_window[1]))
    piece_rows, visit_order = xor_gather(row_block, "row", row_size)
    visit_count = sum(piece.shape[1] for piece in piece_rows)
    pair = pair_block(left_by_window, piece_rows, lag_table)
    pair = jnp.swapaxes(pair.reshape(visit_count, group_rows, LAGS), 0, 1)
    if visit_order is not None:
        pair = pair.reshape(group_rows, row_size, block_size, LAGS)
        pair = jnp.take(pair, visit_order, axis=1).reshape(group_rows, visit_count, LAGS)
    if left_order is not None:
        pair = pair.reshape(col_size, block_size, visit_count, LAGS)
        pair = jnp.take(pair, left_order, axis=0).reshape(group_rows, visit_count, LAGS)
    norm_scale = 1.0 / math.sqrt(white.shape[1] * bin_count)
    pair = pair * norm_scale
    lag_offset = jnp.abs(jnp.arange(LAGS, dtype=jnp.int32) - LH)
    keep_mask = lag_offset[None, :] <= lag_limit[:, None]
    tile_stack = jnp.where(keep_mask[:, None, :], pair, 0.0)
    return tile_stack[:, None]


def solution(mesh):
    placed = (P(("row", "col"), None, None), P(), P("row"))
    return jax.shard_map(
        on_device,
        mesh=mesh,
        in_specs=placed,
        out_specs=P("row", "col", None, None),
        check_vma=False,
    )
```

```python
import functools
import math

import jax
import jax.numpy as jnp
from jax import lax
from jax.experimental import pallas as pl
from jax.experimental.pallas import tpu as pltpu
from jax.sharding import PartitionSpec as P

DECIM = 2
LAGS = 128
BAND = 64
LH = 64


def angle_table(row_count, col_count, period, offset):
    row_ids = jnp.arange(row_count, dtype=jnp.int32)[:, None] + offset
    col_ids = jnp.arange(col_count, dtype=jnp.int32)[None, :]
    phase_int = jnp.mod(row_ids * col_ids, period)
    angles = phase_int.astype(jnp.float32) * (2.0 * math.pi / period)
    return (jnp.cos(angles), jnp.sin(angles))


def decimate(records, fir_taps):
    tap_count = fir_taps.shape[0]
    out_block = 128
    in_block = DECIM * out_block
    lead_dims = records.shape[:2]
    block_count = records.shape[2] // in_block
    blocks = records.reshape(lead_dims + (block_count, in_block))
    tails = blocks[:, :, :-1, in_block - tap_count :]
    tails = jnp.concatenate([jnp.zeros(lead_dims + (1, tap_count), records.dtype), tails], axis=2)
    windows = jnp.concatenate([tails, blocks], axis=3)
    tap_ids = jnp.arange(tap_count, dtype=jnp.int32)[:, None, None]
    in_ids = jnp.arange(in_block + tap_count, dtype=jnp.int32)[None, :, None]
    out_ids = jnp.arange(out_block, dtype=jnp.int32)[None, None, :]
    onehot = (in_ids == DECIM * out_ids + tap_count - tap_ids).astype(jnp.float32)
    band_matrix = jnp.einsum("k,kij->ij", fir_taps, onehot, precision=lax.Precision.HIGHEST)
    summed = jnp.einsum("swbi,ij->swbj", windows, band_matrix, precision=lax.Precision.HIGHEST)
    return summed.reshape(lead_dims + (block_count * out_block,))


def spectrum(decimated):
    out_length = decimated.shape[-1]
    first_len = 64
    second_len = out_length // first_len
    lead_dims = decimated.shape[:-1]
    blocks = decimated.reshape(lead_dims + (first_len, second_len))
    cos_one, sin_one = angle_table(first_len, first_len, first_len, 0)
    real_z = jnp.einsum("bwnq,fn->bwfq", blocks, cos_one, precision=lax.Precision.HIGHEST)
    imag_z = -jnp.einsum("bwnq,fn->bwfq", blocks, sin_one, precision=lax.Precision.HIGHEST)
    cos_two, sin_two = angle_table(first_len, second_len, out_length, 0)
    real_t = real_z * cos_two + imag_z * sin_two
    imag_t = imag_z * cos_two - real_z * sin_two
    cos_three, sin_three = angle_table(second_len // 2, second_len, second_len, 0)
    real_x = jnp.einsum(
        "bwfq,gq->bwgf", real_t, cos_three, precision=lax.Precision.HIGHEST
    ) + jnp.einsum("bwfq,gq->bwgf", imag_t, sin_three, precision=lax.Precision.HIGHEST)
    imag_x = jnp.einsum(
        "bwfq,gq->bwgf", imag_t, cos_three, precision=lax.Precision.HIGHEST
    ) - jnp.einsum("bwfq,gq->bwgf", real_t, sin_three, precision=lax.Precision.HIGHEST)
    bin_count = out_length // 2
    return (real_x.reshape(lead_dims + (bin_count,)), imag_x.reshape(lead_dims + (bin_count,)))


def whiten(spec_real, spec_imag):
    lead_dims = spec_real.shape[:-1]
    bin_count = spec_real.shape[-1]
    banded = lead_dims + (bin_count // BAND, BAND)
    squares = (spec_real * spec_real + spec_imag * spec_imag).reshape(banded)
    band_power = jnp.mean(squares, axis=-1, keepdims=True)
    inverse = 1.0 / jnp.sqrt(band_power + 1e-06)
    white_real = (spec_real.reshape(banded) * inverse).reshape(spec_real.shape)
    white_imag = (spec_imag.reshape(banded) * inverse).reshape(spec_imag.shape)
    return jnp.concatenate([white_real, white_imag], axis=-1).astype(jnp.bfloat16)


def cross_kernel(left_count, visit_count, *refs):
    left_refs = refs[:left_count]
    visit_refs = refs[left_count:left_count + visit_count]
    table_ref, out_ref, left_f32, visit_f32, cross_ref = refs[left_count + visit_count:]
    window_count, piece, width = left_refs[0].shape
    rows_left = left_f32.shape[1]
    bin_count = width // 2
    chunk = 512
    while chunk > 128 and chunk * rows_left > 8192:
        chunk //= 2
    chunks = bin_count // chunk
    group_rows = cross_ref.shape[0]
    group = group_rows // (piece * rows_left)

    for index, ref in enumerate(left_refs):
        left_f32[:, index * piece:(index + 1) * piece, :] = ref[...].astype(jnp.float32)
    for index, ref in enumerate(visit_refs):
        visit_f32[:, index * piece:(index + 1) * piece, :] = ref[...].astype(jnp.float32)

    for first in range(0, visit_count, group):
        base = first * piece

        def one_chunk(step, carry):
            local = step // chunks
            partner = base + local
            off = pl.multiple_of((step % chunks) * chunk, chunk)
            acc_re = jnp.zeros((rows_left, chunk), jnp.float32)
            acc_im = jnp.zeros((rows_left, chunk), jnp.float32)
            for window in range(window_count):
                left_c = left_f32[window, :, pl.ds(off, chunk)]
                left_d = left_f32[window, :, pl.ds(off + bin_count, chunk)]
                vis_c = visit_f32[window, pl.ds(partner, 1), pl.ds(off, chunk)]
                vis_d = visit_f32[window, pl.ds(partner, 1), pl.ds(off + bin_count, chunk)]
                acc_re = acc_re + (left_c * vis_c + left_d * vis_d)
                acc_im = acc_im + (left_c * vis_d - left_d * vis_c)
            row = pl.multiple_of(local * rows_left, rows_left)
            cross_ref[pl.ds(row, rows_left), pl.ds(off, chunk)] = acc_re.astype(jnp.bfloat16)
            cross_ref[pl.ds(row, rows_left), pl.ds(off + bin_count, chunk)] = acc_im.astype(jnp.bfloat16)
            return carry

        lax.fori_loop(0, group * piece * chunks, one_chunk, 0)
        out_ref[base * rows_left:base * rows_left + group_rows, :] = jnp.dot(
            cross_ref[...], table_ref[...], preferred_element_type=jnp.float32
        )


def pair_block(left_pieces, visit_pieces, lag_table):
    window_count, piece, width = left_pieces[0].shape
    left_count = len(left_pieces)
    visit_count = len(visit_pieces)
    rows_left = left_count * piece
    visit_rows = visit_count * piece
    lag_count = lag_table.shape[1]
    group = max(1, min(visit_count, 256 // (piece * rows_left)))
    while visit_count % group:
        group -= 1
    flops = visit_rows * rows_left * width * (4 * window_count + 2 * lag_count)
    vmem = pltpu.VMEM
    return pl.pallas_call(
        functools.partial(cross_kernel, left_count, visit_count),
        out_shape=jax.ShapeDtypeStruct((visit_rows * rows_left, lag_count), jnp.float32),
        in_specs=[pl.BlockSpec(memory_space=vmem)] * (left_count + visit_count + 1),
        out_specs=pl.BlockSpec(memory_space=vmem),
        scratch_shapes=[
            vmem((window_count, rows_left, width), jnp.float32),
            vmem((window_count, visit_rows, width), jnp.float32),
            vmem((group * piece * rows_left, width), jnp.bfloat16),
        ],
        compiler_params=pltpu.CompilerParams(vmem_limit_bytes=60 * 1024 * 1024),
        cost_estimate=pl.CostEstimate(
            flops=flops,
            transcendentals=0,
            bytes_accessed=2 * width * (window_count * (rows_left + visit_rows) + lag_count)
            + 4 * visit_rows * rows_left * lag_count,
        ),
    )(*left_pieces, *visit_pieces, lag_table)


def xor_gather(block, axis_name, size):
    if size & (size - 1):
        return [lax.all_gather(block, axis_name, axis=1, tiled=True)], None
    pieces = [block]
    for step in range(1, size):
        pairs = [(source, source ^ step) for source in range(size)]
        pieces.append(lax.ppermute(block, axis_name, pairs))
    order = lax.axis_index(axis_name) ^ jnp.arange(size, dtype=jnp.int32)
    return pieces, order


def on_device(records, fir_taps, lag_limit):
    block_size = records.shape[0]
    decimated = decimate(records, fir_taps)
    out_length = decimated.shape[-1]
    bin_count = out_length // 2
    spec_real, spec_imag = spectrum(decimated)
    white = whiten(spec_real, spec_imag)
    white_by_window = jnp.moveaxis(white, 1, 0)
    col_size = lax.axis_size("col")
    row_size = lax.axis_size("row")
    left_by_window, left_order = xor_gather(white_by_window, "col", col_size)
    cos_lag, sin_lag = angle_table(LAGS, bin_count, out_length, -LH)
    lag_table = jnp.concatenate([cos_lag.T, sin_lag.T], axis=0).astype(jnp.bfloat16)
    group_rows = sum(piece.shape[1] for piece in left_by_window)
    piece_rows, visit_order = xor_gather(white_by_window, "row", row_size)
    visit_count = sum(piece.shape[1] for piece in piece_rows)
    split = min(2, len(left_by_window))
    parts = [pair_block(left_by_window[:split], piece_rows, lag_table)]
    if len(left_by_window) > split:
        parts.append(pair_block(left_by_window[split:], piece_rows, lag_table))
    parts = [part.reshape(visit_count, -1, LAGS) for part in parts]
    pair = jnp.concatenate(parts, axis=1) if len(parts) > 1 else parts[0]
    pair = jnp.swapaxes(pair.reshape(visit_count, group_rows, LAGS), 0, 1)
    if visit_order is not None:
        pair = pair.reshape(group_rows, row_size, block_size, LAGS)
        pair = jnp.take(pair, visit_order, axis=1).reshape(group_rows, visit_count, LAGS)
    if left_order is not None:
        pair = pair.reshape(col_size, block_size, visit_count, LAGS)
        pair = jnp.take(pair, left_order, axis=0).reshape(group_rows, visit_count, LAGS)
    norm_scale = 1.0 / math.sqrt(white.shape[1] * bin_count)
    pair = pair * norm_scale
    lag_offset = jnp.abs(jnp.arange(LAGS, dtype=jnp.int32) - LH)
    keep_mask = lag_offset[None, :] <= lag_limit[:, None]
    tile_stack = jnp.where(keep_mask[:, None, :], pair, 0.0)
    return tile_stack[:, None]


def solution(mesh):
    placed = (P(("row", "col"), None, None), P(), P("row"))
    return jax.shard_map(
        on_device,
        mesh=mesh,
        in_specs=placed,
        out_specs=P("row", "col", None, None),
        check_vma=False,
    )
```

```python
import functools
import math

import jax
import jax.numpy as jnp
from jax import lax
from jax.experimental import pallas as pl
from jax.experimental.pallas import tpu as pltpu
from jax.sharding import PartitionSpec as P

DECIM = 2
LAGS = 128
BAND = 64
LH = 64


def angle_table(row_count, col_count, period, offset):
    row_ids = jnp.arange(row_count, dtype=jnp.int32)[:, None] + offset
    col_ids = jnp.arange(col_count, dtype=jnp.int32)[None, :]
    phase_int = jnp.mod(row_ids * col_ids, period)
    angles = phase_int.astype(jnp.float32) * (2.0 * math.pi / period)
    return (jnp.cos(angles), jnp.sin(angles))


def decimate(records, fir_taps):
    tap_count = fir_taps.shape[0]
    out_block = 128
    in_block = DECIM * out_block
    lead_dims = records.shape[:2]
    block_count = records.shape[2] // in_block
    blocks = records.reshape(lead_dims + (block_count, in_block))
    tails = blocks[:, :, :-1, in_block - tap_count :]
    tails = jnp.concatenate([jnp.zeros(lead_dims + (1, tap_count), records.dtype), tails], axis=2)
    windows = jnp.concatenate([tails, blocks], axis=3)
    tap_ids = jnp.arange(tap_count, dtype=jnp.int32)[:, None, None]
    in_ids = jnp.arange(in_block + tap_count, dtype=jnp.int32)[None, :, None]
    out_ids = jnp.arange(out_block, dtype=jnp.int32)[None, None, :]
    onehot = (in_ids == DECIM * out_ids + tap_count - tap_ids).astype(jnp.float32)
    band_matrix = jnp.einsum("k,kij->ij", fir_taps, onehot, precision=lax.Precision.HIGHEST)
    summed = jnp.einsum("swbi,ij->swbj", windows, band_matrix, precision=lax.Precision.HIGHEST)
    return summed.reshape(lead_dims + (block_count * out_block,))


def spectrum(decimated):
    out_length = decimated.shape[-1]
    first_len = 64
    second_len = out_length // first_len
    lead_dims = decimated.shape[:-1]
    blocks = decimated.reshape(lead_dims + (first_len, second_len))
    cos_one, sin_one = angle_table(first_len, first_len, first_len, 0)
    real_z = jnp.einsum("bwnq,fn->bwfq", blocks, cos_one, precision=lax.Precision.HIGHEST)
    imag_z = -jnp.einsum("bwnq,fn->bwfq", blocks, sin_one, precision=lax.Precision.HIGHEST)
    cos_two, sin_two = angle_table(first_len, second_len, out_length, 0)
    real_t = real_z * cos_two + imag_z * sin_two
    imag_t = imag_z * cos_two - real_z * sin_two
    cos_three, sin_three = angle_table(second_len // 2, second_len, second_len, 0)
    real_x = jnp.einsum(
        "bwfq,gq->bwgf", real_t, cos_three, precision=lax.Precision.HIGHEST
    ) + jnp.einsum("bwfq,gq->bwgf", imag_t, sin_three, precision=lax.Precision.HIGHEST)
    imag_x = jnp.einsum(
        "bwfq,gq->bwgf", imag_t, cos_three, precision=lax.Precision.HIGHEST
    ) - jnp.einsum("bwfq,gq->bwgf", real_t, sin_three, precision=lax.Precision.HIGHEST)
    bin_count = out_length // 2
    return (real_x.reshape(lead_dims + (bin_count,)), imag_x.reshape(lead_dims + (bin_count,)))


def whiten(spec_real, spec_imag):
    lead_dims = spec_real.shape[:-1]
    bin_count = spec_real.shape[-1]
    banded = lead_dims + (bin_count // BAND, BAND)
    squares = (spec_real * spec_real + spec_imag * spec_imag).reshape(banded)
    band_power = jnp.mean(squares, axis=-1, keepdims=True)
    inverse = 1.0 / jnp.sqrt(band_power + 1e-06)
    white_real = (spec_real.reshape(banded) * inverse).reshape(spec_real.shape)
    white_imag = (spec_imag.reshape(banded) * inverse).reshape(spec_imag.shape)
    return jnp.concatenate([white_real, white_imag], axis=-1).astype(jnp.bfloat16)


def cross_kernel(left_count, visit_count, *refs):
    left_refs = refs[:left_count]
    visit_refs = refs[left_count:left_count + visit_count]
    table_ref, out_ref, left_f32, visit_f32, cross_ref = refs[left_count + visit_count:]
    window_count, piece, width = left_refs[0].shape
    rows_left = left_f32.shape[1]
    bin_count = width // 2
    chunk = 512
    while chunk > 128 and chunk * rows_left > 8192:
        chunk //= 2
    chunks = bin_count // chunk
    group_rows = cross_ref.shape[0]
    group = group_rows // (piece * rows_left)

    for index, ref in enumerate(left_refs):
        left_f32[:, index * piece:(index + 1) * piece, :] = ref[...].astype(jnp.float32)
    for index, ref in enumerate(visit_refs):
        visit_f32[:, index * piece:(index + 1) * piece, :] = ref[...].astype(jnp.float32)

    for first in range(0, visit_count, group):
        base = first * piece

        def one_chunk(step, carry):
            local = step // chunks
            partner = base + local
            off = pl.multiple_of((step % chunks) * chunk, chunk)
            acc_re = jnp.zeros((rows_left, chunk), jnp.float32)
            acc_im = jnp.zeros((rows_left, chunk), jnp.float32)
            for window in range(window_count):
                left_c = left_f32[window, :, pl.ds(off, chunk)]
                left_d = left_f32[window, :, pl.ds(off + bin_count, chunk)]
                vis_c = visit_f32[window, pl.ds(partner, 1), pl.ds(off, chunk)]
                vis_d = visit_f32[window, pl.ds(partner, 1), pl.ds(off + bin_count, chunk)]
                acc_re = acc_re + (left_c * vis_c + left_d * vis_d)
                acc_im = acc_im + (left_c * vis_d - left_d * vis_c)
            row = pl.multiple_of(local * rows_left, rows_left)
            cross_ref[pl.ds(row, rows_left), pl.ds(off, chunk)] = acc_re.astype(jnp.bfloat16)
            cross_ref[pl.ds(row, rows_left), pl.ds(off + bin_count, chunk)] = acc_im.astype(jnp.bfloat16)
            return carry

        lax.fori_loop(0, group * piece * chunks, one_chunk, 0)
        out_ref[base * rows_left:base * rows_left + group_rows, :] = jnp.dot(
            cross_ref[...], table_ref[...], preferred_element_type=jnp.float32
        )


def pair_block(left_pieces, visit_pieces, lag_table):
    window_count, piece, width = left_pieces[0].shape
    left_count = len(left_pieces)
    visit_count = len(visit_pieces)
    rows_left = left_count * piece
    visit_rows = visit_count * piece
    lag_count = lag_table.shape[1]
    group = max(1, min(visit_count, 256 // (piece * rows_left)))
    while visit_count % group:
        group -= 1
    flops = visit_rows * rows_left * width * (4 * window_count + 2 * lag_count)
    vmem = pltpu.VMEM
    return pl.pallas_call(
        functools.partial(cross_kernel, left_count, visit_count),
        out_shape=jax.ShapeDtypeStruct((visit_rows * rows_left, lag_count), jnp.float32),
        in_specs=[pl.BlockSpec(memory_space=vmem)] * (left_count + visit_count + 1),
        out_specs=pl.BlockSpec(memory_space=vmem),
        scratch_shapes=[
            vmem((window_count, rows_left, width), jnp.float32),
            vmem((window_count, visit_rows, width), jnp.float32),
            vmem((group * piece * rows_left, width), jnp.bfloat16),
        ],
        compiler_params=pltpu.CompilerParams(vmem_limit_bytes=60 * 1024 * 1024),
        cost_estimate=pl.CostEstimate(
            flops=flops,
            transcendentals=0,
            bytes_accessed=2 * width * (window_count * (rows_left + visit_rows) + lag_count)
            + 4 * visit_rows * rows_left * lag_count,
        ),
    )(*left_pieces, *visit_pieces, lag_table)


def xor_gather(block, axis_name, size):
    if size & (size - 1):
        return [lax.all_gather(block, axis_name, axis=1, tiled=True)], None
    pieces = [block]
    for step in range(1, size):
        pairs = [(source, source ^ step) for source in range(size)]
        pieces.append(lax.ppermute(block, axis_name, pairs))
    order = lax.axis_index(axis_name) ^ jnp.arange(size, dtype=jnp.int32)
    return pieces, order


def chip_gather(block, axis_name, size):
    if size < 4 or size & (size - 1):
        return xor_gather(block, axis_name, size)
    chips = size // 2
    fetched = []
    for step in range(1, chips):
        pairs = [(source, source ^ (2 * step)) for source in range(size)]
        fetched.append(lax.ppermute(block, axis_name, pairs))
    partner = [(source, source ^ 1) for source in range(size)]
    pieces = [block, lax.ppermute(block, axis_name, partner)]
    swapped = lax.ppermute(fetched, axis_name, partner)
    for step in range(1, chips):
        pieces.append(fetched[step - 1])
        pieces.append(swapped[step - 1])
    order = lax.axis_index(axis_name) ^ jnp.arange(size, dtype=jnp.int32)
    return pieces, order


def on_device(records, fir_taps, lag_limit):
    block_size = records.shape[0]
    decimated = decimate(records, fir_taps)
    out_length = decimated.shape[-1]
    bin_count = out_length // 2
    spec_real, spec_imag = spectrum(decimated)
    white = whiten(spec_real, spec_imag)
    white_by_window = jnp.moveaxis(white, 1, 0)
    col_size = lax.axis_size("col")
    row_size = lax.axis_size("row")
    left_by_window, left_order = xor_gather(white_by_window, "col", col_size)
    cos_lag, sin_lag = angle_table(LAGS, bin_count, out_length, -LH)
    lag_table = jnp.concatenate([cos_lag.T, sin_lag.T], axis=0).astype(jnp.bfloat16)
    group_rows = sum(piece.shape[1] for piece in left_by_window)
    piece_rows, visit_order = chip_gather(white_by_window, "row", row_size)
    visit_count = sum(piece.shape[1] for piece in piece_rows)
    pair = pair_block(left_by_window, piece_rows, lag_table)
    pair = jnp.swapaxes(pair.reshape(visit_count, group_rows, LAGS), 0, 1)
    if visit_order is not None:
        pair = pair.reshape(group_rows, row_size, block_size, LAGS)
        pair = jnp.take(pair, visit_order, axis=1).reshape(group_rows, visit_count, LAGS)
    if left_order is not None:
        pair = pair.reshape(col_size, block_size, visit_count, LAGS)
        pair = jnp.take(pair, left_order, axis=0).reshape(group_rows, visit_count, LAGS)
    norm_scale = 1.0 / math.sqrt(white.shape[1] * bin_count)
    pair = pair * norm_scale
    lag_offset = jnp.abs(jnp.arange(LAGS, dtype=jnp.int32) - LH)
    keep_mask = lag_offset[None, :] <= lag_limit[:, None]
    tile_stack = jnp.where(keep_mask[:, None, :], pair, 0.0)
    return tile_stack[:, None]


def solution(mesh):
    placed = (P(("row", "col"), None, None), P(), P("row"))
    return jax.shard_map(
        on_device,
        mesh=mesh,
        in_specs=placed,
        out_specs=P("row", "col", None, None),
        check_vma=False,
    )
```

```python
import functools
import math

import jax
import jax.numpy as jnp
from jax import lax
from jax.experimental import pallas as pl
from jax.experimental.pallas import tpu as pltpu
from jax.sharding import PartitionSpec as P

DECIM = 2
LAGS = 128
BAND = 64
LH = 64


def angle_table(row_count, col_count, period, offset):
    row_ids = jnp.arange(row_count, dtype=jnp.int32)[:, None] + offset
    col_ids = jnp.arange(col_count, dtype=jnp.int32)[None, :]
    phase_int = jnp.mod(row_ids * col_ids, period)
    angles = phase_int.astype(jnp.float32) * (2.0 * math.pi / period)
    return (jnp.cos(angles), jnp.sin(angles))


def decimate(records, fir_taps):
    tap_count = fir_taps.shape[0]
    out_block = 128
    in_block = DECIM * out_block
    lead_dims = records.shape[:2]
    block_count = records.shape[2] // in_block
    blocks = records.reshape(lead_dims + (block_count, in_block))
    tails = blocks[:, :, :-1, in_block - tap_count :]
    tails = jnp.concatenate([jnp.zeros(lead_dims + (1, tap_count), records.dtype), tails], axis=2)
    windows = jnp.concatenate([tails, blocks], axis=3)
    tap_ids = jnp.arange(tap_count, dtype=jnp.int32)[:, None, None]
    in_ids = jnp.arange(in_block + tap_count, dtype=jnp.int32)[None, :, None]
    out_ids = jnp.arange(out_block, dtype=jnp.int32)[None, None, :]
    onehot = (in_ids == DECIM * out_ids + tap_count - tap_ids).astype(jnp.float32)
    band_matrix = jnp.einsum("k,kij->ij", fir_taps, onehot, precision=lax.Precision.HIGHEST)
    summed = jnp.einsum("swbi,ij->swbj", windows, band_matrix, precision=lax.Precision.HIGHEST)
    return summed.reshape(lead_dims + (block_count * out_block,))


def spectrum(decimated):
    out_length = decimated.shape[-1]
    first_len = 64
    second_len = out_length // first_len
    lead_dims = decimated.shape[:-1]
    blocks = decimated.reshape(lead_dims + (first_len, second_len))
    cos_one, sin_one = angle_table(first_len, first_len, first_len, 0)
    real_z = jnp.einsum("bwnq,fn->bwfq", blocks, cos_one, precision=lax.Precision.HIGHEST)
    imag_z = -jnp.einsum("bwnq,fn->bwfq", blocks, sin_one, precision=lax.Precision.HIGHEST)
    cos_two, sin_two = angle_table(first_len, second_len, out_length, 0)
    real_t = real_z * cos_two + imag_z * sin_two
    imag_t = imag_z * cos_two - real_z * sin_two
    cos_three, sin_three = angle_table(second_len // 2, second_len, second_len, 0)
    real_x = jnp.einsum(
        "bwfq,gq->bwgf", real_t, cos_three, precision=lax.Precision.HIGHEST
    ) + jnp.einsum("bwfq,gq->bwgf", imag_t, sin_three, precision=lax.Precision.HIGHEST)
    imag_x = jnp.einsum(
        "bwfq,gq->bwgf", imag_t, cos_three, precision=lax.Precision.HIGHEST
    ) - jnp.einsum("bwfq,gq->bwgf", real_t, sin_three, precision=lax.Precision.HIGHEST)
    bin_count = out_length // 2
    return (real_x.reshape(lead_dims + (bin_count,)), imag_x.reshape(lead_dims + (bin_count,)))


def whiten(spec_real, spec_imag):
    lead_dims = spec_real.shape[:-1]
    bin_count = spec_real.shape[-1]
    banded = lead_dims + (bin_count // BAND, BAND)
    squares = (spec_real * spec_real + spec_imag * spec_imag).reshape(banded)
    band_power = jnp.mean(squares, axis=-1, keepdims=True)
    inverse = 1.0 / jnp.sqrt(band_power + 1e-06)
    white_real = (spec_real.reshape(banded) * inverse).reshape(spec_real.shape)
    white_imag = (spec_imag.reshape(banded) * inverse).reshape(spec_imag.shape)
    return jnp.concatenate([white_real, white_imag], axis=-1).astype(jnp.bfloat16)


def cross_kernel(slots, *refs):
    piece_refs = refs[:len(slots)]
    table_ref, out_ref, left_f32, visit_f32, cross_ref = refs[len(slots):]
    left_refs = [ref for ref, slot in zip(piece_refs, slots) if slot[0] == 0]
    window_count, piece, width = left_refs[0].shape
    rows_left = left_f32.shape[1]
    bin_count = width // 2
    chunk = 512
    while chunk > 128 and chunk * rows_left > 8192:
        chunk //= 2
    chunks = bin_count // chunk
    group_rows = cross_ref.shape[0]
    group = group_rows // (piece * rows_left)
    visit_count = visit_f32.shape[1] // piece

    for ref, (kind, index) in zip(piece_refs, slots):
        target = left_f32 if kind == 0 else visit_f32
        target[:, index * piece:(index + 1) * piece, :] = ref[...].astype(jnp.float32)

    for first in range(0, visit_count, group):
        base = first * piece

        def one_chunk(step, carry):
            local = step // chunks
            partner = base + local
            off = pl.multiple_of((step % chunks) * chunk, chunk)
            acc_re = jnp.zeros((rows_left, chunk), jnp.float32)
            acc_im = jnp.zeros((rows_left, chunk), jnp.float32)
            for window in range(window_count):
                left_c = left_f32[window, :, pl.ds(off, chunk)]
                left_d = left_f32[window, :, pl.ds(off + bin_count, chunk)]
                vis_c = visit_f32[window, pl.ds(partner, 1), pl.ds(off, chunk)]
                vis_d = visit_f32[window, pl.ds(partner, 1), pl.ds(off + bin_count, chunk)]
                acc_re = acc_re + (left_c * vis_c + left_d * vis_d)
                acc_im = acc_im + (left_c * vis_d - left_d * vis_c)
            row = pl.multiple_of(local * rows_left, rows_left)
            cross_ref[pl.ds(row, rows_left), pl.ds(off, chunk)] = acc_re.astype(jnp.bfloat16)
            cross_ref[pl.ds(row, rows_left), pl.ds(off + bin_count, chunk)] = acc_im.astype(jnp.bfloat16)
            return carry

        lax.fori_loop(0, group * piece * chunks, one_chunk, 0)
        out_ref[base * rows_left:base * rows_left + group_rows, :] = jnp.dot(
            cross_ref[...], table_ref[...], preferred_element_type=jnp.float32
        )


def pair_block(left_pieces, visit_pieces, lag_table, issue_order):
    window_count, piece, width = left_pieces[0].shape
    left_count = len(left_pieces)
    visit_count = len(visit_pieces)
    rows_left = left_count * piece
    visit_rows = visit_count * piece
    lag_count = lag_table.shape[1]
    group = max(1, min(visit_count, 256 // (piece * rows_left)))
    while visit_count % group:
        group -= 1
    flops = visit_rows * rows_left * width * (4 * window_count + 2 * lag_count)
    vmem = pltpu.VMEM
    return pl.pallas_call(
        functools.partial(cross_kernel, tuple(issue_order)),
        out_shape=jax.ShapeDtypeStruct((visit_rows * rows_left, lag_count), jnp.float32),
        in_specs=[pl.BlockSpec(memory_space=vmem)] * (left_count + visit_count + 1),
        out_specs=pl.BlockSpec(memory_space=vmem),
        scratch_shapes=[
            vmem((window_count, rows_left, width), jnp.float32),
            vmem((window_count, visit_rows, width), jnp.float32),
            vmem((group * piece * rows_left, width), jnp.bfloat16),
        ],
        compiler_params=pltpu.CompilerParams(vmem_limit_bytes=60 * 1024 * 1024),
        cost_estimate=pl.CostEstimate(
            flops=flops,
            transcendentals=0,
            bytes_accessed=2 * width * (window_count * (rows_left + visit_rows) + lag_count)
            + 4 * visit_rows * rows_left * lag_count,
        ),
    )(*[(left_pieces, visit_pieces)[kind][index] for kind, index in issue_order], lag_table)


def xor_gather(block, axis_name, size):
    if size & (size - 1):
        return [lax.all_gather(block, axis_name, axis=1, tiled=True)], None
    pieces = [block]
    for step in range(1, size):
        pairs = [(source, source ^ step) for source in range(size)]
        pieces.append(lax.ppermute(block, axis_name, pairs))
    order = lax.axis_index(axis_name) ^ jnp.arange(size, dtype=jnp.int32)
    return pieces, order


def chip_gather(block, axis_name, size):
    if size < 4 or size & (size - 1):
        return xor_gather(block, axis_name, size)
    chips = size // 2
    fetched = []
    for step in range(1, chips):
        pairs = [(source, source ^ (2 * step)) for source in range(size)]
        fetched.append(lax.ppermute(block, axis_name, pairs))
    partner = [(source, source ^ 1) for source in range(size)]
    pieces = [block, lax.ppermute(block, axis_name, partner)]
    swapped = lax.ppermute(fetched, axis_name, partner)
    for step in range(1, chips):
        pieces.append(fetched[step - 1])
        pieces.append(swapped[step - 1])
    order = lax.axis_index(axis_name) ^ jnp.arange(size, dtype=jnp.int32)
    return pieces, order


def on_device(records, fir_taps, lag_limit):
    block_size = records.shape[0]
    decimated = decimate(records, fir_taps)
    out_length = decimated.shape[-1]
    bin_count = out_length // 2
    spec_real, spec_imag = spectrum(decimated)
    white = whiten(spec_real, spec_imag)
    white_by_window = jnp.moveaxis(white, 1, 0)
    col_size = lax.axis_size("col")
    row_size = lax.axis_size("row")
    left_by_window, left_order = xor_gather(white_by_window, "col", col_size)
    cos_lag, sin_lag = angle_table(LAGS, bin_count, out_length, -LH)
    lag_table = jnp.concatenate([cos_lag.T, sin_lag.T], axis=0).astype(jnp.bfloat16)
    group_rows = sum(piece.shape[1] for piece in left_by_window)
    piece_rows, visit_order = chip_gather(white_by_window, "row", row_size)
    visit_count = sum(piece.shape[1] for piece in piece_rows)
    late_first = [(1, index) for index in range(len(piece_rows)) if index > 1 and index % 2 == 1]
    near = [(0, 0), (1, 0), (0, 1), (1, 1)][:2 + min(1, len(left_by_window) - 1) + min(1, len(piece_rows) - 1)]
    fetches = [(1, index) for index in range(len(piece_rows)) if index > 1 and index % 2 == 0]
    far = [(0, index) for index in range(2, len(left_by_window))]
    issue_order = [slot for slot in late_first + near + fetches + far[::-1]]
    issue_order = sorted(set(issue_order), key=issue_order.index)
    assert len(issue_order) == len(left_by_window) + len(piece_rows)
    pair = pair_block(left_by_window, piece_rows, lag_table, issue_order)
    pair = jnp.swapaxes(pair.reshape(visit_count, group_rows, LAGS), 0, 1)
    if visit_order is not None:
        pair = pair.reshape(group_rows, row_size, block_size, LAGS)
        pair = jnp.take(pair, visit_order, axis=1).reshape(group_rows, visit_count, LAGS)
    if left_order is not None:
        pair = pair.reshape(col_size, block_size, visit_count, LAGS)
        pair = jnp.take(pair, left_order, axis=0).reshape(group_rows, visit_count, LAGS)
    norm_scale = 1.0 / math.sqrt(white.shape[1] * bin_count)
    pair = pair * norm_scale
    lag_offset = jnp.abs(jnp.arange(LAGS, dtype=jnp.int32) - LH)
    keep_mask = lag_offset[None, :] <= lag_limit[:, None]
    tile_stack = jnp.where(keep_mask[:, None, :], pair, 0.0)
    return tile_stack[:, None]


def solution(mesh):
    placed = (P(("row", "col"), None, None), P(), P("row"))
    return jax.shard_map(
        on_device,
        mesh=mesh,
        in_specs=placed,
        out_specs=P("row", "col", None, None),
        check_vma=False,
    )
```

```python
import functools
import math

import jax
import jax.numpy as jnp
from jax import lax
from jax.experimental import pallas as pl
from jax.experimental.pallas import tpu as pltpu
from jax.sharding import PartitionSpec as P

DECIM = 2
LAGS = 128
BAND = 64
LH = 64


def angle_table(row_count, col_count, period, offset):
    row_ids = jnp.arange(row_count, dtype=jnp.int32)[:, None] + offset
    col_ids = jnp.arange(col_count, dtype=jnp.int32)[None, :]
    phase_int = jnp.mod(row_ids * col_ids, period)
    angles = phase_int.astype(jnp.float32) * (2.0 * math.pi / period)
    return (jnp.cos(angles), jnp.sin(angles))


def decimate(records, fir_taps):
    tap_count = fir_taps.shape[0]
    out_block = 128
    in_block = DECIM * out_block
    lead_dims = records.shape[:2]
    block_count = records.shape[2] // in_block
    blocks = records.reshape(lead_dims + (block_count, in_block))
    tails = blocks[:, :, :-1, in_block - tap_count :]
    tails = jnp.concatenate([jnp.zeros(lead_dims + (1, tap_count), records.dtype), tails], axis=2)
    windows = jnp.concatenate([tails, blocks], axis=3)
    tap_ids = jnp.arange(tap_count, dtype=jnp.int32)[:, None, None]
    in_ids = jnp.arange(in_block + tap_count, dtype=jnp.int32)[None, :, None]
    out_ids = jnp.arange(out_block, dtype=jnp.int32)[None, None, :]
    onehot = (in_ids == DECIM * out_ids + tap_count - tap_ids).astype(jnp.float32)
    band_matrix = jnp.einsum("k,kij->ij", fir_taps, onehot, precision=lax.Precision.HIGH)
    summed = jnp.einsum("swbi,ij->swbj", windows, band_matrix, precision=lax.Precision.HIGH)
    return summed.reshape(lead_dims + (block_count * out_block,))


def spectrum(decimated):
    out_length = decimated.shape[-1]
    first_len = 64
    second_len = out_length // first_len
    lead_dims = decimated.shape[:-1]
    blocks = decimated.reshape(lead_dims + (first_len, second_len))
    cos_one, sin_one = angle_table(first_len, first_len, first_len, 0)
    real_z = jnp.einsum("bwnq,fn->bwfq", blocks, cos_one, precision=lax.Precision.HIGH)
    imag_z = -jnp.einsum("bwnq,fn->bwfq", blocks, sin_one, precision=lax.Precision.HIGH)
    cos_two, sin_two = angle_table(first_len, second_len, out_length, 0)
    real_t = real_z * cos_two + imag_z * sin_two
    imag_t = imag_z * cos_two - real_z * sin_two
    cos_three, sin_three = angle_table(second_len // 2, second_len, second_len, 0)
    real_x = jnp.einsum(
        "bwfq,gq->bwgf", real_t, cos_three, precision=lax.Precision.HIGH
    ) + jnp.einsum("bwfq,gq->bwgf", imag_t, sin_three, precision=lax.Precision.HIGH)
    imag_x = jnp.einsum(
        "bwfq,gq->bwgf", imag_t, cos_three, precision=lax.Precision.HIGH
    ) - jnp.einsum("bwfq,gq->bwgf", real_t, sin_three, precision=lax.Precision.HIGH)
    bin_count = out_length // 2
    return (real_x.reshape(lead_dims + (bin_count,)), imag_x.reshape(lead_dims + (bin_count,)))


def whiten(spec_real, spec_imag):
    lead_dims = spec_real.shape[:-1]
    bin_count = spec_real.shape[-1]
    banded = lead_dims + (bin_count // BAND, BAND)
    squares = (spec_real * spec_real + spec_imag * spec_imag).reshape(banded)
    band_power = jnp.mean(squares, axis=-1, keepdims=True)
    inverse = 1.0 / jnp.sqrt(band_power + 1e-06)
    white_real = (spec_real.reshape(banded) * inverse).reshape(spec_real.shape)
    white_imag = (spec_imag.reshape(banded) * inverse).reshape(spec_imag.shape)
    return jnp.concatenate([white_real, white_imag], axis=-1).astype(jnp.bfloat16)


def cross_kernel(left_count, visit_count, *refs):
    left_refs = refs[:left_count]
    visit_refs = refs[left_count:left_count + visit_count]
    table_ref, out_ref, left_f32, visit_f32, cross_ref = refs[left_count + visit_count:]
    window_count, piece, width = left_refs[0].shape
    rows_left = left_f32.shape[1]
    bin_count = width // 2
    chunk = 512
    while chunk > 128 and chunk * rows_left > 8192:
        chunk //= 2
    chunks = bin_count // chunk
    group_rows = cross_ref.shape[0]
    group = group_rows // (piece * rows_left)

    for index, ref in enumerate(left_refs):
        left_f32[:, index * piece:(index + 1) * piece, :] = ref[...].astype(jnp.float32)
    for index, ref in enumerate(visit_refs):
        visit_f32[:, index * piece:(index + 1) * piece, :] = ref[...].astype(jnp.float32)

    for first in range(0, visit_count, group):
        base = first * piece

        def one_chunk(step, carry):
            local = step // chunks
            partner = base + local
            off = pl.multiple_of((step % chunks) * chunk, chunk)
            acc_re = jnp.zeros((rows_left, chunk), jnp.float32)
            acc_im = jnp.zeros((rows_left, chunk), jnp.float32)
            for window in range(window_count):
                left_c = left_f32[window, :, pl.ds(off, chunk)]
                left_d = left_f32[window, :, pl.ds(off + bin_count, chunk)]
                vis_c = visit_f32[window, pl.ds(partner, 1), pl.ds(off, chunk)]
                vis_d = visit_f32[window, pl.ds(partner, 1), pl.ds(off + bin_count, chunk)]
                acc_re = acc_re + (left_c * vis_c + left_d * vis_d)
                acc_im = acc_im + (left_c * vis_d - left_d * vis_c)
            row = pl.multiple_of(local * rows_left, rows_left)
            cross_ref[pl.ds(row, rows_left), pl.ds(off, chunk)] = acc_re.astype(jnp.bfloat16)
            cross_ref[pl.ds(row, rows_left), pl.ds(off + bin_count, chunk)] = acc_im.astype(jnp.bfloat16)
            return carry

        lax.fori_loop(0, group * piece * chunks, one_chunk, 0)
        out_ref[base * rows_left:base * rows_left + group_rows, :] = jnp.dot(
            cross_ref[...], table_ref[...], preferred_element_type=jnp.float32
        )


def pair_block(left_pieces, visit_pieces, lag_table):
    window_count, piece, width = left_pieces[0].shape
    left_count = len(left_pieces)
    visit_count = len(visit_pieces)
    rows_left = left_count * piece
    visit_rows = visit_count * piece
    lag_count = lag_table.shape[1]
    group = max(1, min(visit_count, 256 // (piece * rows_left)))
    while visit_count % group:
        group -= 1
    flops = visit_rows * rows_left * width * (4 * window_count + 2 * lag_count)
    vmem = pltpu.VMEM
    return pl.pallas_call(
        functools.partial(cross_kernel, left_count, visit_count),
        out_shape=jax.ShapeDtypeStruct((visit_rows * rows_left, lag_count), jnp.float32),
        in_specs=[pl.BlockSpec(memory_space=vmem)] * (left_count + visit_count + 1),
        out_specs=pl.BlockSpec(memory_space=vmem),
        scratch_shapes=[
            vmem((window_count, rows_left, width), jnp.float32),
            vmem((window_count, visit_rows, width), jnp.float32),
            vmem((group * piece * rows_left, width), jnp.bfloat16),
        ],
        compiler_params=pltpu.CompilerParams(vmem_limit_bytes=60 * 1024 * 1024),
        cost_estimate=pl.CostEstimate(
            flops=flops,
            transcendentals=0,
            bytes_accessed=2 * width * (window_count * (rows_left + visit_rows) + lag_count)
            + 4 * visit_rows * rows_left * lag_count,
        ),
    )(*left_pieces, *visit_pieces, lag_table)


def xor_gather(block, axis_name, size):
    if size & (size - 1):
        return [lax.all_gather(block, axis_name, axis=1, tiled=True)], None
    pieces = [block]
    for step in range(1, size):
        pairs = [(source, source ^ step) for source in range(size)]
        pieces.append(lax.ppermute(block, axis_name, pairs))
    order = lax.axis_index(axis_name) ^ jnp.arange(size, dtype=jnp.int32)
    return pieces, order


def chip_gather(block, axis_name, size):
    if size < 4 or size & (size - 1):
        return xor_gather(block, axis_name, size)
    chips = size // 2
    fetched = []
    for step in range(1, chips):
        pairs = [(source, source ^ (2 * step)) for source in range(size)]
        fetched.append(lax.ppermute(block, axis_name, pairs))
    partner = [(source, source ^ 1) for source in range(size)]
    pieces = [block, lax.ppermute(block, axis_name, partner)]
    swapped = lax.ppermute(fetched, axis_name, partner)
    for step in range(1, chips):
        pieces.append(fetched[step - 1])
        pieces.append(swapped[step - 1])
    order = lax.axis_index(axis_name) ^ jnp.arange(size, dtype=jnp.int32)
    return pieces, order


def on_device(records, fir_taps, lag_limit):
    block_size = records.shape[0]
    decimated = decimate(records, fir_taps)
    out_length = decimated.shape[-1]
    bin_count = out_length // 2
    spec_real, spec_imag = spectrum(decimated)
    white = whiten(spec_real, spec_imag)
    white_by_window = jnp.moveaxis(white, 1, 0)
    col_size = lax.axis_size("col")
    row_size = lax.axis_size("row")
    left_by_window, left_order = xor_gather(white_by_window, "col", col_size)
    cos_lag, sin_lag = angle_table(LAGS, bin_count, out_length, -LH)
    lag_table = jnp.concatenate([cos_lag.T, sin_lag.T], axis=0).astype(jnp.bfloat16)
    group_rows = sum(piece.shape[1] for piece in left_by_window)
    piece_rows, visit_order = chip_gather(white_by_window, "row", row_size)
    visit_count = sum(piece.shape[1] for piece in piece_rows)
    pair = pair_block(left_by_window, piece_rows, lag_table)
    pair = jnp.swapaxes(pair.reshape(visit_count, group_rows, LAGS), 0, 1)
    if visit_order is not None:
        pair = pair.reshape(group_rows, row_size, block_size, LAGS)
        pair = jnp.take(pair, visit_order, axis=1).reshape(group_rows, visit_count, LAGS)
    if left_order is not None:
        pair = pair.reshape(col_size, block_size, visit_count, LAGS)
        pair = jnp.take(pair, left_order, axis=0).reshape(group_rows, visit_count, LAGS)
    norm_scale = 1.0 / math.sqrt(white.shape[1] * bin_count)
    pair = pair * norm_scale
    lag_offset = jnp.abs(jnp.arange(LAGS, dtype=jnp.int32) - LH)
    keep_mask = lag_offset[None, :] <= lag_limit[:, None]
    tile_stack = jnp.where(keep_mask[:, None, :], pair, 0.0)
    return tile_stack[:, None]


def solution(mesh):
    placed = (P(("row", "col"), None, None), P(), P("row"))
    return jax.shard_map(
        on_device,
        mesh=mesh,
        in_specs=placed,
        out_specs=P("row", "col", None, None),
        check_vma=False,
    )
```

```python
import functools
import math

import jax
import jax.numpy as jnp
from jax import lax
from jax.experimental import pallas as pl
from jax.experimental.pallas import tpu as pltpu
from jax.sharding import PartitionSpec as P

DECIM = 2
LAGS = 128
BAND = 64
LH = 64


def angle_table(row_count, col_count, period, offset):
    row_ids = jnp.arange(row_count, dtype=jnp.int32)[:, None] + offset
    col_ids = jnp.arange(col_count, dtype=jnp.int32)[None, :]
    phase_int = jnp.mod(row_ids * col_ids, period)
    angles = phase_int.astype(jnp.float32) * (2.0 * math.pi / period)
    return (jnp.cos(angles), jnp.sin(angles))


def decimate(records, fir_taps):
    tap_count = fir_taps.shape[0]
    out_block = 128
    in_block = DECIM * out_block
    lead_dims = records.shape[:2]
    block_count = records.shape[2] // in_block
    blocks = records.reshape(lead_dims + (block_count, in_block))
    tails = blocks[:, :, :-1, in_block - tap_count :]
    tails = jnp.concatenate([jnp.zeros(lead_dims + (1, tap_count), records.dtype), tails], axis=2)
    windows = jnp.concatenate([tails, blocks], axis=3)
    tap_ids = jnp.arange(tap_count, dtype=jnp.int32)[:, None, None]
    in_ids = jnp.arange(in_block + tap_count, dtype=jnp.int32)[None, :, None]
    out_ids = jnp.arange(out_block, dtype=jnp.int32)[None, None, :]
    onehot = (in_ids == DECIM * out_ids + tap_count - tap_ids).astype(jnp.float32)
    band_matrix = jnp.einsum("k,kij->ij", fir_taps, onehot, precision=lax.Precision.HIGH)
    summed = jnp.einsum("swbi,ij->swbj", windows, band_matrix, precision=lax.Precision.HIGH)
    return summed.reshape(lead_dims + (block_count * out_block,))


def spectrum(decimated):
    out_length = decimated.shape[-1]
    first_len = 64
    second_len = out_length // first_len
    lead_dims = decimated.shape[:-1]
    blocks = decimated.reshape(lead_dims + (first_len, second_len))
    cos_one, sin_one = angle_table(first_len, first_len, first_len, 0)
    real_z = jnp.einsum("bwnq,fn->bwfq", blocks, cos_one, precision=lax.Precision.HIGH)
    imag_z = -jnp.einsum("bwnq,fn->bwfq", blocks, sin_one, precision=lax.Precision.HIGH)
    cos_two, sin_two = angle_table(first_len, second_len, out_length, 0)
    real_t = real_z * cos_two + imag_z * sin_two
    imag_t = imag_z * cos_two - real_z * sin_two
    cos_three, sin_three = angle_table(second_len // 2, second_len, second_len, 0)
    real_x = jnp.einsum(
        "bwfq,gq->bwgf", real_t, cos_three, precision=lax.Precision.HIGH
    ) + jnp.einsum("bwfq,gq->bwgf", imag_t, sin_three, precision=lax.Precision.HIGH)
    imag_x = jnp.einsum(
        "bwfq,gq->bwgf", imag_t, cos_three, precision=lax.Precision.HIGH
    ) - jnp.einsum("bwfq,gq->bwgf", real_t, sin_three, precision=lax.Precision.HIGH)
    bin_count = out_length // 2
    return (real_x.reshape(lead_dims + (bin_count,)), imag_x.reshape(lead_dims + (bin_count,)))


def whiten(spec_real, spec_imag):
    lead_dims = spec_real.shape[:-1]
    bin_count = spec_real.shape[-1]
    banded = lead_dims + (bin_count // BAND, BAND)
    squares = (spec_real * spec_real + spec_imag * spec_imag).reshape(banded)
    band_power = jnp.mean(squares, axis=-1, keepdims=True)
    inverse = 1.0 / jnp.sqrt(band_power + 1e-06)
    white_real = (spec_real.reshape(banded) * inverse).reshape(spec_real.shape)
    white_imag = (spec_imag.reshape(banded) * inverse).reshape(spec_imag.shape)
    return jnp.concatenate([white_real, white_imag], axis=-1).astype(jnp.bfloat16)


def cross_kernel(left_count, visit_count, *refs):
    left_refs = refs[:left_count]
    visit_refs = refs[left_count:left_count + visit_count]
    table_ref, out_ref, left_f32, visit_f32, cross_ref = refs[left_count + visit_count:]
    window_count, piece, width = left_refs[0].shape
    rows_left = left_f32.shape[1]
    bin_count = width // 2
    chunk = 512
    while chunk > 128 and chunk * rows_left > 8192:
        chunk //= 2
    chunks = bin_count // chunk
    group_rows = cross_ref.shape[0]
    group = group_rows // (piece * rows_left)

    for index, ref in enumerate(left_refs):
        left_f32[:, index * piece:(index + 1) * piece, :] = ref[...].astype(jnp.float32)
    for index, ref in enumerate(visit_refs):
        visit_f32[:, index * piece:(index + 1) * piece, :] = ref[...].astype(jnp.float32)

    for first in range(0, visit_count, group):
        base = first * piece

        def one_chunk(step, carry):
            local = step // chunks
            partner = base + local
            off = pl.multiple_of((step % chunks) * chunk, chunk)
            acc_re = jnp.zeros((rows_left, chunk), jnp.float32)
            acc_im = jnp.zeros((rows_left, chunk), jnp.float32)
            for window in range(window_count):
                left_c = left_f32[window, :, pl.ds(off, chunk)]
                left_d = left_f32[window, :, pl.ds(off + bin_count, chunk)]
                vis_c = visit_f32[window, pl.ds(partner, 1), pl.ds(off, chunk)]
                vis_d = visit_f32[window, pl.ds(partner, 1), pl.ds(off + bin_count, chunk)]
                acc_re = acc_re + (left_c * vis_c + left_d * vis_d)
                acc_im = acc_im + (left_c * vis_d - left_d * vis_c)
            row = pl.multiple_of(local * rows_left, rows_left)
            cross_ref[pl.ds(row, rows_left), pl.ds(off, chunk)] = acc_re.astype(jnp.bfloat16)
            cross_ref[pl.ds(row, rows_left), pl.ds(off + bin_count, chunk)] = acc_im.astype(jnp.bfloat16)
            return carry

        lax.fori_loop(0, group * piece * chunks, one_chunk, 0)
        out_ref[base * rows_left:base * rows_left + group_rows, :] = jnp.dot(
            cross_ref[...], table_ref[...], preferred_element_type=jnp.float32
        )


def pair_block(left_pieces, visit_pieces, lag_table):
    window_count, piece, width = left_pieces[0].shape
    left_count = len(left_pieces)
    visit_count = len(visit_pieces)
    rows_left = left_count * piece
    visit_rows = visit_count * piece
    lag_count = lag_table.shape[1]
    group = max(1, min(visit_count, 256 // (piece * rows_left)))
    while visit_count % group:
        group -= 1
    flops = visit_rows * rows_left * width * (4 * window_count + 2 * lag_count)
    vmem = pltpu.VMEM
    return pl.pallas_call(
        functools.partial(cross_kernel, left_count, visit_count),
        out_shape=jax.ShapeDtypeStruct((visit_rows * rows_left, lag_count), jnp.float32),
        in_specs=[pl.BlockSpec(memory_space=vmem)] * (left_count + visit_count + 1),
        out_specs=pl.BlockSpec(memory_space=vmem),
        scratch_shapes=[
            vmem((window_count, rows_left, width), jnp.float32),
            vmem((window_count, visit_rows, width), jnp.float32),
            vmem((group * piece * rows_left, width), jnp.bfloat16),
        ],
        compiler_params=pltpu.CompilerParams(vmem_limit_bytes=60 * 1024 * 1024),
        cost_estimate=pl.CostEstimate(
            flops=flops,
            transcendentals=0,
            bytes_accessed=2 * width * (window_count * (rows_left + visit_rows) + lag_count)
            + 4 * visit_rows * rows_left * lag_count,
        ),
    )(*left_pieces, *visit_pieces, lag_table)


def xor_gather(block, axis_name, size):
    if size & (size - 1):
        return [lax.all_gather(block, axis_name, axis=1, tiled=True)], None
    pieces = [block]
    for step in range(1, size):
        pairs = [(source, source ^ step) for source in range(size)]
        pieces.append(lax.ppermute(block, axis_name, pairs))
    order = lax.axis_index(axis_name) ^ jnp.arange(size, dtype=jnp.int32)
    return pieces, order


def line_gather(block, axis_name, size):
    if size != 4:
        return xor_gather(block, axis_name, size)
    outer = lax.ppermute(block, axis_name, [(0, 1), (1, 0), (2, 3), (3, 2)])
    middle = lax.ppermute(block, axis_name, [(1, 2), (2, 1)])
    outward = lax.ppermute(middle, axis_name, [(1, 0), (2, 3)])
    inward = lax.ppermute(outer, axis_name, [(1, 2), (2, 1)])
    last = lax.ppermute(inward, axis_name, [(1, 0), (2, 3)])
    me = lax.axis_index(axis_name)
    is_end = (me == 0) | (me == size - 1)
    third = jnp.where(is_end, outward, middle)
    fourth = jnp.where(is_end, last, inward)
    table = jnp.array([[0, 1, 2, 3], [1, 0, 2, 3], [3, 2, 0, 1], [3, 2, 1, 0]], jnp.int32)
    return [block, outer, third, fourth], table[me]


def chip_gather(block, axis_name, size):
    if size < 4 or size & (size - 1):
        return xor_gather(block, axis_name, size)
    chips = size // 2
    fetched = []
    for step in range(1, chips):
        pairs = [(source, source ^ (2 * step)) for source in range(size)]
        fetched.append(lax.ppermute(block, axis_name, pairs))
    partner = [(source, source ^ 1) for source in range(size)]
    pieces = [block, lax.ppermute(block, axis_name, partner)]
    swapped = lax.ppermute(fetched, axis_name, partner)
    for step in range(1, chips):
        pieces.append(fetched[step - 1])
        pieces.append(swapped[step - 1])
    order = lax.axis_index(axis_name) ^ jnp.arange(size, dtype=jnp.int32)
    return pieces, order


def on_device(records, fir_taps, lag_limit):
    block_size = records.shape[0]
    decimated = decimate(records, fir_taps)
    out_length = decimated.shape[-1]
    bin_count = out_length // 2
    spec_real, spec_imag = spectrum(decimated)
    white = whiten(spec_real, spec_imag)
    white_by_window = jnp.moveaxis(white, 1, 0)
    col_size = lax.axis_size("col")
    row_size = lax.axis_size("row")
    left_by_window, left_order = line_gather(white_by_window, "col", col_size)
    cos_lag, sin_lag = angle_table(LAGS, bin_count, out_length, -LH)
    lag_table = jnp.concatenate([cos_lag.T, sin_lag.T], axis=0).astype(jnp.bfloat16)
    group_rows = sum(piece.shape[1] for piece in left_by_window)
    piece_rows, visit_order = chip_gather(white_by_window, "row", row_size)
    visit_count = sum(piece.shape[1] for piece in piece_rows)
    pair = pair_block(left_by_window, piece_rows, lag_table)
    pair = jnp.swapaxes(pair.reshape(visit_count, group_rows, LAGS), 0, 1)
    if visit_order is not None:
        pair = pair.reshape(group_rows, row_size, block_size, LAGS)
        pair = jnp.take(pair, visit_order, axis=1).reshape(group_rows, visit_count, LAGS)
    if left_order is not None:
        pair = pair.reshape(col_size, block_size, visit_count, LAGS)
        pair = jnp.take(pair, left_order, axis=0).reshape(group_rows, visit_count, LAGS)
    norm_scale = 1.0 / math.sqrt(white.shape[1] * bin_count)
    pair = pair * norm_scale
    lag_offset = jnp.abs(jnp.arange(LAGS, dtype=jnp.int32) - LH)
    keep_mask = lag_offset[None, :] <= lag_limit[:, None]
    tile_stack = jnp.where(keep_mask[:, None, :], pair, 0.0)
    return tile_stack[:, None]


def solution(mesh):
    placed = (P(("row", "col"), None, None), P(), P("row"))
    return jax.shard_map(
        on_device,
        mesh=mesh,
        in_specs=placed,
        out_specs=P("row", "col", None, None),
        check_vma=False,
    )
```

```python
import functools
import math

import jax
import jax.numpy as jnp
from jax import lax
from jax.experimental import pallas as pl
from jax.experimental.pallas import tpu as pltpu
from jax.sharding import PartitionSpec as P

DECIM = 2
LAGS = 128
BAND = 64
LH = 64


def angle_table(row_count, col_count, period, offset):
    row_ids = jnp.arange(row_count, dtype=jnp.int32)[:, None] + offset
    col_ids = jnp.arange(col_count, dtype=jnp.int32)[None, :]
    phase_int = jnp.mod(row_ids * col_ids, period)
    angles = phase_int.astype(jnp.float32) * (2.0 * math.pi / period)
    return (jnp.cos(angles), jnp.sin(angles))


def decimate(records, fir_taps):
    tap_count = fir_taps.shape[0]
    out_block = 128
    in_block = DECIM * out_block
    lead_dims = records.shape[:2]
    block_count = records.shape[2] // in_block
    blocks = records.reshape(lead_dims + (block_count, in_block))
    tails = blocks[:, :, :-1, in_block - tap_count :]
    tails = jnp.concatenate([jnp.zeros(lead_dims + (1, tap_count), records.dtype), tails], axis=2)
    windows = jnp.concatenate([tails, blocks], axis=3)
    tap_ids = jnp.arange(tap_count, dtype=jnp.int32)[:, None, None]
    in_ids = jnp.arange(in_block + tap_count, dtype=jnp.int32)[None, :, None]
    out_ids = jnp.arange(out_block, dtype=jnp.int32)[None, None, :]
    onehot = (in_ids == DECIM * out_ids + tap_count - tap_ids).astype(jnp.float32)
    band_matrix = jnp.einsum("k,kij->ij", fir_taps, onehot, precision=lax.Precision.HIGH)
    summed = jnp.einsum("swbi,ij->swbj", windows, band_matrix, precision=lax.Precision.HIGH)
    return summed.reshape(lead_dims + (block_count * out_block,))


def spectrum(decimated):
    out_length = decimated.shape[-1]
    first_len = 64
    second_len = out_length // first_len
    lead_dims = decimated.shape[:-1]
    blocks = decimated.reshape(lead_dims + (first_len, second_len))
    cos_one, sin_one = angle_table(first_len, first_len, first_len, 0)
    real_z = jnp.einsum("bwnq,fn->bwfq", blocks, cos_one, precision=lax.Precision.HIGH)
    imag_z = -jnp.einsum("bwnq,fn->bwfq", blocks, sin_one, precision=lax.Precision.HIGH)
    cos_two, sin_two = angle_table(first_len, second_len, out_length, 0)
    real_t = real_z * cos_two + imag_z * sin_two
    imag_t = imag_z * cos_two - real_z * sin_two
    cos_three, sin_three = angle_table(second_len // 2, second_len, second_len, 0)
    real_x = jnp.einsum(
        "bwfq,gq->bwgf", real_t, cos_three, precision=lax.Precision.HIGH
    ) + jnp.einsum("bwfq,gq->bwgf", imag_t, sin_three, precision=lax.Precision.HIGH)
    imag_x = jnp.einsum(
        "bwfq,gq->bwgf", imag_t, cos_three, precision=lax.Precision.HIGH
    ) - jnp.einsum("bwfq,gq->bwgf", real_t, sin_three, precision=lax.Precision.HIGH)
    bin_count = out_length // 2
    return (real_x.reshape(lead_dims + (bin_count,)), imag_x.reshape(lead_dims + (bin_count,)))


def whiten(spec_real, spec_imag):
    lead_dims = spec_real.shape[:-1]
    bin_count = spec_real.shape[-1]
    banded = lead_dims + (bin_count // BAND, BAND)
    squares = (spec_real * spec_real + spec_imag * spec_imag).reshape(banded)
    band_power = jnp.mean(squares, axis=-1, keepdims=True)
    inverse = 1.0 / jnp.sqrt(band_power + 1e-06)
    white_real = (spec_real.reshape(banded) * inverse).reshape(spec_real.shape)
    white_imag = (spec_imag.reshape(banded) * inverse).reshape(spec_imag.shape)
    return jnp.concatenate([white_real, white_imag], axis=-1).astype(jnp.bfloat16)


def cross_kernel(left_count, visit_count, *refs):
    left_refs = refs[:left_count]
    visit_refs = refs[left_count:left_count + visit_count]
    table_ref, out_ref, left_f32, visit_f32, cross_ref = refs[left_count + visit_count:]
    window_count, piece, width = left_refs[0].shape
    rows_left = left_f32.shape[1]
    bin_count = width // 2
    chunk = 512
    while chunk > 128 and chunk * rows_left > 8192:
        chunk //= 2
    chunks = bin_count // chunk
    group_rows = cross_ref.shape[0]
    group = group_rows // (piece * rows_left)

    for index, ref in enumerate(left_refs):
        left_f32[:, index * piece:(index + 1) * piece, :] = ref[...].astype(jnp.float32)
    for index, ref in enumerate(visit_refs):
        visit_f32[:, index * piece:(index + 1) * piece, :] = ref[...].astype(jnp.float32)

    for first in range(0, visit_count, group):
        base = first * piece

        def one_chunk(step, carry):
            local = step // chunks
            partner = base + local
            off = pl.multiple_of((step % chunks) * chunk, chunk)
            acc_re = jnp.zeros((rows_left, chunk), jnp.float32)
            acc_im = jnp.zeros((rows_left, chunk), jnp.float32)
            for window in range(window_count):
                left_c = left_f32[window, :, pl.ds(off, chunk)]
                left_d = left_f32[window, :, pl.ds(off + bin_count, chunk)]
                vis_c = visit_f32[window, pl.ds(partner, 1), pl.ds(off, chunk)]
                vis_d = visit_f32[window, pl.ds(partner, 1), pl.ds(off + bin_count, chunk)]
                acc_re = acc_re + (left_c * vis_c + left_d * vis_d)
                acc_im = acc_im + (left_c * vis_d - left_d * vis_c)
            row = pl.multiple_of(local * rows_left, rows_left)
            cross_ref[pl.ds(row, rows_left), pl.ds(off, chunk)] = acc_re.astype(jnp.bfloat16)
            cross_ref[pl.ds(row, rows_left), pl.ds(off + bin_count, chunk)] = acc_im.astype(jnp.bfloat16)
            return carry

        lax.fori_loop(0, group * piece * chunks, one_chunk, 0)
        out_ref[base * rows_left:base * rows_left + group_rows, :] = jnp.dot(
            cross_ref[...], table_ref[...], preferred_element_type=jnp.float32
        )


def pair_block(left_pieces, visit_pieces, lag_table):
    window_count, piece, width = left_pieces[0].shape
    left_count = len(left_pieces)
    visit_count = len(visit_pieces)
    rows_left = left_count * piece
    visit_rows = visit_count * piece
    lag_count = lag_table.shape[1]
    group = max(1, min(visit_count, 256 // (piece * rows_left)))
    while visit_count % group:
        group -= 1
    flops = visit_rows * rows_left * width * (4 * window_count + 2 * lag_count)
    vmem = pltpu.VMEM
    return pl.pallas_call(
        functools.partial(cross_kernel, left_count, visit_count),
        out_shape=jax.ShapeDtypeStruct((visit_rows * rows_left, lag_count), jnp.float32),
        in_specs=[pl.BlockSpec(memory_space=vmem)] * (left_count + visit_count + 1),
        out_specs=pl.BlockSpec(memory_space=vmem),
        scratch_shapes=[
            vmem((window_count, rows_left, width), jnp.float32),
            vmem((window_count, visit_rows, width), jnp.float32),
            vmem((group * piece * rows_left, width), jnp.bfloat16),
        ],
        compiler_params=pltpu.CompilerParams(vmem_limit_bytes=60 * 1024 * 1024),
        cost_estimate=pl.CostEstimate(
            flops=flops,
            transcendentals=0,
            bytes_accessed=2 * width * (window_count * (rows_left + visit_rows) + lag_count)
            + 4 * visit_rows * rows_left * lag_count,
        ),
    )(*left_pieces, *visit_pieces, lag_table)


def xor_gather(block, axis_name, size):
    if size & (size - 1):
        return [lax.all_gather(block, axis_name, axis=1, tiled=True)], None
    pieces = [block]
    for step in range(1, size):
        pairs = [(source, source ^ step) for source in range(size)]
        pieces.append(lax.ppermute(block, axis_name, pairs))
    order = lax.axis_index(axis_name) ^ jnp.arange(size, dtype=jnp.int32)
    return pieces, order


def chip_gather(block, axis_name, size):
    if size < 4 or size & (size - 1):
        return xor_gather(block, axis_name, size)
    chips = size // 2
    fetched = []
    for step in range(1, chips):
        pairs = [(source, source ^ (2 * step)) for source in range(size)]
        fetched.append(lax.ppermute(block, axis_name, pairs))
    partner = [(source, source ^ 1) for source in range(size)]
    pieces = [block, lax.ppermute(block, axis_name, partner)]
    piece = block.shape[1]
    swapped = lax.ppermute(jnp.concatenate(fetched, axis=1), axis_name, partner)
    for step in range(1, chips):
        pieces.append(fetched[step - 1])
        pieces.append(swapped[:, (step - 1) * piece:step * piece, :])
    order = lax.axis_index(axis_name) ^ jnp.arange(size, dtype=jnp.int32)
    return pieces, order


def on_device(records, fir_taps, lag_limit):
    block_size = records.shape[0]
    decimated = decimate(records, fir_taps)
    out_length = decimated.shape[-1]
    bin_count = out_length // 2
    spec_real, spec_imag = spectrum(decimated)
    white = whiten(spec_real, spec_imag)
    white_by_window = jnp.moveaxis(white, 1, 0)
    col_size = lax.axis_size("col")
    row_size = lax.axis_size("row")
    left_by_window, left_order = xor_gather(white_by_window, "col", col_size)
    cos_lag, sin_lag = angle_table(LAGS, bin_count, out_length, -LH)
    lag_table = jnp.concatenate([cos_lag.T, sin_lag.T], axis=0).astype(jnp.bfloat16)
    group_rows = sum(piece.shape[1] for piece in left_by_window)
    piece_rows, visit_order = chip_gather(white_by_window, "row", row_size)
    visit_count = sum(piece.shape[1] for piece in piece_rows)
    pair = pair_block(left_by_window, piece_rows, lag_table)
    pair = jnp.swapaxes(pair.reshape(visit_count, group_rows, LAGS), 0, 1)
    if visit_order is not None:
        pair = pair.reshape(group_rows, row_size, block_size, LAGS)
        pair = jnp.take(pair, visit_order, axis=1).reshape(group_rows, visit_count, LAGS)
    if left_order is not None:
        pair = pair.reshape(col_size, block_size, visit_count, LAGS)
        pair = jnp.take(pair, left_order, axis=0).reshape(group_rows, visit_count, LAGS)
    norm_scale = 1.0 / math.sqrt(white.shape[1] * bin_count)
    pair = pair * norm_scale
    lag_offset = jnp.abs(jnp.arange(LAGS, dtype=jnp.int32) - LH)
    keep_mask = lag_offset[None, :] <= lag_limit[:, None]
    tile_stack = jnp.where(keep_mask[:, None, :], pair, 0.0)
    return tile_stack[:, None]


def solution(mesh):
    placed = (P(("row", "col"), None, None), P(), P("row"))
    return jax.shard_map(
        on_device,
        mesh=mesh,
        in_specs=placed,
        out_specs=P("row", "col", None, None),
        check_vma=False,
    )
```

```python
import functools
import math

import jax
import jax.numpy as jnp
from jax import lax
from jax.experimental import pallas as pl
from jax.experimental.pallas import tpu as pltpu
from jax.sharding import PartitionSpec as P

DECIM = 2
LAGS = 128
BAND = 64
LH = 64


def angle_table(row_count, col_count, period, offset):
    row_ids = jnp.arange(row_count, dtype=jnp.int32)[:, None] + offset
    col_ids = jnp.arange(col_count, dtype=jnp.int32)[None, :]
    phase_int = jnp.mod(row_ids * col_ids, period)
    angles = phase_int.astype(jnp.float32) * (2.0 * math.pi / period)
    return (jnp.cos(angles), jnp.sin(angles))


def decimate(records, fir_taps):
    tap_count = fir_taps.shape[0]
    out_block = 128
    in_block = DECIM * out_block
    lead_dims = records.shape[:2]
    block_count = records.shape[2] // in_block
    blocks = records.reshape(lead_dims + (block_count, in_block))
    tails = blocks[:, :, :-1, in_block - tap_count :]
    tails = jnp.concatenate([jnp.zeros(lead_dims + (1, tap_count), records.dtype), tails], axis=2)
    windows = jnp.concatenate([tails, blocks], axis=3)
    tap_ids = jnp.arange(tap_count, dtype=jnp.int32)[:, None, None]
    in_ids = jnp.arange(in_block + tap_count, dtype=jnp.int32)[None, :, None]
    out_ids = jnp.arange(out_block, dtype=jnp.int32)[None, None, :]
    onehot = (in_ids == DECIM * out_ids + tap_count - tap_ids).astype(jnp.float32)
    band_matrix = jnp.einsum("k,kij->ij", fir_taps, onehot, precision=lax.Precision.HIGH)
    summed = jnp.einsum("swbi,ij->swbj", windows, band_matrix, precision=lax.Precision.HIGH)
    return summed.reshape(lead_dims + (block_count * out_block,))


def spectrum(decimated):
    out_length = decimated.shape[-1]
    first_len = 64
    second_len = out_length // first_len
    lead_dims = decimated.shape[:-1]
    blocks = decimated.reshape(lead_dims + (first_len, second_len))
    cos_one, sin_one = angle_table(first_len, first_len, first_len, 0)
    real_z = jnp.einsum("bwnq,fn->bwfq", blocks, cos_one, precision=lax.Precision.HIGH)
    imag_z = -jnp.einsum("bwnq,fn->bwfq", blocks, sin_one, precision=lax.Precision.HIGH)
    cos_two, sin_two = angle_table(first_len, second_len, out_length, 0)
    real_t = real_z * cos_two + imag_z * sin_two
    imag_t = imag_z * cos_two - real_z * sin_two
    cos_three, sin_three = angle_table(second_len // 2, second_len, second_len, 0)
    real_x = jnp.einsum(
        "bwfq,gq->bwgf", real_t, cos_three, precision=lax.Precision.HIGH
    ) + jnp.einsum("bwfq,gq->bwgf", imag_t, sin_three, precision=lax.Precision.HIGH)
    imag_x = jnp.einsum(
        "bwfq,gq->bwgf", imag_t, cos_three, precision=lax.Precision.HIGH
    ) - jnp.einsum("bwfq,gq->bwgf", real_t, sin_three, precision=lax.Precision.HIGH)
    bin_count = out_length // 2
    return (real_x.reshape(lead_dims + (bin_count,)), imag_x.reshape(lead_dims + (bin_count,)))


def whiten(spec_real, spec_imag):
    lead_dims = spec_real.shape[:-1]
    bin_count = spec_real.shape[-1]
    banded = lead_dims + (bin_count // BAND, BAND)
    squares = (spec_real * spec_real + spec_imag * spec_imag).reshape(banded)
    band_power = jnp.mean(squares, axis=-1, keepdims=True)
    inverse = 1.0 / jnp.sqrt(band_power + 1e-06)
    white_real = (spec_real.reshape(banded) * inverse).reshape(spec_real.shape)
    white_imag = (spec_imag.reshape(banded) * inverse).reshape(spec_imag.shape)
    return jnp.concatenate([white_real, white_imag], axis=-1).astype(jnp.bfloat16)


def cross_kernel(slots, *refs):
    piece_refs = refs[:len(slots)]
    table_ref, out_ref, left_f32, visit_f32, cross_ref = refs[len(slots):]
    left_refs = [ref for ref, slot in zip(piece_refs, slots) if slot[0] == 0]
    window_count, piece, width = left_refs[0].shape
    rows_left = left_f32.shape[1]
    bin_count = width // 2
    chunk = 512
    while chunk > 128 and chunk * rows_left > 8192:
        chunk //= 2
    chunks = bin_count // chunk
    group_rows = cross_ref.shape[0]
    group = group_rows // (piece * rows_left)
    visit_count = visit_f32.shape[1] // piece

    for ref, (kind, index) in zip(piece_refs, slots):
        target = left_f32 if kind == 0 else visit_f32
        target[:, index * piece:(index + 1) * piece, :] = ref[...].astype(jnp.float32)

    for first in range(0, visit_count, group):
        base = first * piece

        def one_chunk(step, carry):
            local = step // chunks
            partner = base + local
            off = pl.multiple_of((step % chunks) * chunk, chunk)
            acc_re = jnp.zeros((rows_left, chunk), jnp.float32)
            acc_im = jnp.zeros((rows_left, chunk), jnp.float32)
            for window in range(window_count):
                left_c = left_f32[window, :, pl.ds(off, chunk)]
                left_d = left_f32[window, :, pl.ds(off + bin_count, chunk)]
                vis_c = visit_f32[window, pl.ds(partner, 1), pl.ds(off, chunk)]
                vis_d = visit_f32[window, pl.ds(partner, 1), pl.ds(off + bin_count, chunk)]
                acc_re = acc_re + (left_c * vis_c + left_d * vis_d)
                acc_im = acc_im + (left_c * vis_d - left_d * vis_c)
            row = pl.multiple_of(local * rows_left, rows_left)
            cross_ref[pl.ds(row, rows_left), pl.ds(off, chunk)] = acc_re.astype(jnp.bfloat16)
            cross_ref[pl.ds(row, rows_left), pl.ds(off + bin_count, chunk)] = acc_im.astype(jnp.bfloat16)
            return carry

        lax.fori_loop(0, group * piece * chunks, one_chunk, 0)
        out_ref[base * rows_left:base * rows_left + group_rows, :] = jnp.dot(
            cross_ref[...], table_ref[...], preferred_element_type=jnp.float32
        )


def pair_block(left_pieces, visit_pieces, lag_table, issue_order):
    window_count, piece, width = left_pieces[0].shape
    left_count = len(left_pieces)
    visit_count = len(visit_pieces)
    rows_left = left_count * piece
    visit_rows = visit_count * piece
    lag_count = lag_table.shape[1]
    group = max(1, min(visit_count, 256 // (piece * rows_left)))
    while visit_count % group:
        group -= 1
    flops = visit_rows * rows_left * width * (4 * window_count + 2 * lag_count)
    vmem = pltpu.VMEM
    return pl.pallas_call(
        functools.partial(cross_kernel, tuple(issue_order)),
        out_shape=jax.ShapeDtypeStruct((visit_rows * rows_left, lag_count), jnp.float32),
        in_specs=[pl.BlockSpec(memory_space=vmem)] * (left_count + visit_count + 1),
        out_specs=pl.BlockSpec(memory_space=vmem),
        scratch_shapes=[
            vmem((window_count, rows_left, width), jnp.float32),
            vmem((window_count, visit_rows, width), jnp.float32),
            vmem((group * piece * rows_left, width), jnp.bfloat16),
        ],
        compiler_params=pltpu.CompilerParams(vmem_limit_bytes=60 * 1024 * 1024),
        cost_estimate=pl.CostEstimate(
            flops=flops,
            transcendentals=0,
            bytes_accessed=2 * width * (window_count * (rows_left + visit_rows) + lag_count)
            + 4 * visit_rows * rows_left * lag_count,
        ),
    )(*[(left_pieces, visit_pieces)[kind][index] for kind, index in issue_order], lag_table)


def xor_gather(block, axis_name, size):
    if size & (size - 1):
        return [lax.all_gather(block, axis_name, axis=1, tiled=True)], None
    pieces = [block]
    for step in range(1, size):
        pairs = [(source, source ^ step) for source in range(size)]
        pieces.append(lax.ppermute(block, axis_name, pairs))
    order = lax.axis_index(axis_name) ^ jnp.arange(size, dtype=jnp.int32)
    return pieces, order


def chip_gather(block, axis_name, size):
    if size < 4 or size & (size - 1):
        return xor_gather(block, axis_name, size)
    chips = size // 2
    fetched = []
    for step in range(1, chips):
        pairs = [(source, source ^ (2 * step)) for source in range(size)]
        fetched.append(lax.ppermute(block, axis_name, pairs))
    partner = [(source, source ^ 1) for source in range(size)]
    pieces = [block, lax.ppermute(block, axis_name, partner)]
    piece = block.shape[1]
    swapped = lax.ppermute(jnp.concatenate(fetched, axis=1), axis_name, partner)
    for step in range(1, chips):
        pieces.append(fetched[step - 1])
        pieces.append(swapped[:, (step - 1) * piece:step * piece, :])
    order = lax.axis_index(axis_name) ^ jnp.arange(size, dtype=jnp.int32)
    return pieces, order


def on_device(records, fir_taps, lag_limit):
    block_size = records.shape[0]
    decimated = decimate(records, fir_taps)
    out_length = decimated.shape[-1]
    bin_count = out_length // 2
    spec_real, spec_imag = spectrum(decimated)
    white = whiten(spec_real, spec_imag)
    white_by_window = jnp.moveaxis(white, 1, 0)
    col_size = lax.axis_size("col")
    row_size = lax.axis_size("row")
    left_by_window, left_order = xor_gather(white_by_window, "col", col_size)
    cos_lag, sin_lag = angle_table(LAGS, bin_count, out_length, -LH)
    lag_table = jnp.concatenate([cos_lag.T, sin_lag.T], axis=0).astype(jnp.bfloat16)
    group_rows = sum(piece.shape[1] for piece in left_by_window)
    piece_rows, visit_order = chip_gather(white_by_window, "row", row_size)
    visit_count = sum(piece.shape[1] for piece in piece_rows)
    late_first = [(1, index) for index in range(len(piece_rows)) if index > 1 and index % 2 == 1]
    near = [(0, 0), (1, 0), (0, 1), (1, 1)][:2 + min(1, len(left_by_window) - 1) + min(1, len(piece_rows) - 1)]
    fetches = [(1, index) for index in range(len(piece_rows)) if index > 1 and index % 2 == 0]
    far = [(0, index) for index in range(2, len(left_by_window))]
    issue_order = [slot for slot in late_first + near + fetches + far[::-1]]
    issue_order = sorted(set(issue_order), key=issue_order.index)
    assert len(issue_order) == len(left_by_window) + len(piece_rows)
    pair = pair_block(left_by_window, piece_rows, lag_table, issue_order)
    pair = jnp.swapaxes(pair.reshape(visit_count, group_rows, LAGS), 0, 1)
    if visit_order is not None:
        pair = pair.reshape(group_rows, row_size, block_size, LAGS)
        pair = jnp.take(pair, visit_order, axis=1).reshape(group_rows, visit_count, LAGS)
    if left_order is not None:
        pair = pair.reshape(col_size, block_size, visit_count, LAGS)
        pair = jnp.take(pair, left_order, axis=0).reshape(group_rows, visit_count, LAGS)
    norm_scale = 1.0 / math.sqrt(white.shape[1] * bin_count)
    pair = pair * norm_scale
    lag_offset = jnp.abs(jnp.arange(LAGS, dtype=jnp.int32) - LH)
    keep_mask = lag_offset[None, :] <= lag_limit[:, None]
    tile_stack = jnp.where(keep_mask[:, None, :], pair, 0.0)
    return tile_stack[:, None]


def solution(mesh):
    placed = (P(("row", "col"), None, None), P(), P("row"))
    return jax.shard_map(
        on_device,
        mesh=mesh,
        in_specs=placed,
        out_specs=P("row", "col", None, None),
        check_vma=False,
    )
```

```python
import functools
import math

import jax
import jax.numpy as jnp
from jax import lax
from jax.experimental import pallas as pl
from jax.experimental.pallas import tpu as pltpu
from jax.sharding import PartitionSpec as P

DECIM = 2
LAGS = 128
BAND = 64
LH = 64


def angle_table(row_count, col_count, period, offset):
    row_ids = jnp.arange(row_count, dtype=jnp.int32)[:, None] + offset
    col_ids = jnp.arange(col_count, dtype=jnp.int32)[None, :]
    phase_int = jnp.mod(row_ids * col_ids, period)
    angles = phase_int.astype(jnp.float32) * (2.0 * math.pi / period)
    return (jnp.cos(angles), jnp.sin(angles))


def decimate(records, fir_taps):
    tap_count = fir_taps.shape[0]
    out_block = 128
    in_block = DECIM * out_block
    lead_dims = records.shape[:2]
    block_count = records.shape[2] // in_block
    blocks = records.reshape(lead_dims + (block_count, in_block))
    tails = blocks[:, :, :-1, in_block - tap_count :]
    tails = jnp.concatenate([jnp.zeros(lead_dims + (1, tap_count), records.dtype), tails], axis=2)
    windows = jnp.concatenate([tails, blocks], axis=3)
    tap_ids = jnp.arange(tap_count, dtype=jnp.int32)[:, None, None]
    in_ids = jnp.arange(in_block + tap_count, dtype=jnp.int32)[None, :, None]
    out_ids = jnp.arange(out_block, dtype=jnp.int32)[None, None, :]
    onehot = (in_ids == DECIM * out_ids + tap_count - tap_ids).astype(jnp.float32)
    band_matrix = jnp.einsum("k,kij->ij", fir_taps, onehot, precision=lax.Precision.HIGH)
    summed = jnp.einsum("swbi,ij->swbj", windows, band_matrix, precision=lax.Precision.HIGH)
    return summed.reshape(lead_dims + (block_count * out_block,))


def spectrum(decimated):
    out_length = decimated.shape[-1]
    first_len = 64
    second_len = out_length // first_len
    lead_dims = decimated.shape[:-1]
    blocks = decimated.reshape(lead_dims + (first_len, second_len))
    cos_one, sin_one = angle_table(first_len, first_len, first_len, 0)
    real_z = jnp.einsum("bwnq,fn->bwfq", blocks, cos_one, precision=lax.Precision.HIGH)
    imag_z = -jnp.einsum("bwnq,fn->bwfq", blocks, sin_one, precision=lax.Precision.HIGH)
    cos_two, sin_two = angle_table(first_len, second_len, out_length, 0)
    real_t = real_z * cos_two + imag_z * sin_two
    imag_t = imag_z * cos_two - real_z * sin_two
    cos_three, sin_three = angle_table(second_len // 2, second_len, second_len, 0)
    real_x = jnp.einsum(
        "bwfq,gq->bwgf", real_t, cos_three, precision=lax.Precision.HIGH
    ) + jnp.einsum("bwfq,gq->bwgf", imag_t, sin_three, precision=lax.Precision.HIGH)
    imag_x = jnp.einsum(
        "bwfq,gq->bwgf", imag_t, cos_three, precision=lax.Precision.HIGH
    ) - jnp.einsum("bwfq,gq->bwgf", real_t, sin_three, precision=lax.Precision.HIGH)
    bin_count = out_length // 2
    return (real_x.reshape(lead_dims + (bin_count,)), imag_x.reshape(lead_dims + (bin_count,)))


def whiten(spec_real, spec_imag):
    lead_dims = spec_real.shape[:-1]
    bin_count = spec_real.shape[-1]
    banded = lead_dims + (bin_count // BAND, BAND)
    squares = (spec_real * spec_real + spec_imag * spec_imag).reshape(banded)
    band_power = jnp.mean(squares, axis=-1, keepdims=True)
    inverse = 1.0 / jnp.sqrt(band_power + 1e-06)
    white_real = (spec_real.reshape(banded) * inverse).reshape(spec_real.shape)
    white_imag = (spec_imag.reshape(banded) * inverse).reshape(spec_imag.shape)
    return jnp.concatenate([white_real, white_imag], axis=-1).astype(jnp.bfloat16)


def cross_kernel(slots, *refs):
    piece_refs = refs[:len(slots)]
    table_ref, out_ref, left_f32, visit_f32, cross_ref = refs[len(slots):]
    left_refs = [ref for ref, slot in zip(piece_refs, slots) if slot[0] == 0]
    window_count, piece, width = left_refs[0].shape
    rows_left = left_f32.shape[1]
    bin_count = width // 2
    chunk = 512
    while chunk > 128 and chunk * rows_left > 8192:
        chunk //= 2
    chunks = bin_count // chunk
    group_rows = cross_ref.shape[0]
    group = group_rows // (piece * rows_left)
    visit_count = visit_f32.shape[1] // piece

    for ref, (kind, index) in zip(piece_refs, slots):
        target = left_f32 if kind == 0 else visit_f32
        target[:, index * piece:(index + 1) * piece, :] = ref[...].astype(jnp.float32)

    for first in range(0, visit_count, group):
        base = first * piece

        def one_chunk(step, carry):
            local = step // chunks
            partner = base + local
            off = pl.multiple_of((step % chunks) * chunk, chunk)
            acc_re = jnp.zeros((rows_left, chunk), jnp.float32)
            acc_im = jnp.zeros((rows_left, chunk), jnp.float32)
            for window in range(window_count):
                left_c = left_f32[window, :, pl.ds(off, chunk)]
                left_d = left_f32[window, :, pl.ds(off + bin_count, chunk)]
                vis_c = visit_f32[window, pl.ds(partner, 1), pl.ds(off, chunk)]
                vis_d = visit_f32[window, pl.ds(partner, 1), pl.ds(off + bin_count, chunk)]
                acc_re = acc_re + (left_c * vis_c + left_d * vis_d)
                acc_im = acc_im + (left_c * vis_d - left_d * vis_c)
            row = pl.multiple_of(local * rows_left, rows_left)
            cross_ref[pl.ds(row, rows_left), pl.ds(off, chunk)] = acc_re.astype(jnp.bfloat16)
            cross_ref[pl.ds(row, rows_left), pl.ds(off + bin_count, chunk)] = acc_im.astype(jnp.bfloat16)
            return carry

        lax.fori_loop(0, group * piece * chunks, one_chunk, 0)
        out_ref[base * rows_left:base * rows_left + group_rows, :] = jnp.dot(
            cross_ref[...], table_ref[...], preferred_element_type=jnp.float32
        )


def pair_block(left_pieces, visit_pieces, lag_table, issue_order):
    window_count, piece, width = left_pieces[0].shape
    left_count = len(left_pieces)
    visit_count = len(visit_pieces)
    rows_left = left_count * piece
    visit_rows = visit_count * piece
    lag_count = lag_table.shape[1]
    group = max(1, min(visit_count, 256 // (piece * rows_left)))
    while visit_count % group:
        group -= 1
    flops = visit_rows * rows_left * width * (4 * window_count + 2 * lag_count)
    vmem = pltpu.VMEM
    return pl.pallas_call(
        functools.partial(cross_kernel, tuple(issue_order)),
        out_shape=jax.ShapeDtypeStruct((visit_rows * rows_left, lag_count), jnp.float32),
        in_specs=[pl.BlockSpec(memory_space=vmem)] * (left_count + visit_count + 1),
        out_specs=pl.BlockSpec(memory_space=vmem),
        scratch_shapes=[
            vmem((window_count, rows_left, width), jnp.float32),
            vmem((window_count, visit_rows, width), jnp.float32),
            vmem((group * piece * rows_left, width), jnp.bfloat16),
        ],
        compiler_params=pltpu.CompilerParams(vmem_limit_bytes=60 * 1024 * 1024),
        cost_estimate=pl.CostEstimate(
            flops=flops,
            transcendentals=0,
            bytes_accessed=2 * width * (window_count * (rows_left + visit_rows) + lag_count)
            + 4 * visit_rows * rows_left * lag_count,
        ),
    )(*[(left_pieces, visit_pieces)[kind][index] for kind, index in issue_order], lag_table)


def xor_gather(block, axis_name, size):
    if size & (size - 1):
        return [lax.all_gather(block, axis_name, axis=1, tiled=True)], None
    pieces = [block]
    for step in range(1, size):
        pairs = [(source, source ^ step) for source in range(size)]
        pieces.append(lax.ppermute(block, axis_name, pairs))
    order = lax.axis_index(axis_name) ^ jnp.arange(size, dtype=jnp.int32)
    return pieces, order


def chip_gather(block, axis_name, size):
    if size < 4 or size & (size - 1):
        return xor_gather(block, axis_name, size)
    chips = size // 2
    fetched = []
    for step in range(1, chips):
        pairs = [(source, source ^ (2 * step)) for source in range(size)]
        fetched.append(lax.ppermute(block, axis_name, pairs))
    partner = [(source, source ^ 1) for source in range(size)]
    pieces = [block, lax.ppermute(block, axis_name, partner)]
    piece = block.shape[1]
    swapped = lax.ppermute(jnp.concatenate(fetched, axis=1), axis_name, partner)
    for step in range(1, chips):
        pieces.append(fetched[step - 1])
        pieces.append(swapped[:, (step - 1) * piece:step * piece, :])
    order = lax.axis_index(axis_name) ^ jnp.arange(size, dtype=jnp.int32)
    return pieces, order


def on_device(records, fir_taps, lag_limit):
    block_size = records.shape[0]
    decimated = decimate(records, fir_taps)
    out_length = decimated.shape[-1]
    bin_count = out_length // 2
    spec_real, spec_imag = spectrum(decimated)
    white = whiten(spec_real, spec_imag)
    white_by_window = jnp.moveaxis(white, 1, 0)
    col_size = lax.axis_size("col")
    row_size = lax.axis_size("row")
    left_by_window, left_order = xor_gather(white_by_window, "col", col_size)
    cos_lag, sin_lag = angle_table(LAGS, bin_count, out_length, -LH)
    lag_table = jnp.concatenate([cos_lag.T, sin_lag.T], axis=0).astype(jnp.bfloat16)
    group_rows = sum(piece.shape[1] for piece in left_by_window)
    piece_rows, visit_order = chip_gather(white_by_window, "row", row_size)
    visit_count = sum(piece.shape[1] for piece in piece_rows)
    late_first = [(1, index) for index in range(len(piece_rows)) if index > 1 and index % 2 == 1]
    near = [(0, 0), (1, 0), (0, 1), (1, 1)][:2 + min(1, len(left_by_window) - 1) + min(1, len(piece_rows) - 1)]
    fetches = [(1, index) for index in range(len(piece_rows)) if index > 1 and index % 2 == 0]
    far = [(0, index) for index in range(2, len(left_by_window))]
    issue_order = [slot for slot in late_first + near + fetches + far[::-1]]
    issue_order = sorted(set(issue_order), key=issue_order.index)
    assert len(issue_order) == len(left_by_window) + len(piece_rows)
    pair = pair_block(left_by_window, piece_rows, lag_table, issue_order)
    piece = block_size
    left_pos = jnp.arange(group_rows, dtype=jnp.int32)
    visit_pos = jnp.arange(visit_count, dtype=jnp.int32)
    if left_order is not None:
        left_pos = left_order[left_pos // piece] * piece + left_pos % piece
    if visit_order is not None:
        visit_pos = visit_order[visit_pos // piece] * piece + visit_pos % piece
    source_row = visit_pos[None, :] * group_rows + left_pos[:, None]
    pair = jnp.take(pair, source_row.reshape(-1), axis=0).reshape(group_rows, visit_count, LAGS)
    norm_scale = 1.0 / math.sqrt(white.shape[1] * bin_count)
    pair = pair * norm_scale
    lag_offset = jnp.abs(jnp.arange(LAGS, dtype=jnp.int32) - LH)
    keep_mask = lag_offset[None, :] <= lag_limit[:, None]
    tile_stack = jnp.where(keep_mask[:, None, :], pair, 0.0)
    return tile_stack[:, None]


def solution(mesh):
    placed = (P(("row", "col"), None, None), P(), P("row"))
    return jax.shard_map(
        on_device,
        mesh=mesh,
        in_specs=placed,
        out_specs=P("row", "col", None, None),
        check_vma=False,
    )
```

```python
import functools
import math

import jax
import jax.numpy as jnp
from jax import lax
from jax.experimental import pallas as pl
from jax.experimental.pallas import tpu as pltpu
from jax.sharding import PartitionSpec as P

DECIM = 2
LAGS = 128
BAND = 64
LH = 64


def angle_table(row_count, col_count, period, offset):
    row_ids = jnp.arange(row_count, dtype=jnp.int32)[:, None] + offset
    col_ids = jnp.arange(col_count, dtype=jnp.int32)[None, :]
    phase_int = jnp.mod(row_ids * col_ids, period)
    angles = phase_int.astype(jnp.float32) * (2.0 * math.pi / period)
    return (jnp.cos(angles), jnp.sin(angles))


def decimate(records, fir_taps):
    tap_count = fir_taps.shape[0]
    out_block = 128
    in_block = DECIM * out_block
    lead_dims = records.shape[:2]
    block_count = records.shape[2] // in_block
    blocks = records.reshape(lead_dims + (block_count, in_block))
    tails = blocks[:, :, :-1, in_block - tap_count :]
    tails = jnp.concatenate([jnp.zeros(lead_dims + (1, tap_count), records.dtype), tails], axis=2)
    windows = jnp.concatenate([tails, blocks], axis=3)
    tap_ids = jnp.arange(tap_count, dtype=jnp.int32)[:, None, None]
    in_ids = jnp.arange(in_block + tap_count, dtype=jnp.int32)[None, :, None]
    out_ids = jnp.arange(out_block, dtype=jnp.int32)[None, None, :]
    onehot = (in_ids == DECIM * out_ids + tap_count - tap_ids).astype(jnp.float32)
    band_matrix = jnp.einsum("k,kij->ij", fir_taps, onehot, precision=lax.Precision.HIGH)
    summed = jnp.einsum("swbi,ij->swbj", windows, band_matrix, precision=lax.Precision.HIGH)
    return summed.reshape(lead_dims + (block_count * out_block,))


def spectrum(decimated):
    out_length = decimated.shape[-1]
    first_len = 64
    second_len = out_length // first_len
    lead_dims = decimated.shape[:-1]
    blocks = decimated.reshape(lead_dims + (first_len, second_len))
    cos_one, sin_one = angle_table(first_len, first_len, first_len, 0)
    real_z = jnp.einsum("bwnq,fn->bwfq", blocks, cos_one, precision=lax.Precision.HIGH)
    imag_z = -jnp.einsum("bwnq,fn->bwfq", blocks, sin_one, precision=lax.Precision.HIGH)
    cos_two, sin_two = angle_table(first_len, second_len, out_length, 0)
    real_t = real_z * cos_two + imag_z * sin_two
    imag_t = imag_z * cos_two - real_z * sin_two
    cos_three, sin_three = angle_table(second_len // 2, second_len, second_len, 0)
    real_x = jnp.einsum(
        "bwfq,gq->bwgf", real_t, cos_three, precision=lax.Precision.HIGH
    ) + jnp.einsum("bwfq,gq->bwgf", imag_t, sin_three, precision=lax.Precision.HIGH)
    imag_x = jnp.einsum(
        "bwfq,gq->bwgf", imag_t, cos_three, precision=lax.Precision.HIGH
    ) - jnp.einsum("bwfq,gq->bwgf", real_t, sin_three, precision=lax.Precision.HIGH)
    bin_count = out_length // 2
    return (real_x.reshape(lead_dims + (bin_count,)), imag_x.reshape(lead_dims + (bin_count,)))


def whiten(spec_real, spec_imag):
    lead_dims = spec_real.shape[:-1]
    bin_count = spec_real.shape[-1]
    banded = lead_dims + (bin_count // BAND, BAND)
    squares = (spec_real * spec_real + spec_imag * spec_imag).reshape(banded)
    band_power = jnp.mean(squares, axis=-1, keepdims=True)
    inverse = 1.0 / jnp.sqrt(band_power + 1e-06)
    white_real = (spec_real.reshape(banded) * inverse).reshape(spec_real.shape)
    white_imag = (spec_imag.reshape(banded) * inverse).reshape(spec_imag.shape)
    return jnp.concatenate([white_real, white_imag], axis=-1).astype(jnp.bfloat16)


def cross_kernel(slots, *refs):
    piece_refs = refs[:len(slots)]
    left_perm, visit_perm, table_ref, out_ref, left_f32, visit_f32, cross_ref = refs[len(slots):]
    left_refs = [ref for ref, slot in zip(piece_refs, slots) if slot[0] == 0]
    window_count, piece, width = left_refs[0].shape
    rows_left = left_f32.shape[1]
    bin_count = width // 2
    chunk = 512
    while chunk > 128 and chunk * rows_left > 8192:
        chunk //= 2
    chunks = bin_count // chunk
    group_rows = cross_ref.shape[0]
    group = group_rows // (piece * rows_left)
    visit_count = visit_f32.shape[1] // piece

    for ref, (kind, index) in zip(piece_refs, slots):
        target = left_f32 if kind == 0 else visit_f32
        target[:, index * piece:(index + 1) * piece, :] = ref[...].astype(jnp.float32)
    for window in range(window_count):
        for perm_ref, target in ((left_perm, left_f32), (visit_perm, visit_f32)):
            target[window] = jnp.dot(
                perm_ref[...], target[window].astype(jnp.bfloat16), preferred_element_type=jnp.float32
            )

    for first in range(0, visit_count, group):
        base = first * piece

        def one_chunk(step, carry):
            local = step // chunks
            partner = base + local
            off = pl.multiple_of((step % chunks) * chunk, chunk)
            acc_re = jnp.zeros((rows_left, chunk), jnp.float32)
            acc_im = jnp.zeros((rows_left, chunk), jnp.float32)
            for window in range(window_count):
                left_c = left_f32[window, :, pl.ds(off, chunk)]
                left_d = left_f32[window, :, pl.ds(off + bin_count, chunk)]
                vis_c = visit_f32[window, pl.ds(partner, 1), pl.ds(off, chunk)]
                vis_d = visit_f32[window, pl.ds(partner, 1), pl.ds(off + bin_count, chunk)]
                acc_re = acc_re + (left_c * vis_c + left_d * vis_d)
                acc_im = acc_im + (left_c * vis_d - left_d * vis_c)
            row = pl.multiple_of(local * rows_left, rows_left)
            cross_ref[pl.ds(row, rows_left), pl.ds(off, chunk)] = acc_re.astype(jnp.bfloat16)
            cross_ref[pl.ds(row, rows_left), pl.ds(off + bin_count, chunk)] = acc_im.astype(jnp.bfloat16)
            return carry

        lax.fori_loop(0, group * piece * chunks, one_chunk, 0)
        out_ref[base * rows_left:base * rows_left + group_rows, :] = jnp.dot(
            cross_ref[...], table_ref[...], preferred_element_type=jnp.float32
        )


def pair_block(left_pieces, visit_pieces, left_perm, visit_perm, lag_table, issue_order):
    window_count, piece, width = left_pieces[0].shape
    left_count = len(left_pieces)
    visit_count = len(visit_pieces)
    rows_left = left_count * piece
    visit_rows = visit_count * piece
    lag_count = lag_table.shape[1]
    group = max(1, min(visit_count, 256 // (piece * rows_left)))
    while visit_count % group:
        group -= 1
    flops = visit_rows * rows_left * width * (4 * window_count + 2 * lag_count)
    vmem = pltpu.VMEM
    return pl.pallas_call(
        functools.partial(cross_kernel, tuple(issue_order)),
        out_shape=jax.ShapeDtypeStruct((visit_rows * rows_left, lag_count), jnp.float32),
        in_specs=[pl.BlockSpec(memory_space=vmem)] * (left_count + visit_count + 3),
        out_specs=pl.BlockSpec(memory_space=vmem),
        scratch_shapes=[
            vmem((window_count, rows_left, width), jnp.float32),
            vmem((window_count, visit_rows, width), jnp.float32),
            vmem((group * piece * rows_left, width), jnp.bfloat16),
        ],
        compiler_params=pltpu.CompilerParams(vmem_limit_bytes=60 * 1024 * 1024),
        cost_estimate=pl.CostEstimate(
            flops=flops,
            transcendentals=0,
            bytes_accessed=2 * width * (window_count * (rows_left + visit_rows) + lag_count)
            + 4 * visit_rows * rows_left * lag_count,
        ),
    )(*[(left_pieces, visit_pieces)[kind][index] for kind, index in issue_order], left_perm, visit_perm, lag_table)


def xor_gather(block, axis_name, size):
    if size & (size - 1):
        return [lax.all_gather(block, axis_name, axis=1, tiled=True)], None
    pieces = [block]
    for step in range(1, size):
        pairs = [(source, source ^ step) for source in range(size)]
        pieces.append(lax.ppermute(block, axis_name, pairs))
    order = lax.axis_index(axis_name) ^ jnp.arange(size, dtype=jnp.int32)
    return pieces, order


def chip_gather(block, axis_name, size):
    if size < 4 or size & (size - 1):
        return xor_gather(block, axis_name, size)
    chips = size // 2
    fetched = []
    for step in range(1, chips):
        pairs = [(source, source ^ (2 * step)) for source in range(size)]
        fetched.append(lax.ppermute(block, axis_name, pairs))
    partner = [(source, source ^ 1) for source in range(size)]
    pieces = [block, lax.ppermute(block, axis_name, partner)]
    piece = block.shape[1]
    swapped = lax.ppermute(jnp.concatenate(fetched, axis=1), axis_name, partner)
    for step in range(1, chips):
        pieces.append(fetched[step - 1])
        pieces.append(swapped[:, (step - 1) * piece:step * piece, :])
    order = lax.axis_index(axis_name) ^ jnp.arange(size, dtype=jnp.int32)
    return pieces, order


def on_device(records, fir_taps, lag_limit):
    block_size = records.shape[0]
    decimated = decimate(records, fir_taps)
    out_length = decimated.shape[-1]
    bin_count = out_length // 2
    spec_real, spec_imag = spectrum(decimated)
    white = whiten(spec_real, spec_imag)
    white_by_window = jnp.moveaxis(white, 1, 0)
    col_size = lax.axis_size("col")
    row_size = lax.axis_size("row")
    left_by_window, left_order = xor_gather(white_by_window, "col", col_size)
    cos_lag, sin_lag = angle_table(LAGS, bin_count, out_length, -LH)
    lag_table = jnp.concatenate([cos_lag.T, sin_lag.T], axis=0).astype(jnp.bfloat16)
    group_rows = sum(piece.shape[1] for piece in left_by_window)
    piece_rows, visit_order = chip_gather(white_by_window, "row", row_size)
    visit_count = sum(piece.shape[1] for piece in piece_rows)
    late_first = [(1, index) for index in range(len(piece_rows)) if index > 1 and index % 2 == 1]
    near = [(0, 0), (1, 0), (0, 1), (1, 1)][:2 + min(1, len(left_by_window) - 1) + min(1, len(piece_rows) - 1)]
    fetches = [(1, index) for index in range(len(piece_rows)) if index > 1 and index % 2 == 0]
    far = [(0, index) for index in range(2, len(left_by_window))]
    issue_order = [slot for slot in late_first + near + fetches + far[::-1]]
    issue_order = sorted(set(issue_order), key=issue_order.index)
    assert len(issue_order) == len(left_by_window) + len(piece_rows)
    piece = block_size
    left_pos = jnp.arange(group_rows, dtype=jnp.int32)
    visit_pos = jnp.arange(visit_count, dtype=jnp.int32)
    if left_order is not None:
        left_pos = left_order[left_pos // piece] * piece + left_pos % piece
    if visit_order is not None:
        visit_pos = visit_order[visit_pos // piece] * piece + visit_pos % piece
    left_perm = (jnp.arange(group_rows)[None, :] == left_pos[:, None]).astype(jnp.bfloat16)
    visit_perm = (jnp.arange(visit_count)[None, :] == visit_pos[:, None]).astype(jnp.bfloat16)
    pair = pair_block(left_by_window, piece_rows, left_perm, visit_perm, lag_table, issue_order)
    pair = jnp.swapaxes(pair.reshape(visit_count, group_rows, LAGS), 0, 1)
    norm_scale = 1.0 / math.sqrt(white.shape[1] * bin_count)
    pair = pair * norm_scale
    lag_offset = jnp.abs(jnp.arange(LAGS, dtype=jnp.int32) - LH)
    keep_mask = lag_offset[None, :] <= lag_limit[:, None]
    tile_stack = jnp.where(keep_mask[:, None, :], pair, 0.0)
    return tile_stack[:, None]


def solution(mesh):
    placed = (P(("row", "col"), None, None), P(), P("row"))
    return jax.shard_map(
        on_device,
        mesh=mesh,
        in_specs=placed,
        out_specs=P("row", "col", None, None),
        check_vma=False,
    )
```

```python
import functools
import math

import jax
import numpy as np
import jax.numpy as jnp
from jax import lax
from jax.experimental import pallas as pl
from jax.experimental.pallas import tpu as pltpu
from jax.sharding import PartitionSpec as P

DECIM = 2
LAGS = 128
BAND = 64
LH = 64


def angle_table(row_count, col_count, period, offset):
    row_ids = jnp.arange(row_count, dtype=jnp.int32)[:, None] + offset
    col_ids = jnp.arange(col_count, dtype=jnp.int32)[None, :]
    phase_int = jnp.mod(row_ids * col_ids, period)
    angles = phase_int.astype(jnp.float32) * (2.0 * math.pi / period)
    return (jnp.cos(angles), jnp.sin(angles))


def decimate(records, fir_taps):
    tap_count = fir_taps.shape[0]
    out_block = 128
    in_block = DECIM * out_block
    lead_dims = records.shape[:2]
    block_count = records.shape[2] // in_block
    blocks = records.reshape(lead_dims + (block_count, in_block))
    tails = blocks[:, :, :-1, in_block - tap_count :]
    tails = jnp.concatenate([jnp.zeros(lead_dims + (1, tap_count), records.dtype), tails], axis=2)
    windows = jnp.concatenate([tails, blocks], axis=3)
    in_ids = np.arange(in_block + tap_count)[:, None]
    out_ids = np.arange(out_block)[None, :]
    tap_index = DECIM * out_ids + tap_count - in_ids
    inside = (tap_index >= 0) & (tap_index < tap_count)
    padded_taps = jnp.concatenate([fir_taps, jnp.zeros((1,), fir_taps.dtype)])
    band_matrix = padded_taps[np.where(inside, tap_index, tap_count).astype(np.int32)]
    summed = jnp.einsum("swbi,ij->swbj", windows, band_matrix, precision=lax.Precision.HIGH)
    return summed.reshape(lead_dims + (block_count * out_block,))


def spectrum(decimated):
    out_length = decimated.shape[-1]
    first_len = 64
    second_len = out_length // first_len
    lead_dims = decimated.shape[:-1]
    blocks = decimated.reshape(lead_dims + (first_len, second_len))
    cos_one, sin_one = angle_table(first_len, first_len, first_len, 0)
    real_z = jnp.einsum("bwnq,fn->bwfq", blocks, cos_one, precision=lax.Precision.HIGH)
    imag_z = -jnp.einsum("bwnq,fn->bwfq", blocks, sin_one, precision=lax.Precision.HIGH)
    cos_two, sin_two = angle_table(first_len, second_len, out_length, 0)
    real_t = real_z * cos_two + imag_z * sin_two
    imag_t = imag_z * cos_two - real_z * sin_two
    cos_three, sin_three = angle_table(second_len // 2, second_len, second_len, 0)
    real_x = jnp.einsum(
        "bwfq,gq->bwgf", real_t, cos_three, precision=lax.Precision.HIGH
    ) + jnp.einsum("bwfq,gq->bwgf", imag_t, sin_three, precision=lax.Precision.HIGH)
    imag_x = jnp.einsum(
        "bwfq,gq->bwgf", imag_t, cos_three, precision=lax.Precision.HIGH
    ) - jnp.einsum("bwfq,gq->bwgf", real_t, sin_three, precision=lax.Precision.HIGH)
    bin_count = out_length // 2
    return (real_x.reshape(lead_dims + (bin_count,)), imag_x.reshape(lead_dims + (bin_count,)))


def whiten(spec_real, spec_imag):
    lead_dims = spec_real.shape[:-1]
    bin_count = spec_real.shape[-1]
    banded = lead_dims + (bin_count // BAND, BAND)
    squares = (spec_real * spec_real + spec_imag * spec_imag).reshape(banded)
    band_power = jnp.mean(squares, axis=-1, keepdims=True)
    inverse = 1.0 / jnp.sqrt(band_power + 1e-06)
    white_real = (spec_real.reshape(banded) * inverse).reshape(spec_real.shape)
    white_imag = (spec_imag.reshape(banded) * inverse).reshape(spec_imag.shape)
    return jnp.concatenate([white_real, white_imag], axis=-1).astype(jnp.bfloat16)


def cross_kernel(slots, *refs):
    piece_refs = refs[:len(slots)]
    left_perm, visit_perm, limit_ref, table_ref, out_ref, left_f32, visit_f32, cross_ref = refs[len(slots):]
    left_refs = [ref for ref, slot in zip(piece_refs, slots) if slot[0] == 0]
    window_count, piece, width = left_refs[0].shape
    rows_left = left_f32.shape[1]
    bin_count = width // 2
    chunk = 512
    while chunk > 128 and chunk * rows_left > 8192:
        chunk //= 2
    chunks = bin_count // chunk
    group_rows = cross_ref.shape[0]
    group = group_rows // (piece * rows_left)
    visit_count = visit_f32.shape[1] // piece
    scale = 1.0 / math.sqrt(window_count * bin_count)

    for ref, (kind, index) in zip(piece_refs, slots):
        target = left_f32 if kind == 0 else visit_f32
        target[:, index * piece:(index + 1) * piece, :] = ref[...].astype(jnp.float32)
    for window in range(window_count):
        for perm_ref, target in ((left_perm, left_f32), (visit_perm, visit_f32)):
            target[window] = jnp.dot(
                perm_ref[...], target[window].astype(jnp.bfloat16), preferred_element_type=jnp.float32
            )

    for first in range(0, visit_count, group):
        base = first * piece

        def one_chunk(step, carry):
            local = step // chunks
            partner = base + local
            off = pl.multiple_of((step % chunks) * chunk, chunk)
            acc_re = jnp.zeros((rows_left, chunk), jnp.float32)
            acc_im = jnp.zeros((rows_left, chunk), jnp.float32)
            for window in range(window_count):
                left_c = left_f32[window, :, pl.ds(off, chunk)]
                left_d = left_f32[window, :, pl.ds(off + bin_count, chunk)]
                vis_c = visit_f32[window, pl.ds(partner, 1), pl.ds(off, chunk)]
                vis_d = visit_f32[window, pl.ds(partner, 1), pl.ds(off + bin_count, chunk)]
                acc_re = acc_re + (left_c * vis_c + left_d * vis_d)
                acc_im = acc_im + (left_c * vis_d - left_d * vis_c)
            row = pl.multiple_of(local * rows_left, rows_left)
            cross_ref[pl.ds(row, rows_left), pl.ds(off, chunk)] = acc_re.astype(jnp.bfloat16)
            cross_ref[pl.ds(row, rows_left), pl.ds(off + bin_count, chunk)] = acc_im.astype(jnp.bfloat16)
            return carry

        lax.fori_loop(0, group * piece * chunks, one_chunk, 0)
        rows = pl.ds(base * rows_left, group_rows)
        block = jnp.dot(cross_ref[...], table_ref[...], preferred_element_type=jnp.float32) * scale
        lag = lax.broadcasted_iota(jnp.int32, block.shape, 1)
        keep = jnp.abs(lag - block.shape[1] // 2) <= limit_ref[rows, :]
        out_ref[rows, :] = jnp.where(keep, block, 0.0)


def pair_block(left_pieces, visit_pieces, left_perm, visit_perm, limit, lag_table, issue_order):
    window_count, piece, width = left_pieces[0].shape
    left_count = len(left_pieces)
    visit_count = len(visit_pieces)
    rows_left = left_count * piece
    visit_rows = visit_count * piece
    lag_count = lag_table.shape[1]
    group = max(1, min(visit_count, 256 // (piece * rows_left)))
    while visit_count % group:
        group -= 1
    flops = visit_rows * rows_left * width * (4 * window_count + 2 * lag_count)
    vmem = pltpu.VMEM
    return pl.pallas_call(
        functools.partial(cross_kernel, tuple(issue_order)),
        out_shape=jax.ShapeDtypeStruct((visit_rows * rows_left, lag_count), jnp.float32),
        in_specs=[pl.BlockSpec(memory_space=vmem)] * (left_count + visit_count + 4),
        out_specs=pl.BlockSpec(memory_space=vmem),
        scratch_shapes=[
            vmem((window_count, rows_left, width), jnp.float32),
            vmem((window_count, visit_rows, width), jnp.float32),
            vmem((group * piece * rows_left, width), jnp.bfloat16),
        ],
        compiler_params=pltpu.CompilerParams(vmem_limit_bytes=60 * 1024 * 1024),
        cost_estimate=pl.CostEstimate(
            flops=flops,
            transcendentals=0,
            bytes_accessed=2 * width * (window_count * (rows_left + visit_rows) + lag_count)
            + 4 * visit_rows * rows_left * lag_count,
        ),
    )(*[(left_pieces, visit_pieces)[kind][index] for kind, index in issue_order], left_perm, visit_perm, limit, lag_table)


def xor_gather(block, axis_name, size):
    if size & (size - 1):
        return [lax.all_gather(block, axis_name, axis=1, tiled=True)], None
    pieces = [block]
    for step in range(1, size):
        pairs = [(source, source ^ step) for source in range(size)]
        pieces.append(lax.ppermute(block, axis_name, pairs))
    order = lax.axis_index(axis_name) ^ jnp.arange(size, dtype=jnp.int32)
    return pieces, order


def chip_gather(block, axis_name, size):
    if size < 4 or size & (size - 1):
        return xor_gather(block, axis_name, size)
    chips = size // 2
    fetched = []
    for step in range(1, chips):
        pairs = [(source, source ^ (2 * step)) for source in range(size)]
        fetched.append(lax.ppermute(block, axis_name, pairs))
    partner = [(source, source ^ 1) for source in range(size)]
    pieces = [block, lax.ppermute(block, axis_name, partner)]
    piece = block.shape[1]
    swapped = lax.ppermute(jnp.concatenate(fetched, axis=1), axis_name, partner)
    for step in range(1, chips):
        pieces.append(fetched[step - 1])
        pieces.append(swapped[:, (step - 1) * piece:step * piece, :])
    order = lax.axis_index(axis_name) ^ jnp.arange(size, dtype=jnp.int32)
    return pieces, order


def on_device(records, fir_taps, lag_limit):
    block_size = records.shape[0]
    decimated = decimate(records, fir_taps)
    out_length = decimated.shape[-1]
    bin_count = out_length // 2
    spec_real, spec_imag = spectrum(decimated)
    white = whiten(spec_real, spec_imag)
    white_by_window = jnp.moveaxis(white, 1, 0)
    col_size = lax.axis_size("col")
    row_size = lax.axis_size("row")
    left_by_window, left_order = xor_gather(white_by_window, "col", col_size)
    cos_lag, sin_lag = angle_table(LAGS, bin_count, out_length, -LH)
    lag_table = jnp.concatenate([cos_lag.T, sin_lag.T], axis=0).astype(jnp.bfloat16)
    group_rows = sum(piece.shape[1] for piece in left_by_window)
    piece_rows, visit_order = chip_gather(white_by_window, "row", row_size)
    visit_count = sum(piece.shape[1] for piece in piece_rows)
    late_first = [(1, index) for index in range(len(piece_rows)) if index > 1 and index % 2 == 1]
    near = [(0, 0), (1, 0), (0, 1), (1, 1)][:2 + min(1, len(left_by_window) - 1) + min(1, len(piece_rows) - 1)]
    fetches = [(1, index) for index in range(len(piece_rows)) if index > 1 and index % 2 == 0]
    far = [(0, index) for index in range(2, len(left_by_window))]
    issue_order = [slot for slot in late_first + near + fetches + far[::-1]]
    issue_order = sorted(set(issue_order), key=issue_order.index)
    assert len(issue_order) == len(left_by_window) + len(piece_rows)
    piece = block_size
    left_pos = jnp.arange(group_rows, dtype=jnp.int32)
    visit_pos = jnp.arange(visit_count, dtype=jnp.int32)
    if left_order is not None:
        left_pos = left_order[left_pos // piece] * piece + left_pos % piece
    if visit_order is not None:
        visit_pos = visit_order[visit_pos // piece] * piece + visit_pos % piece
    left_perm = (jnp.arange(group_rows)[None, :] == left_pos[:, None]).astype(jnp.bfloat16)
    visit_perm = (jnp.arange(visit_count)[None, :] == visit_pos[:, None]).astype(jnp.bfloat16)
    limit = jnp.tile(lag_limit, visit_count)[:, None]
    pair = pair_block(left_by_window, piece_rows, left_perm, visit_perm, limit, lag_table, issue_order)
    pair = jnp.swapaxes(pair.reshape(visit_count, group_rows, LAGS), 0, 1)
    return pair[:, None]


def solution(mesh):
    placed = (P(("row", "col"), None, None), P(), P("row"))
    return jax.shard_map(
        on_device,
        mesh=mesh,
        in_specs=placed,
        out_specs=P("row", "col", None, None),
        check_vma=False,
    )
```

```python
import functools
import math

import jax
import jax.numpy as jnp
from jax import lax
from jax.experimental import pallas as pl
from jax.experimental.pallas import tpu as pltpu
from jax.sharding import PartitionSpec as P

DECIM = 2
LAGS = 128
BAND = 64
LH = 64


def angle_table(row_count, col_count, period, offset):
    row_ids = jnp.arange(row_count, dtype=jnp.int32)[:, None] + offset
    col_ids = jnp.arange(col_count, dtype=jnp.int32)[None, :]
    phase_int = jnp.mod(row_ids * col_ids, period)
    angles = phase_int.astype(jnp.float32) * (2.0 * math.pi / period)
    return (jnp.cos(angles), jnp.sin(angles))


def decimate(records, fir_taps):
    tap_count = fir_taps.shape[0]
    out_block = 128
    in_block = DECIM * out_block
    lead_dims = records.shape[:2]
    block_count = records.shape[2] // in_block
    blocks = records.reshape(lead_dims + (block_count, in_block))
    tails = blocks[:, :, :-1, in_block - tap_count :]
    tails = jnp.concatenate([jnp.zeros(lead_dims + (1, tap_count), records.dtype), tails], axis=2)
    windows = jnp.concatenate([tails, blocks], axis=3)
    tap_ids = jnp.arange(tap_count, dtype=jnp.int32)[:, None, None]
    in_ids = jnp.arange(in_block + tap_count, dtype=jnp.int32)[None, :, None]
    out_ids = jnp.arange(out_block, dtype=jnp.int32)[None, None, :]
    onehot = (in_ids == DECIM * out_ids + tap_count - tap_ids).astype(jnp.float32)
    band_matrix = jnp.einsum("k,kij->ij", fir_taps, onehot, precision=lax.Precision.HIGH)
    summed = jnp.einsum("swbi,ij->swbj", windows, band_matrix, precision=lax.Precision.HIGH)
    return summed.reshape(lead_dims + (block_count * out_block,))


def spectrum(decimated):
    out_length = decimated.shape[-1]
    first_len = 64
    second_len = out_length // first_len
    lead_dims = decimated.shape[:-1]
    blocks = decimated.reshape(lead_dims + (first_len, second_len))
    cos_one, sin_one = angle_table(first_len, first_len, first_len, 0)
    real_z = jnp.einsum("bwnq,fn->bwfq", blocks, cos_one, precision=lax.Precision.HIGH)
    imag_z = -jnp.einsum("bwnq,fn->bwfq", blocks, sin_one, precision=lax.Precision.HIGH)
    cos_two, sin_two = angle_table(first_len, second_len, out_length, 0)
    real_t = real_z * cos_two + imag_z * sin_two
    imag_t = imag_z * cos_two - real_z * sin_two
    cos_three, sin_three = angle_table(second_len // 2, second_len, second_len, 0)
    real_x = jnp.einsum(
        "bwfq,gq->bwgf", real_t, cos_three, precision=lax.Precision.HIGH
    ) + jnp.einsum("bwfq,gq->bwgf", imag_t, sin_three, precision=lax.Precision.HIGH)
    imag_x = jnp.einsum(
        "bwfq,gq->bwgf", imag_t, cos_three, precision=lax.Precision.HIGH
    ) - jnp.einsum("bwfq,gq->bwgf", real_t, sin_three, precision=lax.Precision.HIGH)
    bin_count = out_length // 2
    return (real_x.reshape(lead_dims + (bin_count,)), imag_x.reshape(lead_dims + (bin_count,)))


def whiten(spec_real, spec_imag):
    lead_dims = spec_real.shape[:-1]
    bin_count = spec_real.shape[-1]
    banded = lead_dims + (bin_count // BAND, BAND)
    squares = (spec_real * spec_real + spec_imag * spec_imag).reshape(banded)
    band_power = jnp.mean(squares, axis=-1, keepdims=True)
    inverse = 1.0 / jnp.sqrt(band_power + 1e-06)
    white_real = (spec_real.reshape(banded) * inverse).reshape(spec_real.shape)
    white_imag = (spec_imag.reshape(banded) * inverse).reshape(spec_imag.shape)
    return jnp.concatenate([white_real, white_imag], axis=-1).astype(jnp.bfloat16)


def cross_kernel(slots, *refs):
    piece_refs = refs[:len(slots)]
    left_perm, visit_perm, limit_ref, table_ref, out_ref, left_f32, visit_f32, cross_ref = refs[len(slots):]
    left_refs = [ref for ref, slot in zip(piece_refs, slots) if slot[0] == 0]
    window_count, piece, width = left_refs[0].shape
    rows_left = left_f32.shape[1]
    bin_count = width // 2
    chunk = 512
    while chunk > 128 and chunk * rows_left > 8192:
        chunk //= 2
    chunks = bin_count // chunk
    group_rows = cross_ref.shape[0]
    group = group_rows // (piece * rows_left)
    visit_count = visit_f32.shape[1] // piece
    scale = 1.0 / math.sqrt(window_count * bin_count)

    for ref, (kind, index) in zip(piece_refs, slots):
        target = left_f32 if kind == 0 else visit_f32
        target[:, index * piece:(index + 1) * piece, :] = ref[...].astype(jnp.float32)
    for window in range(window_count):
        for perm_ref, target in ((left_perm, left_f32), (visit_perm, visit_f32)):
            target[window] = jnp.dot(
                perm_ref[...], target[window].astype(jnp.bfloat16), preferred_element_type=jnp.float32
            )

    for first in range(0, visit_count, group):
        base = first * piece

        def one_chunk(step, carry):
            local = step // chunks
            partner = base + local
            off = pl.multiple_of((step % chunks) * chunk, chunk)
            acc_re = jnp.zeros((rows_left, chunk), jnp.float32)
            acc_im = jnp.zeros((rows_left, chunk), jnp.float32)
            for window in range(window_count):
                left_c = left_f32[window, :, pl.ds(off, chunk)]
                left_d = left_f32[window, :, pl.ds(off + bin_count, chunk)]
                vis_c = visit_f32[window, pl.ds(partner, 1), pl.ds(off, chunk)]
                vis_d = visit_f32[window, pl.ds(partner, 1), pl.ds(off + bin_count, chunk)]
                acc_re = acc_re + (left_c * vis_c + left_d * vis_d)
                acc_im = acc_im + (left_c * vis_d - left_d * vis_c)
            row = pl.multiple_of(local * rows_left, rows_left)
            cross_ref[pl.ds(row, rows_left), pl.ds(off, chunk)] = acc_re.astype(jnp.bfloat16)
            cross_ref[pl.ds(row, rows_left), pl.ds(off + bin_count, chunk)] = acc_im.astype(jnp.bfloat16)
            return carry

        lax.fori_loop(0, group * piece * chunks, one_chunk, 0)
        rows = pl.ds(base * rows_left, group_rows)
        block = jnp.dot(cross_ref[...], table_ref[...], preferred_element_type=jnp.float32) * scale
        lag = lax.broadcasted_iota(jnp.int32, block.shape, 1)
        keep = jnp.abs(lag - block.shape[1] // 2) <= limit_ref[rows, :]
        out_ref[rows, :] = jnp.where(keep, block, 0.0)


def pair_block(left_pieces, visit_pieces, left_perm, visit_perm, limit, lag_table, issue_order):
    window_count, piece, width = left_pieces[0].shape
    left_count = len(left_pieces)
    visit_count = len(visit_pieces)
    rows_left = left_count * piece
    visit_rows = visit_count * piece
    lag_count = lag_table.shape[1]
    group = max(1, min(visit_count, 256 // (piece * rows_left)))
    while visit_count % group:
        group -= 1
    flops = visit_rows * rows_left * width * (4 * window_count + 2 * lag_count)
    vmem = pltpu.VMEM
    return pl.pallas_call(
        functools.partial(cross_kernel, tuple(issue_order)),
        out_shape=jax.ShapeDtypeStruct((visit_rows * rows_left, lag_count), jnp.float32),
        in_specs=[pl.BlockSpec(memory_space=vmem)] * (left_count + visit_count + 4),
        out_specs=pl.BlockSpec(memory_space=vmem),
        scratch_shapes=[
            vmem((window_count, rows_left, width), jnp.float32),
            vmem((window_count, visit_rows, width), jnp.float32),
            vmem((group * piece * rows_left, width), jnp.bfloat16),
        ],
        compiler_params=pltpu.CompilerParams(vmem_limit_bytes=60 * 1024 * 1024),
        cost_estimate=pl.CostEstimate(
            flops=flops,
            transcendentals=0,
            bytes_accessed=2 * width * (window_count * (rows_left + visit_rows) + lag_count)
            + 4 * visit_rows * rows_left * lag_count,
        ),
    )(*[(left_pieces, visit_pieces)[kind][index] for kind, index in issue_order], left_perm, visit_perm, limit, lag_table)


def xor_gather(block, axis_name, size):
    if size & (size - 1):
        return [lax.all_gather(block, axis_name, axis=1, tiled=True)], None
    pieces = [block]
    for step in range(1, size):
        pairs = [(source, source ^ step) for source in range(size)]
        pieces.append(lax.ppermute(block, axis_name, pairs))
    order = lax.axis_index(axis_name) ^ jnp.arange(size, dtype=jnp.int32)
    return pieces, order


def chip_gather(block, axis_name, size):
    if size < 4 or size & (size - 1):
        return xor_gather(block, axis_name, size)
    chips = size // 2
    fetched = []
    for step in range(1, chips):
        pairs = [(source, source ^ (2 * step)) for source in range(size)]
        fetched.append(lax.ppermute(block, axis_name, pairs))
    partner = [(source, source ^ 1) for source in range(size)]
    pieces = [block, lax.ppermute(block, axis_name, partner)]
    piece = block.shape[1]
    swapped = lax.ppermute(jnp.concatenate(fetched, axis=1), axis_name, partner)
    for step in range(1, chips):
        pieces.append(fetched[step - 1])
        pieces.append(swapped[:, (step - 1) * piece:step * piece, :])
    order = lax.axis_index(axis_name) ^ jnp.arange(size, dtype=jnp.int32)
    return pieces, order


def on_device(records, fir_taps, lag_limit):
    block_size = records.shape[0]
    decimated = decimate(records, fir_taps)
    out_length = decimated.shape[-1]
    bin_count = out_length // 2
    spec_real, spec_imag = spectrum(decimated)
    white = whiten(spec_real, spec_imag)
    white_by_window = jnp.moveaxis(white, 1, 0)
    col_size = lax.axis_size("col")
    row_size = lax.axis_size("row")
    left_by_window, left_order = xor_gather(white_by_window, "col", col_size)
    cos_lag, sin_lag = angle_table(LAGS, bin_count, out_length, -LH)
    lag_table = jnp.concatenate([cos_lag.T, sin_lag.T], axis=0).astype(jnp.bfloat16)
    group_rows = sum(piece.shape[1] for piece in left_by_window)
    piece_rows, visit_order = chip_gather(white_by_window, "row", row_size)
    visit_count = sum(piece.shape[1] for piece in piece_rows)
    late_first = [(1, index) for index in range(len(piece_rows)) if index > 1 and index % 2 == 1]
    near = [(0, 0), (1, 0), (0, 1), (1, 1)][:2 + min(1, len(left_by_window) - 1) + min(1, len(piece_rows) - 1)]
    fetches = [(1, index) for index in range(len(piece_rows)) if index > 1 and index % 2 == 0]
    far = [(0, index) for index in range(2, len(left_by_window))]
    issue_order = [slot for slot in late_first + near + fetches + far[::-1]]
    issue_order = sorted(set(issue_order), key=issue_order.index)
    assert len(issue_order) == len(left_by_window) + len(piece_rows)
    piece = block_size
    left_pos = jnp.arange(group_rows, dtype=jnp.int32)
    visit_pos = jnp.arange(visit_count, dtype=jnp.int32)
    if left_order is not None:
        left_pos = left_order[left_pos // piece] * piece + left_pos % piece
    if visit_order is not None:
        visit_pos = visit_order[visit_pos // piece] * piece + visit_pos % piece
    left_perm = (jnp.arange(group_rows)[None, :] == left_pos[:, None]).astype(jnp.bfloat16)
    visit_perm = (jnp.arange(visit_count)[None, :] == visit_pos[:, None]).astype(jnp.bfloat16)
    limit = jnp.tile(lag_limit, visit_count)[:, None]
    pair = pair_block(left_by_window, piece_rows, left_perm, visit_perm, limit, lag_table, issue_order)
    pair = jnp.swapaxes(pair.reshape(visit_count, group_rows, LAGS), 0, 1)
    return pair[:, None]


def solution(mesh):
    placed = (P(("row", "col"), None, None), P(), P("row"))
    return jax.shard_map(
        on_device,
        mesh=mesh,
        in_specs=placed,
        out_specs=P("row", "col", None, None),
        check_vma=False,
    )
```

```python
import functools
import math

import jax
import jax.numpy as jnp
from jax import lax
from jax.experimental import pallas as pl
from jax.experimental.pallas import tpu as pltpu
from jax.sharding import PartitionSpec as P

DECIM = 2
LAGS = 128
BAND = 64
LH = 64


def angle_table(row_count, col_count, period, offset):
    row_ids = jnp.arange(row_count, dtype=jnp.int32)[:, None] + offset
    col_ids = jnp.arange(col_count, dtype=jnp.int32)[None, :]
    phase_int = jnp.mod(row_ids * col_ids, period)
    angles = phase_int.astype(jnp.float32) * (2.0 * math.pi / period)
    return (jnp.cos(angles), jnp.sin(angles))


def decimate(records, fir_taps):
    tap_count = fir_taps.shape[0]
    out_block = 128
    in_block = DECIM * out_block
    lead_dims = records.shape[:2]
    block_count = records.shape[2] // in_block
    blocks = records.reshape(lead_dims + (block_count, in_block))
    tails = blocks[:, :, :-1, in_block - tap_count :]
    tails = jnp.concatenate([jnp.zeros(lead_dims + (1, tap_count), records.dtype), tails], axis=2)
    windows = jnp.concatenate([tails, blocks], axis=3)
    tap_ids = jnp.arange(tap_count, dtype=jnp.int32)[:, None, None]
    in_ids = jnp.arange(in_block + tap_count, dtype=jnp.int32)[None, :, None]
    out_ids = jnp.arange(out_block, dtype=jnp.int32)[None, None, :]
    onehot = (in_ids == DECIM * out_ids + tap_count - tap_ids).astype(jnp.float32)
    band_matrix = jnp.einsum("k,kij->ij", fir_taps, onehot, precision=lax.Precision.HIGH)
    summed = jnp.einsum("swbi,ij->swbj", windows, band_matrix, precision=lax.Precision.HIGH)
    return summed.reshape(lead_dims + (block_count * out_block,))


def spectrum(decimated):
    out_length = decimated.shape[-1]
    first_len = 64
    second_len = out_length // first_len
    lead_dims = decimated.shape[:-1]
    blocks = decimated.reshape(lead_dims + (first_len, second_len))
    cos_one, sin_one = angle_table(first_len, first_len, first_len, 0)
    real_z = jnp.einsum("bwnq,fn->bwfq", blocks, cos_one, precision=lax.Precision.HIGH)
    imag_z = -jnp.einsum("bwnq,fn->bwfq", blocks, sin_one, precision=lax.Precision.HIGH)
    cos_two, sin_two = angle_table(first_len, second_len, out_length, 0)
    real_t = real_z * cos_two + imag_z * sin_two
    imag_t = imag_z * cos_two - real_z * sin_two
    cos_three, sin_three = angle_table(second_len // 2, second_len, second_len, 0)
    real_x = jnp.einsum(
        "bwfq,gq->bwgf", real_t, cos_three, precision=lax.Precision.HIGH
    ) + jnp.einsum("bwfq,gq->bwgf", imag_t, sin_three, precision=lax.Precision.HIGH)
    imag_x = jnp.einsum(
        "bwfq,gq->bwgf", imag_t, cos_three, precision=lax.Precision.HIGH
    ) - jnp.einsum("bwfq,gq->bwgf", real_t, sin_three, precision=lax.Precision.HIGH)
    bin_count = out_length // 2
    return (real_x.reshape(lead_dims + (bin_count,)), imag_x.reshape(lead_dims + (bin_count,)))


def whiten(spec_real, spec_imag):
    lead_dims = spec_real.shape[:-1]
    bin_count = spec_real.shape[-1]
    banded = lead_dims + (bin_count // BAND, BAND)
    squares = (spec_real * spec_real + spec_imag * spec_imag).reshape(banded)
    band_power = jnp.mean(squares, axis=-1, keepdims=True)
    inverse = 1.0 / jnp.sqrt(band_power + 1e-06)
    white_real = (spec_real.reshape(banded) * inverse).reshape(spec_real.shape)
    white_imag = (spec_imag.reshape(banded) * inverse).reshape(spec_imag.shape)
    return jnp.concatenate([white_real, white_imag], axis=-1).astype(jnp.bfloat16)


def cross_kernel(slots, *refs):
    piece_refs = refs[:len(slots)]
    left_perm, visit_perm, table_ref, out_ref, left_f32, visit_f32, cross_ref = refs[len(slots):]
    left_refs = [ref for ref, slot in zip(piece_refs, slots) if slot[0] == 0]
    window_count, piece, width = left_refs[0].shape
    rows_left = left_f32.shape[1]
    bin_count = width // 2
    chunk = 512
    while chunk > 128 and chunk * rows_left > 8192:
        chunk //= 2
    chunks = bin_count // chunk
    group_rows = cross_ref.shape[0]
    group = group_rows // (piece * rows_left)
    visit_count = visit_f32.shape[1] // piece

    for ref, (kind, index) in zip(piece_refs, slots):
        target = left_f32 if kind == 0 else visit_f32
        target[:, index * piece:(index + 1) * piece, :] = ref[...].astype(jnp.float32)
    for window in range(window_count):
        for perm_ref, target in ((left_perm, left_f32), (visit_perm, visit_f32)):
            target[window] = jnp.dot(
                perm_ref[...], target[window].astype(jnp.bfloat16), preferred_element_type=jnp.float32
            )

    for first in range(0, visit_count, group):
        base = first * piece

        def one_chunk(step, carry):
            local = step // chunks
            partner = base + local
            off = pl.multiple_of((step % chunks) * chunk, chunk)
            acc_re = jnp.zeros((rows_left, chunk), jnp.float32)
            acc_im = jnp.zeros((rows_left, chunk), jnp.float32)
            for window in range(window_count):
                left_c = left_f32[window, :, pl.ds(off, chunk)]
                left_d = left_f32[window, :, pl.ds(off + bin_count, chunk)]
                vis_c = visit_f32[window, pl.ds(partner, 1), pl.ds(off, chunk)]
                vis_d = visit_f32[window, pl.ds(partner, 1), pl.ds(off + bin_count, chunk)]
                acc_re = acc_re + (left_c * vis_c + left_d * vis_d)
                acc_im = acc_im + (left_c * vis_d - left_d * vis_c)
            row = pl.multiple_of(local * rows_left, rows_left)
            cross_ref[pl.ds(row, rows_left), pl.ds(off, chunk)] = acc_re.astype(jnp.bfloat16)
            cross_ref[pl.ds(row, rows_left), pl.ds(off + bin_count, chunk)] = acc_im.astype(jnp.bfloat16)
            return carry

        lax.fori_loop(0, group * piece * chunks, one_chunk, 0)
        out_ref[base * rows_left:base * rows_left + group_rows, :] = jnp.dot(
            cross_ref[...], table_ref[...], preferred_element_type=jnp.float32
        )


def pair_block(left_pieces, visit_pieces, left_perm, visit_perm, lag_table, issue_order):
    window_count, piece, width = left_pieces[0].shape
    left_count = len(left_pieces)
    visit_count = len(visit_pieces)
    rows_left = left_count * piece
    visit_rows = visit_count * piece
    lag_count = lag_table.shape[1]
    group = max(1, min(visit_count, 256 // (piece * rows_left)))
    while visit_count % group:
        group -= 1
    flops = visit_rows * rows_left * width * (4 * window_count + 2 * lag_count)
    vmem = pltpu.VMEM
    return pl.pallas_call(
        functools.partial(cross_kernel, tuple(issue_order)),
        out_shape=jax.ShapeDtypeStruct((visit_rows * rows_left, lag_count), jnp.float32),
        in_specs=[pl.BlockSpec(memory_space=vmem)] * (left_count + visit_count + 3),
        out_specs=pl.BlockSpec(memory_space=vmem),
        scratch_shapes=[
            vmem((window_count, rows_left, width), jnp.float32),
            vmem((window_count, visit_rows, width), jnp.float32),
            vmem((group * piece * rows_left, width), jnp.bfloat16),
        ],
        compiler_params=pltpu.CompilerParams(vmem_limit_bytes=60 * 1024 * 1024),
        cost_estimate=pl.CostEstimate(
            flops=flops,
            transcendentals=0,
            bytes_accessed=2 * width * (window_count * (rows_left + visit_rows) + lag_count)
            + 4 * visit_rows * rows_left * lag_count,
        ),
    )(*[(left_pieces, visit_pieces)[kind][index] for kind, index in issue_order], left_perm, visit_perm, lag_table)


def xor_gather(block, axis_name, size):
    if size & (size - 1):
        return [lax.all_gather(block, axis_name, axis=1, tiled=True)], None
    pieces = [block]
    for step in range(1, size):
        pairs = [(source, source ^ step) for source in range(size)]
        pieces.append(lax.ppermute(block, axis_name, pairs))
    order = lax.axis_index(axis_name) ^ jnp.arange(size, dtype=jnp.int32)
    return pieces, order


def chip_gather(block, axis_name, size):
    if size < 4 or size & (size - 1):
        return xor_gather(block, axis_name, size)
    chips = size // 2
    fetched = []
    for step in range(1, chips):
        pairs = [(source, source ^ (2 * step)) for source in range(size)]
        fetched.append(lax.ppermute(block, axis_name, pairs))
    partner = [(source, source ^ 1) for source in range(size)]
    pieces = [block, lax.ppermute(block, axis_name, partner)]
    piece = block.shape[1]
    swapped = lax.ppermute(jnp.concatenate(fetched, axis=1), axis_name, partner)
    for step in range(1, chips):
        pieces.append(fetched[step - 1])
        pieces.append(swapped[:, (step - 1) * piece:step * piece, :])
    order = lax.axis_index(axis_name) ^ jnp.arange(size, dtype=jnp.int32)
    return pieces, order


def on_device(records, fir_taps, lag_limit):
    block_size = records.shape[0]
    decimated = decimate(records, fir_taps)
    out_length = decimated.shape[-1]
    bin_count = out_length // 2
    spec_real, spec_imag = spectrum(decimated)
    white = whiten(spec_real, spec_imag)
    white_by_window = jnp.moveaxis(white, 1, 0)
    col_size = lax.axis_size("col")
    row_size = lax.axis_size("row")
    left_by_window, left_order = xor_gather(white_by_window, "col", col_size)
    cos_lag, sin_lag = angle_table(LAGS, bin_count, out_length, -LH)
    lag_table = jnp.concatenate([cos_lag.T, sin_lag.T], axis=0).astype(jnp.bfloat16)
    group_rows = sum(piece.shape[1] for piece in left_by_window)
    piece_rows, visit_order = chip_gather(white_by_window, "row", row_size)
    visit_count = sum(piece.shape[1] for piece in piece_rows)
    late_first = [(1, index) for index in range(len(piece_rows)) if index > 1 and index % 2 == 1]
    near = [(0, 0), (1, 0), (0, 1), (1, 1)][:2 + min(1, len(left_by_window) - 1) + min(1, len(piece_rows) - 1)]
    fetches = [(1, index) for index in range(len(piece_rows)) if index > 1 and index % 2 == 0]
    far = [(0, index) for index in range(2, len(left_by_window))]
    issue_order = [slot for slot in late_first + near[:2] + near[3:] + fetches[:1] + near[2:3] + fetches[1:] + far[::-1]]
    issue_order = sorted(set(issue_order), key=issue_order.index)
    assert len(issue_order) == len(left_by_window) + len(piece_rows)
    piece = block_size
    left_pos = jnp.arange(group_rows, dtype=jnp.int32)
    visit_pos = jnp.arange(visit_count, dtype=jnp.int32)
    if left_order is not None:
        left_pos = left_order[left_pos // piece] * piece + left_pos % piece
    if visit_order is not None:
        visit_pos = visit_order[visit_pos // piece] * piece + visit_pos % piece
    left_perm = (jnp.arange(group_rows)[None, :] == left_pos[:, None]).astype(jnp.bfloat16)
    visit_perm = (jnp.arange(visit_count)[None, :] == visit_pos[:, None]).astype(jnp.bfloat16)
    pair = pair_block(left_by_window, piece_rows, left_perm, visit_perm, lag_table, issue_order)
    pair = jnp.swapaxes(pair.reshape(visit_count, group_rows, LAGS), 0, 1)
    norm_scale = 1.0 / math.sqrt(white.shape[1] * bin_count)
    pair = pair * norm_scale
    lag_offset = jnp.abs(jnp.arange(LAGS, dtype=jnp.int32) - LH)
    keep_mask = lag_offset[None, :] <= lag_limit[:, None]
    tile_stack = jnp.where(keep_mask[:, None, :], pair, 0.0)
    return tile_stack[:, None]


def solution(mesh):
    placed = (P(("row", "col"), None, None), P(), P("row"))
    return jax.shard_map(
        on_device,
        mesh=mesh,
        in_specs=placed,
        out_specs=P("row", "col", None, None),
        check_vma=False,
    )
```

```python
import functools
import math

import jax
import jax.numpy as jnp
from jax import lax
from jax.experimental import pallas as pl
from jax.experimental.pallas import tpu as pltpu
from jax.sharding import PartitionSpec as P

DECIM = 2
LAGS = 128
BAND = 64
LH = 64


def angle_table(row_count, col_count, period, offset):
    row_ids = jnp.arange(row_count, dtype=jnp.int32)[:, None] + offset
    col_ids = jnp.arange(col_count, dtype=jnp.int32)[None, :]
    phase_int = jnp.mod(row_ids * col_ids, period)
    angles = phase_int.astype(jnp.float32) * (2.0 * math.pi / period)
    return (jnp.cos(angles), jnp.sin(angles))


def decimate(records, fir_taps):
    tap_count = fir_taps.shape[0]
    out_block = 128
    in_block = DECIM * out_block
    lead_dims = records.shape[:2]
    block_count = records.shape[2] // in_block
    blocks = records.reshape(lead_dims + (block_count, in_block))
    tails = blocks[:, :, :-1, in_block - tap_count :]
    tails = jnp.concatenate([jnp.zeros(lead_dims + (1, tap_count), records.dtype), tails], axis=2)
    windows = jnp.concatenate([tails, blocks], axis=3)
    tap_ids = jnp.arange(tap_count, dtype=jnp.int32)[:, None, None]
    in_ids = jnp.arange(in_block + tap_count, dtype=jnp.int32)[None, :, None]
    out_ids = jnp.arange(out_block, dtype=jnp.int32)[None, None, :]
    onehot = (in_ids == DECIM * out_ids + tap_count - tap_ids).astype(jnp.float32)
    band_matrix = jnp.einsum("k,kij->ij", fir_taps, onehot, precision=lax.Precision.HIGH)
    summed = jnp.einsum("swbi,ij->swbj", windows, band_matrix, precision=lax.Precision.HIGH)
    return summed.reshape(lead_dims + (block_count * out_block,))


def spectrum(decimated):
    out_length = decimated.shape[-1]
    first_len = 64
    second_len = out_length // first_len
    lead_dims = decimated.shape[:-1]
    blocks = decimated.reshape(lead_dims + (first_len, second_len))
    cos_one, sin_one = angle_table(first_len, first_len, first_len, 0)
    real_z = jnp.einsum("bwnq,fn->bwfq", blocks, cos_one, precision=lax.Precision.HIGH)
    imag_z = -jnp.einsum("bwnq,fn->bwfq", blocks, sin_one, precision=lax.Precision.HIGH)
    cos_two, sin_two = angle_table(first_len, second_len, out_length, 0)
    real_t = real_z * cos_two + imag_z * sin_two
    imag_t = imag_z * cos_two - real_z * sin_two
    cos_three, sin_three = angle_table(second_len // 2, second_len, second_len, 0)
    real_x = jnp.einsum(
        "bwfq,gq->bwgf", real_t, cos_three, precision=lax.Precision.HIGH
    ) + jnp.einsum("bwfq,gq->bwgf", imag_t, sin_three, precision=lax.Precision.HIGH)
    imag_x = jnp.einsum(
        "bwfq,gq->bwgf", imag_t, cos_three, precision=lax.Precision.HIGH
    ) - jnp.einsum("bwfq,gq->bwgf", real_t, sin_three, precision=lax.Precision.HIGH)
    bin_count = out_length // 2
    return (real_x.reshape(lead_dims + (bin_count,)), imag_x.reshape(lead_dims + (bin_count,)))


def whiten(spec_real, spec_imag):
    lead_dims = spec_real.shape[:-1]
    bin_count = spec_real.shape[-1]
    banded = lead_dims + (bin_count // BAND, BAND)
    squares = (spec_real * spec_real + spec_imag * spec_imag).reshape(banded)
    band_power = jnp.mean(squares, axis=-1, keepdims=True)
    inverse = 1.0 / jnp.sqrt(band_power + 1e-06)
    white_real = (spec_real.reshape(banded) * inverse).reshape(spec_real.shape)
    white_imag = (spec_imag.reshape(banded) * inverse).reshape(spec_imag.shape)
    return jnp.concatenate([white_real, white_imag], axis=-1).astype(jnp.bfloat16)


def cross_kernel(slots, *refs):
    piece_refs = refs[:len(slots)]
    left_perm, visit_perm, table_ref, out_ref, left_f32, visit_f32, cross_ref = refs[len(slots):]
    left_refs = [ref for ref, slot in zip(piece_refs, slots) if slot[0] == 0]
    window_count, piece, width = left_refs[0].shape
    rows_left = left_f32.shape[1]
    bin_count = width // 2
    chunk = 256
    while chunk > 128 and chunk * rows_left > 8192:
        chunk //= 2
    chunks = bin_count // chunk
    group_rows = cross_ref.shape[0]
    group = group_rows // (piece * rows_left)
    visit_count = visit_f32.shape[1] // piece

    for ref, (kind, index) in zip(piece_refs, slots):
        target = left_f32 if kind == 0 else visit_f32
        target[:, index * piece:(index + 1) * piece, :] = ref[...].astype(jnp.float32)
    for window in range(window_count):
        for perm_ref, target in ((left_perm, left_f32), (visit_perm, visit_f32)):
            target[window] = jnp.dot(
                perm_ref[...], target[window].astype(jnp.bfloat16), preferred_element_type=jnp.float32
            )

    for first in range(0, visit_count, group):
        base = first * piece

        def one_chunk(step, carry):
            local = (step // chunks) * 2
            off = pl.multiple_of((step % chunks) * chunk, chunk)
            sums = [jnp.zeros((rows_left, chunk), jnp.float32) for _ in range(4)]
            for window in range(window_count):
                left_c = left_f32[window, :, pl.ds(off, chunk)]
                left_d = left_f32[window, :, pl.ds(off + bin_count, chunk)]
                for pick in range(2):
                    partner = base + local + pick
                    vis_c = visit_f32[window, pl.ds(partner, 1), pl.ds(off, chunk)]
                    vis_d = visit_f32[window, pl.ds(partner, 1), pl.ds(off + bin_count, chunk)]
                    sums[2 * pick] = sums[2 * pick] + (left_c * vis_c + left_d * vis_d)
                    sums[2 * pick + 1] = sums[2 * pick + 1] + (left_c * vis_d - left_d * vis_c)
            for pick in range(2):
                row = pl.multiple_of((local + pick) * rows_left, rows_left)
                cross_ref[pl.ds(row, rows_left), pl.ds(off, chunk)] = sums[2 * pick].astype(jnp.bfloat16)
                cross_ref[pl.ds(row, rows_left), pl.ds(off + bin_count, chunk)] = sums[2 * pick + 1].astype(
                    jnp.bfloat16
                )
            return carry

        lax.fori_loop(0, group * piece // 2 * chunks, one_chunk, 0)
        out_ref[base * rows_left:base * rows_left + group_rows, :] = jnp.dot(
            cross_ref[...], table_ref[...], preferred_element_type=jnp.float32
        )


def pair_block(left_pieces, visit_pieces, left_perm, visit_perm, lag_table, issue_order):
    window_count, piece, width = left_pieces[0].shape
    left_count = len(left_pieces)
    visit_count = len(visit_pieces)
    rows_left = left_count * piece
    visit_rows = visit_count * piece
    lag_count = lag_table.shape[1]
    group = max(1, min(visit_count, 256 // (piece * rows_left)))
    while visit_count % group:
        group -= 1
    flops = visit_rows * rows_left * width * (4 * window_count + 2 * lag_count)
    vmem = pltpu.VMEM
    return pl.pallas_call(
        functools.partial(cross_kernel, tuple(issue_order)),
        out_shape=jax.ShapeDtypeStruct((visit_rows * rows_left, lag_count), jnp.float32),
        in_specs=[pl.BlockSpec(memory_space=vmem)] * (left_count + visit_count + 3),
        out_specs=pl.BlockSpec(memory_space=vmem),
        scratch_shapes=[
            vmem((window_count, rows_left, width), jnp.float32),
            vmem((window_count, visit_rows, width), jnp.float32),
            vmem((group * piece * rows_left, width), jnp.bfloat16),
        ],
        compiler_params=pltpu.CompilerParams(vmem_limit_bytes=60 * 1024 * 1024),
        cost_estimate=pl.CostEstimate(
            flops=flops,
            transcendentals=0,
            bytes_accessed=2 * width * (window_count * (rows_left + visit_rows) + lag_count)
            + 4 * visit_rows * rows_left * lag_count,
        ),
    )(*[(left_pieces, visit_pieces)[kind][index] for kind, index in issue_order], left_perm, visit_perm, lag_table)


def xor_gather(block, axis_name, size):
    if size & (size - 1):
        return [lax.all_gather(block, axis_name, axis=1, tiled=True)], None
    pieces = [block]
    for step in range(1, size):
        pairs = [(source, source ^ step) for source in range(size)]
        pieces.append(lax.ppermute(block, axis_name, pairs))
    order = lax.axis_index(axis_name) ^ jnp.arange(size, dtype=jnp.int32)
    return pieces, order


def chip_gather(block, axis_name, size):
    if size < 4 or size & (size - 1):
        return xor_gather(block, axis_name, size)
    chips = size // 2
    fetched = []
    for step in range(1, chips):
        pairs = [(source, source ^ (2 * step)) for source in range(size)]
        fetched.append(lax.ppermute(block, axis_name, pairs))
    partner = [(source, source ^ 1) for source in range(size)]
    pieces = [block, lax.ppermute(block, axis_name, partner)]
    piece = block.shape[1]
    swapped = lax.ppermute(jnp.concatenate(fetched, axis=1), axis_name, partner)
    for step in range(1, chips):
        pieces.append(fetched[step - 1])
        pieces.append(swapped[:, (step - 1) * piece:step * piece, :])
    order = lax.axis_index(axis_name) ^ jnp.arange(size, dtype=jnp.int32)
    return pieces, order


def on_device(records, fir_taps, lag_limit):
    block_size = records.shape[0]
    decimated = decimate(records, fir_taps)
    out_length = decimated.shape[-1]
    bin_count = out_length // 2
    spec_real, spec_imag = spectrum(decimated)
    white = whiten(spec_real, spec_imag)
    white_by_window = jnp.moveaxis(white, 1, 0)
    col_size = lax.axis_size("col")
    row_size = lax.axis_size("row")
    left_by_window, left_order = xor_gather(white_by_window, "col", col_size)
    cos_lag, sin_lag = angle_table(LAGS, bin_count, out_length, -LH)
    lag_table = jnp.concatenate([cos_lag.T, sin_lag.T], axis=0).astype(jnp.bfloat16)
    group_rows = sum(piece.shape[1] for piece in left_by_window)
    piece_rows, visit_order = chip_gather(white_by_window, "row", row_size)
    visit_count = sum(piece.shape[1] for piece in piece_rows)
    late_first = [(1, index) for index in range(len(piece_rows)) if index > 1 and index % 2 == 1]
    near = [(0, 0), (1, 0), (0, 1), (1, 1)][:2 + min(1, len(left_by_window) - 1) + min(1, len(piece_rows) - 1)]
    fetches = [(1, index) for index in range(len(piece_rows)) if index > 1 and index % 2 == 0]
    far = [(0, index) for index in range(2, len(left_by_window))]
    issue_order = [slot for slot in late_first + near[:2] + near[3:] + fetches[:1] + near[2:3] + fetches[1:] + far[::-1]]
    issue_order = sorted(set(issue_order), key=issue_order.index)
    assert len(issue_order) == len(left_by_window) + len(piece_rows)
    piece = block_size
    left_pos = jnp.arange(group_rows, dtype=jnp.int32)
    visit_pos = jnp.arange(visit_count, dtype=jnp.int32)
    if left_order is not None:
        left_pos = left_order[left_pos // piece] * piece + left_pos % piece
    if visit_order is not None:
        visit_pos = visit_order[visit_pos // piece] * piece + visit_pos % piece
    left_perm = (jnp.arange(group_rows)[None, :] == left_pos[:, None]).astype(jnp.bfloat16)
    visit_perm = (jnp.arange(visit_count)[None, :] == visit_pos[:, None]).astype(jnp.bfloat16)
    pair = pair_block(left_by_window, piece_rows, left_perm, visit_perm, lag_table, issue_order)
    pair = jnp.swapaxes(pair.reshape(visit_count, group_rows, LAGS), 0, 1)
    norm_scale = 1.0 / math.sqrt(white.shape[1] * bin_count)
    pair = pair * norm_scale
    lag_offset = jnp.abs(jnp.arange(LAGS, dtype=jnp.int32) - LH)
    keep_mask = lag_offset[None, :] <= lag_limit[:, None]
    tile_stack = jnp.where(keep_mask[:, None, :], pair, 0.0)
    return tile_stack[:, None]


def solution(mesh):
    placed = (P(("row", "col"), None, None), P(), P("row"))
    return jax.shard_map(
        on_device,
        mesh=mesh,
        in_specs=placed,
        out_specs=P("row", "col", None, None),
        check_vma=False,
    )
```

```python
import functools
import math

import jax
import jax.numpy as jnp
from jax import lax
from jax.experimental import pallas as pl
from jax.experimental.pallas import tpu as pltpu
from jax.sharding import PartitionSpec as P

DECIM = 2
LAGS = 128
BAND = 64
LH = 64


def angle_table(row_count, col_count, period, offset):
    row_ids = jnp.arange(row_count, dtype=jnp.int32)[:, None] + offset
    col_ids = jnp.arange(col_count, dtype=jnp.int32)[None, :]
    phase_int = jnp.mod(row_ids * col_ids, period)
    angles = phase_int.astype(jnp.float32) * (2.0 * math.pi / period)
    return (jnp.cos(angles), jnp.sin(angles))


def decimate(records, fir_taps):
    tap_count = fir_taps.shape[0]
    out_block = 128
    in_block = DECIM * out_block
    lead_dims = records.shape[:2]
    block_count = records.shape[2] // in_block
    blocks = records.reshape(lead_dims + (block_count, in_block))
    tails = blocks[:, :, :-1, in_block - tap_count :]
    tails = jnp.concatenate([jnp.zeros(lead_dims + (1, tap_count), records.dtype), tails], axis=2)
    windows = jnp.concatenate([tails, blocks], axis=3)
    tap_ids = jnp.arange(tap_count, dtype=jnp.int32)[:, None, None]
    in_ids = jnp.arange(in_block + tap_count, dtype=jnp.int32)[None, :, None]
    out_ids = jnp.arange(out_block, dtype=jnp.int32)[None, None, :]
    onehot = (in_ids == DECIM * out_ids + tap_count - tap_ids).astype(jnp.float32)
    band_matrix = jnp.einsum("k,kij->ij", fir_taps, onehot, precision=lax.Precision.HIGH)
    summed = jnp.einsum("swbi,ij->swbj", windows, band_matrix, precision=lax.Precision.HIGH)
    return summed.reshape(lead_dims + (block_count * out_block,))


def spectrum(decimated):
    out_length = decimated.shape[-1]
    first_len = 64
    second_len = out_length // first_len
    lead_dims = decimated.shape[:-1]
    blocks = decimated.reshape(lead_dims + (first_len, second_len))
    cos_one, sin_one = angle_table(first_len, first_len, first_len, 0)
    real_z = jnp.einsum("bwnq,fn->bwfq", blocks, cos_one, precision=lax.Precision.HIGH)
    imag_z = -jnp.einsum("bwnq,fn->bwfq", blocks, sin_one, precision=lax.Precision.HIGH)
    cos_two, sin_two = angle_table(first_len, second_len, out_length, 0)
    real_t = real_z * cos_two + imag_z * sin_two
    imag_t = imag_z * cos_two - real_z * sin_two
    cos_three, sin_three = angle_table(second_len // 2, second_len, second_len, 0)
    real_x = jnp.einsum(
        "bwfq,gq->bwgf", real_t, cos_three, precision=lax.Precision.HIGH
    ) + jnp.einsum("bwfq,gq->bwgf", imag_t, sin_three, precision=lax.Precision.HIGH)
    imag_x = jnp.einsum(
        "bwfq,gq->bwgf", imag_t, cos_three, precision=lax.Precision.HIGH
    ) - jnp.einsum("bwfq,gq->bwgf", real_t, sin_three, precision=lax.Precision.HIGH)
    bin_count = out_length // 2
    return (real_x.reshape(lead_dims + (bin_count,)), imag_x.reshape(lead_dims + (bin_count,)))


def whiten(spec_real, spec_imag):
    lead_dims = spec_real.shape[:-1]
    bin_count = spec_real.shape[-1]
    banded = lead_dims + (bin_count // BAND, BAND)
    squares = (spec_real * spec_real + spec_imag * spec_imag).reshape(banded)
    band_power = jnp.mean(squares, axis=-1, keepdims=True)
    inverse = 1.0 / jnp.sqrt(band_power + 1e-06)
    white_real = (spec_real.reshape(banded) * inverse).reshape(spec_real.shape)
    white_imag = (spec_imag.reshape(banded) * inverse).reshape(spec_imag.shape)
    return jnp.concatenate([white_real, white_imag], axis=-1).astype(jnp.bfloat16)


def cross_kernel(slots, *refs):
    piece_refs = refs[:len(slots)]
    left_perm, visit_perm, table_ref, out_ref, left_f32, visit_f32, left_diff, visit_mix, cross_ref = refs[
        len(slots):
    ]
    left_refs = [ref for ref, slot in zip(piece_refs, slots) if slot[0] == 0]
    window_count, piece, width = left_refs[0].shape
    rows_left = left_f32.shape[1]
    bin_count = width // 2
    chunk = 512
    while chunk > 128 and chunk * rows_left > 8192:
        chunk //= 2
    chunks = bin_count // chunk
    group_rows = cross_ref.shape[0]
    group = group_rows // (piece * rows_left)
    visit_count = visit_f32.shape[1] // piece

    for ref, (kind, index) in zip(piece_refs, slots):
        target = left_f32 if kind == 0 else visit_f32
        target[:, index * piece:(index + 1) * piece, :] = ref[...].astype(jnp.float32)
    for window in range(window_count):
        for perm_ref, target in ((left_perm, left_f32), (visit_perm, visit_f32)):
            target[window] = jnp.dot(
                perm_ref[...], target[window].astype(jnp.bfloat16), preferred_element_type=jnp.float32
            )
        left_diff[window] = left_f32[window, :, :bin_count] - left_f32[window, :, bin_count:]
        vis_c = visit_f32[window, :, :bin_count]
        vis_d = visit_f32[window, :, bin_count:]
        visit_mix[window, :, :bin_count] = vis_c + vis_d
        visit_mix[window, :, bin_count:] = vis_d - vis_c

    for first in range(0, visit_count, group):
        base = first * piece

        def one_chunk(step, carry):
            local = step // chunks
            partner = base + local
            off = pl.multiple_of((step % chunks) * chunk, chunk)
            acc_re = jnp.zeros((rows_left, chunk), jnp.float32)
            acc_im = jnp.zeros((rows_left, chunk), jnp.float32)
            for window in range(window_count):
                left_c = left_f32[window, :, pl.ds(off, chunk)]
                left_d = left_f32[window, :, pl.ds(off + bin_count, chunk)]
                left_cd = left_diff[window, :, pl.ds(off, chunk)]
                vis_c = visit_f32[window, pl.ds(partner, 1), pl.ds(off, chunk)]
                vis_sum = visit_mix[window, pl.ds(partner, 1), pl.ds(off, chunk)]
                vis_diff = visit_mix[window, pl.ds(partner, 1), pl.ds(off + bin_count, chunk)]
                shared = vis_c * left_cd
                acc_re = acc_re + (shared + left_d * vis_sum)
                acc_im = acc_im + (shared + left_c * vis_diff)
            row = pl.multiple_of(local * rows_left, rows_left)
            cross_ref[pl.ds(row, rows_left), pl.ds(off, chunk)] = acc_re.astype(jnp.bfloat16)
            cross_ref[pl.ds(row, rows_left), pl.ds(off + bin_count, chunk)] = acc_im.astype(jnp.bfloat16)
            return carry

        lax.fori_loop(0, group * piece * chunks, one_chunk, 0)
        out_ref[base * rows_left:base * rows_left + group_rows, :] = jnp.dot(
            cross_ref[...], table_ref[...], preferred_element_type=jnp.float32
        )


def pair_block(left_pieces, visit_pieces, left_perm, visit_perm, lag_table, issue_order):
    window_count, piece, width = left_pieces[0].shape
    left_count = len(left_pieces)
    visit_count = len(visit_pieces)
    rows_left = left_count * piece
    visit_rows = visit_count * piece
    lag_count = lag_table.shape[1]
    group = max(1, min(visit_count, 256 // (piece * rows_left)))
    while visit_count % group:
        group -= 1
    flops = visit_rows * rows_left * width * (4 * window_count + 2 * lag_count)
    vmem = pltpu.VMEM
    return pl.pallas_call(
        functools.partial(cross_kernel, tuple(issue_order)),
        out_shape=jax.ShapeDtypeStruct((visit_rows * rows_left, lag_count), jnp.float32),
        in_specs=[pl.BlockSpec(memory_space=vmem)] * (left_count + visit_count + 3),
        out_specs=pl.BlockSpec(memory_space=vmem),
        scratch_shapes=[
            vmem((window_count, rows_left, width), jnp.float32),
            vmem((window_count, visit_rows, width), jnp.float32),
            vmem((window_count, rows_left, width // 2), jnp.float32),
            vmem((window_count, visit_rows, width), jnp.float32),
            vmem((group * piece * rows_left, width), jnp.bfloat16),
        ],
        compiler_params=pltpu.CompilerParams(vmem_limit_bytes=60 * 1024 * 1024),
        cost_estimate=pl.CostEstimate(
            flops=flops,
            transcendentals=0,
            bytes_accessed=2 * width * (window_count * (rows_left + visit_rows) + lag_count)
            + 4 * visit_rows * rows_left * lag_count,
        ),
    )(*[(left_pieces, visit_pieces)[kind][index] for kind, index in issue_order], left_perm, visit_perm, lag_table)


def xor_gather(block, axis_name, size):
    if size & (size - 1):
        return [lax.all_gather(block, axis_name, axis=1, tiled=True)], None
    pieces = [block]
    for step in range(1, size):
        pairs = [(source, source ^ step) for source in range(size)]
        pieces.append(lax.ppermute(block, axis_name, pairs))
    order = lax.axis_index(axis_name) ^ jnp.arange(size, dtype=jnp.int32)
    return pieces, order


def chip_gather(block, axis_name, size):
    if size < 4 or size & (size - 1):
        return xor_gather(block, axis_name, size)
    chips = size // 2
    fetched = []
    for step in range(1, chips):
        pairs = [(source, source ^ (2 * step)) for source in range(size)]
        fetched.append(lax.ppermute(block, axis_name, pairs))
    partner = [(source, source ^ 1) for source in range(size)]
    pieces = [block, lax.ppermute(block, axis_name, partner)]
    piece = block.shape[1]
    swapped = lax.ppermute(jnp.concatenate(fetched, axis=1), axis_name, partner)
    for step in range(1, chips):
        pieces.append(fetched[step - 1])
        pieces.append(swapped[:, (step - 1) * piece:step * piece, :])
    order = lax.axis_index(axis_name) ^ jnp.arange(size, dtype=jnp.int32)
    return pieces, order


def on_device(records, fir_taps, lag_limit):
    block_size = records.shape[0]
    decimated = decimate(records, fir_taps)
    out_length = decimated.shape[-1]
    bin_count = out_length // 2
    spec_real, spec_imag = spectrum(decimated)
    white = whiten(spec_real, spec_imag)
    white_by_window = jnp.moveaxis(white, 1, 0)
    col_size = lax.axis_size("col")
    row_size = lax.axis_size("row")
    left_by_window, left_order = xor_gather(white_by_window, "col", col_size)
    cos_lag, sin_lag = angle_table(LAGS, bin_count, out_length, -LH)
    lag_table = jnp.concatenate([cos_lag.T, sin_lag.T], axis=0).astype(jnp.bfloat16)
    group_rows = sum(piece.shape[1] for piece in left_by_window)
    piece_rows, visit_order = chip_gather(white_by_window, "row", row_size)
    visit_count = sum(piece.shape[1] for piece in piece_rows)
    late_first = [(1, index) for index in range(len(piece_rows)) if index > 1 and index % 2 == 1]
    near = [(0, 0), (1, 0), (0, 1), (1, 1)][:2 + min(1, len(left_by_window) - 1) + min(1, len(piece_rows) - 1)]
    fetches = [(1, index) for index in range(len(piece_rows)) if index > 1 and index % 2 == 0]
    far = [(0, index) for index in range(2, len(left_by_window))]
    issue_order = [slot for slot in late_first + near[:2] + near[3:] + fetches[:1] + near[2:3] + fetches[1:] + far[::-1]]
    issue_order = sorted(set(issue_order), key=issue_order.index)
    assert len(issue_order) == len(left_by_window) + len(piece_rows)
    piece = block_size
    left_pos = jnp.arange(group_rows, dtype=jnp.int32)
    visit_pos = jnp.arange(visit_count, dtype=jnp.int32)
    if left_order is not None:
        left_pos = left_order[left_pos // piece] * piece + left_pos % piece
    if visit_order is not None:
        visit_pos = visit_order[visit_pos // piece] * piece + visit_pos % piece
    left_perm = (jnp.arange(group_rows)[None, :] == left_pos[:, None]).astype(jnp.bfloat16)
    visit_perm = (jnp.arange(visit_count)[None, :] == visit_pos[:, None]).astype(jnp.bfloat16)
    pair = pair_block(left_by_window, piece_rows, left_perm, visit_perm, lag_table, issue_order)
    pair = jnp.swapaxes(pair.reshape(visit_count, group_rows, LAGS), 0, 1)
    norm_scale = 1.0 / math.sqrt(white.shape[1] * bin_count)
    pair = pair * norm_scale
    lag_offset = jnp.abs(jnp.arange(LAGS, dtype=jnp.int32) - LH)
    keep_mask = lag_offset[None, :] <= lag_limit[:, None]
    tile_stack = jnp.where(keep_mask[:, None, :], pair, 0.0)
    return tile_stack[:, None]


def solution(mesh):
    placed = (P(("row", "col"), None, None), P(), P("row"))
    return jax.shard_map(
        on_device,
        mesh=mesh,
        in_specs=placed,
        out_specs=P("row", "col", None, None),
        check_vma=False,
    )
```

```python
import functools
import math

import jax
import jax.numpy as jnp
from jax import lax
from jax.experimental import pallas as pl
from jax.experimental.pallas import tpu as pltpu
from jax.sharding import PartitionSpec as P

DECIM = 2
LAGS = 128
BAND = 64
LH = 64


def angle_table(row_count, col_count, period, offset):
    row_ids = jnp.arange(row_count, dtype=jnp.int32)[:, None] + offset
    col_ids = jnp.arange(col_count, dtype=jnp.int32)[None, :]
    phase_int = jnp.mod(row_ids * col_ids, period)
    angles = phase_int.astype(jnp.float32) * (2.0 * math.pi / period)
    return (jnp.cos(angles), jnp.sin(angles))


def decimate(records, fir_taps):
    tap_count = fir_taps.shape[0]
    out_block = 128
    in_block = DECIM * out_block
    lead_dims = records.shape[:2]
    block_count = records.shape[2] // in_block
    blocks = records.reshape(lead_dims + (block_count, in_block))
    tails = blocks[:, :, :-1, in_block - tap_count :]
    tails = jnp.concatenate([jnp.zeros(lead_dims + (1, tap_count), records.dtype), tails], axis=2)
    tap_ids = jnp.arange(tap_count, dtype=jnp.int32)[:, None, None]
    in_ids = jnp.arange(in_block + tap_count, dtype=jnp.int32)[None, :, None]
    out_ids = jnp.arange(out_block, dtype=jnp.int32)[None, None, :]
    onehot = (in_ids == DECIM * out_ids + tap_count - tap_ids).astype(jnp.float32)
    band_matrix = jnp.einsum("k,kij->ij", fir_taps, onehot, precision=lax.Precision.HIGH)
    summed = jnp.einsum(
        "swbi,ij->swbj", blocks, band_matrix[tap_count:], precision=lax.Precision.HIGH
    ) + jnp.einsum("swbi,ij->swbj", tails, band_matrix[:tap_count], precision=lax.Precision.HIGH)
    return summed.reshape(lead_dims + (block_count * out_block,))


def spectrum(decimated):
    out_length = decimated.shape[-1]
    first_len = 64
    second_len = out_length // first_len
    lead_dims = decimated.shape[:-1]
    blocks = decimated.reshape(lead_dims + (first_len, second_len))
    cos_one, sin_one = angle_table(first_len, first_len, first_len, 0)
    real_z = jnp.einsum("bwnq,fn->bwfq", blocks, cos_one, precision=lax.Precision.HIGH)
    imag_z = -jnp.einsum("bwnq,fn->bwfq", blocks, sin_one, precision=lax.Precision.HIGH)
    cos_two, sin_two = angle_table(first_len, second_len, out_length, 0)
    real_t = real_z * cos_two + imag_z * sin_two
    imag_t = imag_z * cos_two - real_z * sin_two
    cos_three, sin_three = angle_table(second_len // 2, second_len, second_len, 0)
    real_x = jnp.einsum(
        "bwfq,gq->bwgf", real_t, cos_three, precision=lax.Precision.HIGH
    ) + jnp.einsum("bwfq,gq->bwgf", imag_t, sin_three, precision=lax.Precision.HIGH)
    imag_x = jnp.einsum(
        "bwfq,gq->bwgf", imag_t, cos_three, precision=lax.Precision.HIGH
    ) - jnp.einsum("bwfq,gq->bwgf", real_t, sin_three, precision=lax.Precision.HIGH)
    bin_count = out_length // 2
    return (real_x.reshape(lead_dims + (bin_count,)), imag_x.reshape(lead_dims + (bin_count,)))


def whiten(spec_real, spec_imag):
    lead_dims = spec_real.shape[:-1]
    bin_count = spec_real.shape[-1]
    banded = lead_dims + (bin_count // BAND, BAND)
    squares = (spec_real * spec_real + spec_imag * spec_imag).reshape(banded)
    band_power = jnp.mean(squares, axis=-1, keepdims=True)
    inverse = 1.0 / jnp.sqrt(band_power + 1e-06)
    white_real = (spec_real.reshape(banded) * inverse).reshape(spec_real.shape)
    white_imag = (spec_imag.reshape(banded) * inverse).reshape(spec_imag.shape)
    return jnp.concatenate([white_real, white_imag], axis=-1).astype(jnp.bfloat16)


def cross_kernel(slots, *refs):
    piece_refs = refs[:len(slots)]
    left_perm, visit_perm, table_ref, out_ref, left_f32, visit_f32, cross_ref = refs[len(slots):]
    left_refs = [ref for ref, slot in zip(piece_refs, slots) if slot[0] == 0]
    window_count, piece, width = left_refs[0].shape
    rows_left = left_f32.shape[1]
    bin_count = width // 2
    chunk = 512
    while chunk > 128 and chunk * rows_left > 8192:
        chunk //= 2
    chunks = bin_count // chunk
    group_rows = cross_ref.shape[0]
    group = group_rows // (piece * rows_left)
    visit_count = visit_f32.shape[1] // piece

    for ref, (kind, index) in zip(piece_refs, slots):
        target = left_f32 if kind == 0 else visit_f32
        target[:, index * piece:(index + 1) * piece, :] = ref[...].astype(jnp.float32)
    for window in range(window_count):
        for perm_ref, target in ((left_perm, left_f32), (visit_perm, visit_f32)):
            target[window] = jnp.dot(
                perm_ref[...], target[window].astype(jnp.bfloat16), preferred_element_type=jnp.float32
            )

    for first in range(0, visit_count, group):
        base = first * piece

        def one_chunk(step, carry):
            local = step // chunks
            partner = base + local
            off = pl.multiple_of((step % chunks) * chunk, chunk)
            acc_re = jnp.zeros((rows_left, chunk), jnp.float32)
            acc_im = jnp.zeros((rows_left, chunk), jnp.float32)
            for window in range(window_count):
                left_c = left_f32[window, :, pl.ds(off, chunk)]
                left_d = left_f32[window, :, pl.ds(off + bin_count, chunk)]
                vis_c = visit_f32[window, pl.ds(partner, 1), pl.ds(off, chunk)]
                vis_d = visit_f32[window, pl.ds(partner, 1), pl.ds(off + bin_count, chunk)]
                acc_re = acc_re + (left_c * vis_c + left_d * vis_d)
                acc_im = acc_im + (left_c * vis_d - left_d * vis_c)
            row = pl.multiple_of(local * rows_left, rows_left)
            cross_ref[pl.ds(row, rows_left), pl.ds(off, chunk)] = acc_re.astype(jnp.bfloat16)
            cross_ref[pl.ds(row, rows_left), pl.ds(off + bin_count, chunk)] = acc_im.astype(jnp.bfloat16)
            return carry

        lax.fori_loop(0, group * piece * chunks, one_chunk, 0)
        out_ref[base * rows_left:base * rows_left + group_rows, :] = jnp.dot(
            cross_ref[...], table_ref[...], preferred_element_type=jnp.float32
        )


def pair_block(left_pieces, visit_pieces, left_perm, visit_perm, lag_table, issue_order):
    window_count, piece, width = left_pieces[0].shape
    left_count = len(left_pieces)
    visit_count = len(visit_pieces)
    rows_left = left_count * piece
    visit_rows = visit_count * piece
    lag_count = lag_table.shape[1]
    group = max(1, min(visit_count, 256 // (piece * rows_left)))
    while visit_count % group:
        group -= 1
    flops = visit_rows * rows_left * width * (4 * window_count + 2 * lag_count)
    vmem = pltpu.VMEM
    return pl.pallas_call(
        functools.partial(cross_kernel, tuple(issue_order)),
        out_shape=jax.ShapeDtypeStruct((visit_rows * rows_left, lag_count), jnp.float32),
        in_specs=[pl.BlockSpec(memory_space=vmem)] * (left_count + visit_count + 3),
        out_specs=pl.BlockSpec(memory_space=vmem),
        scratch_shapes=[
            vmem((window_count, rows_left, width), jnp.float32),
            vmem((window_count, visit_rows, width), jnp.float32),
            vmem((group * piece * rows_left, width), jnp.bfloat16),
        ],
        compiler_params=pltpu.CompilerParams(vmem_limit_bytes=60 * 1024 * 1024),
        cost_estimate=pl.CostEstimate(
            flops=flops,
            transcendentals=0,
            bytes_accessed=2 * width * (window_count * (rows_left + visit_rows) + lag_count)
            + 4 * visit_rows * rows_left * lag_count,
        ),
    )(*[(left_pieces, visit_pieces)[kind][index] for kind, index in issue_order], left_perm, visit_perm, lag_table)


def xor_gather(block, axis_name, size):
    if size & (size - 1):
        return [lax.all_gather(block, axis_name, axis=1, tiled=True)], None
    pieces = [block]
    for step in range(1, size):
        pairs = [(source, source ^ step) for source in range(size)]
        pieces.append(lax.ppermute(block, axis_name, pairs))
    order = lax.axis_index(axis_name) ^ jnp.arange(size, dtype=jnp.int32)
    return pieces, order


def chip_gather(block, axis_name, size):
    if size < 4 or size & (size - 1):
        return xor_gather(block, axis_name, size)
    chips = size // 2
    fetched = []
    for step in range(1, chips):
        pairs = [(source, source ^ (2 * step)) for source in range(size)]
        fetched.append(lax.ppermute(block, axis_name, pairs))
    partner = [(source, source ^ 1) for source in range(size)]
    pieces = [block, lax.ppermute(block, axis_name, partner)]
    piece = block.shape[1]
    swapped = lax.ppermute(jnp.concatenate(fetched, axis=1), axis_name, partner)
    for step in range(1, chips):
        pieces.append(fetched[step - 1])
        pieces.append(swapped[:, (step - 1) * piece:step * piece, :])
    order = lax.axis_index(axis_name) ^ jnp.arange(size, dtype=jnp.int32)
    return pieces, order


def on_device(records, fir_taps, lag_limit):
    block_size = records.shape[0]
    decimated = decimate(records, fir_taps)
    out_length = decimated.shape[-1]
    bin_count = out_length // 2
    spec_real, spec_imag = spectrum(decimated)
    white = whiten(spec_real, spec_imag)
    white_by_window = jnp.moveaxis(white, 1, 0)
    col_size = lax.axis_size("col")
    row_size = lax.axis_size("row")
    left_by_window, left_order = xor_gather(white_by_window, "col", col_size)
    cos_lag, sin_lag = angle_table(LAGS, bin_count, out_length, -LH)
    lag_table = jnp.concatenate([cos_lag.T, sin_lag.T], axis=0).astype(jnp.bfloat16)
    group_rows = sum(piece.shape[1] for piece in left_by_window)
    piece_rows, visit_order = chip_gather(white_by_window, "row", row_size)
    visit_count = sum(piece.shape[1] for piece in piece_rows)
    late_first = [(1, index) for index in range(len(piece_rows)) if index > 1 and index % 2 == 1]
    near = [(0, 0), (1, 0), (0, 1), (1, 1)][:2 + min(1, len(left_by_window) - 1) + min(1, len(piece_rows) - 1)]
    fetches = [(1, index) for index in range(len(piece_rows)) if index > 1 and index % 2 == 0]
    far = [(0, index) for index in range(2, len(left_by_window))]
    issue_order = [slot for slot in late_first + near[:2] + near[3:] + fetches[:1] + near[2:3] + fetches[1:] + far[::-1]]
    issue_order = sorted(set(issue_order), key=issue_order.index)
    assert len(issue_order) == len(left_by_window) + len(piece_rows)
    piece = block_size
    left_pos = jnp.arange(group_rows, dtype=jnp.int32)
    visit_pos = jnp.arange(visit_count, dtype=jnp.int32)
    if left_order is not None:
        left_pos = left_order[left_pos // piece] * piece + left_pos % piece
    if visit_order is not None:
        visit_pos = visit_order[visit_pos // piece] * piece + visit_pos % piece
    left_perm = (jnp.arange(group_rows)[None, :] == left_pos[:, None]).astype(jnp.bfloat16)
    visit_perm = (jnp.arange(visit_count)[None, :] == visit_pos[:, None]).astype(jnp.bfloat16)
    pair = pair_block(left_by_window, piece_rows, left_perm, visit_perm, lag_table, issue_order)
    pair = jnp.swapaxes(pair.reshape(visit_count, group_rows, LAGS), 0, 1)
    norm_scale = 1.0 / math.sqrt(white.shape[1] * bin_count)
    pair = pair * norm_scale
    lag_offset = jnp.abs(jnp.arange(LAGS, dtype=jnp.int32) - LH)
    keep_mask = lag_offset[None, :] <= lag_limit[:, None]
    tile_stack = jnp.where(keep_mask[:, None, :], pair, 0.0)
    return tile_stack[:, None]


def solution(mesh):
    placed = (P(("row", "col"), None, None), P(), P("row"))
    return jax.shard_map(
        on_device,
        mesh=mesh,
        in_specs=placed,
        out_specs=P("row", "col", None, None),
        check_vma=False,
    )
```

```python
import functools
import math

import jax
import jax.numpy as jnp
from jax import lax
from jax.experimental import pallas as pl
from jax.experimental.pallas import tpu as pltpu
from jax.sharding import PartitionSpec as P

DECIM = 2
LAGS = 128
BAND = 64
LH = 64


def angle_table(row_count, col_count, period, offset):
    row_ids = jnp.arange(row_count, dtype=jnp.int32)[:, None] + offset
    col_ids = jnp.arange(col_count, dtype=jnp.int32)[None, :]
    phase_int = jnp.mod(row_ids * col_ids, period)
    angles = phase_int.astype(jnp.float32) * (2.0 * math.pi / period)
    return (jnp.cos(angles), jnp.sin(angles))


def decimate(records, fir_taps):
    tap_count = fir_taps.shape[0]
    out_block = 128
    in_block = DECIM * out_block
    lead_dims = records.shape[:2]
    block_count = records.shape[2] // in_block
    blocks = records.reshape(lead_dims + (block_count, in_block))
    tails = blocks[:, :, :-1, in_block - tap_count :]
    tails = jnp.concatenate([jnp.zeros(lead_dims + (1, tap_count), records.dtype), tails], axis=2)
    in_ids = jnp.arange(in_block + tap_count, dtype=jnp.int32)[:, None]
    out_ids = jnp.arange(out_block, dtype=jnp.int32)[None, :]
    tap_index = DECIM * out_ids + tap_count - in_ids
    band_matrix = jnp.zeros(tap_index.shape, jnp.float32)
    for tap in range(tap_count):
        band_matrix = jnp.where(tap_index == tap, fir_taps[tap], band_matrix)
    summed = jnp.einsum(
        "swbi,ij->swbj", blocks, band_matrix[tap_count:], precision=lax.Precision.HIGH
    ) + jnp.einsum("swbi,ij->swbj", tails, band_matrix[:tap_count], precision=lax.Precision.HIGH)
    return summed.reshape(lead_dims + (block_count * out_block,))


def spectrum(decimated):
    out_length = decimated.shape[-1]
    first_len = 64
    second_len = out_length // first_len
    lead_dims = decimated.shape[:-1]
    blocks = decimated.reshape(lead_dims + (first_len, second_len))
    cos_one, sin_one = angle_table(first_len, first_len, first_len, 0)
    real_z = jnp.einsum("bwnq,fn->bwfq", blocks, cos_one, precision=lax.Precision.HIGH)
    imag_z = -jnp.einsum("bwnq,fn->bwfq", blocks, sin_one, precision=lax.Precision.HIGH)
    cos_two, sin_two = angle_table(first_len, second_len, out_length, 0)
    real_t = real_z * cos_two + imag_z * sin_two
    imag_t = imag_z * cos_two - real_z * sin_two
    cos_three, sin_three = angle_table(second_len // 2, second_len, second_len, 0)
    real_x = jnp.einsum(
        "bwfq,gq->bwgf", real_t, cos_three, precision=lax.Precision.HIGH
    ) + jnp.einsum("bwfq,gq->bwgf", imag_t, sin_three, precision=lax.Precision.HIGH)
    imag_x = jnp.einsum(
        "bwfq,gq->bwgf", imag_t, cos_three, precision=lax.Precision.HIGH
    ) - jnp.einsum("bwfq,gq->bwgf", real_t, sin_three, precision=lax.Precision.HIGH)
    bin_count = out_length // 2
    return (real_x.reshape(lead_dims + (bin_count,)), imag_x.reshape(lead_dims + (bin_count,)))


def whiten(spec_real, spec_imag):
    lead_dims = spec_real.shape[:-1]
    bin_count = spec_real.shape[-1]
    banded = lead_dims + (bin_count // BAND, BAND)
    squares = (spec_real * spec_real + spec_imag * spec_imag).reshape(banded)
    band_power = jnp.mean(squares, axis=-1, keepdims=True)
    inverse = 1.0 / jnp.sqrt(band_power + 1e-06)
    white_real = (spec_real.reshape(banded) * inverse).reshape(spec_real.shape)
    white_imag = (spec_imag.reshape(banded) * inverse).reshape(spec_imag.shape)
    return jnp.concatenate([white_real, white_imag], axis=-1).astype(jnp.bfloat16)


def cross_kernel(slots, *refs):
    piece_refs = refs[:len(slots)]
    left_perm, visit_perm, table_ref, out_ref, left_f32, visit_f32, cross_ref = refs[len(slots):]
    left_refs = [ref for ref, slot in zip(piece_refs, slots) if slot[0] == 0]
    window_count, piece, width = left_refs[0].shape
    rows_left = left_f32.shape[1]
    bin_count = width // 2
    chunk = 512
    while chunk > 128 and chunk * rows_left > 8192:
        chunk //= 2
    chunks = bin_count // chunk
    group_rows = cross_ref.shape[0]
    group = group_rows // (piece * rows_left)
    visit_count = visit_f32.shape[1] // piece

    for ref, (kind, index) in zip(piece_refs, slots):
        target = left_f32 if kind == 0 else visit_f32
        target[:, index * piece:(index + 1) * piece, :] = ref[...].astype(jnp.float32)
    for window in range(window_count):
        for perm_ref, target in ((left_perm, left_f32), (visit_perm, visit_f32)):
            target[window] = jnp.dot(
                perm_ref[...], target[window].astype(jnp.bfloat16), preferred_element_type=jnp.float32
            )

    for first in range(0, visit_count, group):
        base = first * piece

        def one_chunk(step, carry):
            local = step // chunks
            partner = base + local
            off = pl.multiple_of((step % chunks) * chunk, chunk)
            acc_re = jnp.zeros((rows_left, chunk), jnp.float32)
            acc_im = jnp.zeros((rows_left, chunk), jnp.float32)
            for window in range(window_count):
                left_c = left_f32[window, :, pl.ds(off, chunk)]
                left_d = left_f32[window, :, pl.ds(off + bin_count, chunk)]
                vis_c = visit_f32[window, pl.ds(partner, 1), pl.ds(off, chunk)]
                vis_d = visit_f32[window, pl.ds(partner, 1), pl.ds(off + bin_count, chunk)]
                acc_re = acc_re + (left_c * vis_c + left_d * vis_d)
                acc_im = acc_im + (left_c * vis_d - left_d * vis_c)
            row = pl.multiple_of(local * rows_left, rows_left)
            cross_ref[pl.ds(row, rows_left), pl.ds(off, chunk)] = acc_re.astype(jnp.bfloat16)
            cross_ref[pl.ds(row, rows_left), pl.ds(off + bin_count, chunk)] = acc_im.astype(jnp.bfloat16)
            return carry

        lax.fori_loop(0, group * piece * chunks, one_chunk, 0)
        out_ref[base * rows_left:base * rows_left + group_rows, :] = jnp.dot(
            cross_ref[...], table_ref[...], preferred_element_type=jnp.float32
        )


def pair_block(left_pieces, visit_pieces, left_perm, visit_perm, lag_table, issue_order):
    window_count, piece, width = left_pieces[0].shape
    left_count = len(left_pieces)
    visit_count = len(visit_pieces)
    rows_left = left_count * piece
    visit_rows = visit_count * piece
    lag_count = lag_table.shape[1]
    group = max(1, min(visit_count, 256 // (piece * rows_left)))
    while visit_count % group:
        group -= 1
    flops = visit_rows * rows_left * width * (4 * window_count + 2 * lag_count)
    vmem = pltpu.VMEM
    return pl.pallas_call(
        functools.partial(cross_kernel, tuple(issue_order)),
        out_shape=jax.ShapeDtypeStruct((visit_rows * rows_left, lag_count), jnp.float32),
        in_specs=[pl.BlockSpec(memory_space=vmem)] * (left_count + visit_count + 3),
        out_specs=pl.BlockSpec(memory_space=vmem),
        scratch_shapes=[
            vmem((window_count, rows_left, width), jnp.float32),
            vmem((window_count, visit_rows, width), jnp.float32),
            vmem((group * piece * rows_left, width), jnp.bfloat16),
        ],
        compiler_params=pltpu.CompilerParams(vmem_limit_bytes=60 * 1024 * 1024),
        cost_estimate=pl.CostEstimate(
            flops=flops,
            transcendentals=0,
            bytes_accessed=2 * width * (window_count * (rows_left + visit_rows) + lag_count)
            + 4 * visit_rows * rows_left * lag_count,
        ),
    )(*[(left_pieces, visit_pieces)[kind][index] for kind, index in issue_order], left_perm, visit_perm, lag_table)


def xor_gather(block, axis_name, size):
    if size & (size - 1):
        return [lax.all_gather(block, axis_name, axis=1, tiled=True)], None
    pieces = [block]
    for step in range(1, size):
        pairs = [(source, source ^ step) for source in range(size)]
        pieces.append(lax.ppermute(block, axis_name, pairs))
    order = lax.axis_index(axis_name) ^ jnp.arange(size, dtype=jnp.int32)
    return pieces, order


def chip_gather(block, axis_name, size):
    if size < 4 or size & (size - 1):
        return xor_gather(block, axis_name, size)
    chips = size // 2
    fetched = []
    for step in range(1, chips):
        pairs = [(source, source ^ (2 * step)) for source in range(size)]
        fetched.append(lax.ppermute(block, axis_name, pairs))
    partner = [(source, source ^ 1) for source in range(size)]
    pieces = [block, lax.ppermute(block, axis_name, partner)]
    piece = block.shape[1]
    swapped = lax.ppermute(jnp.concatenate(fetched, axis=1), axis_name, partner)
    for step in range(1, chips):
        pieces.append(fetched[step - 1])
        pieces.append(swapped[:, (step - 1) * piece:step * piece, :])
    order = lax.axis_index(axis_name) ^ jnp.arange(size, dtype=jnp.int32)
    return pieces, order


def on_device(records, fir_taps, lag_limit):
    block_size = records.shape[0]
    decimated = decimate(records, fir_taps)
    out_length = decimated.shape[-1]
    bin_count = out_length // 2
    spec_real, spec_imag = spectrum(decimated)
    white = whiten(spec_real, spec_imag)
    white_by_window = jnp.moveaxis(white, 1, 0)
    col_size = lax.axis_size("col")
    row_size = lax.axis_size("row")
    left_by_window, left_order = xor_gather(white_by_window, "col", col_size)
    cos_lag, sin_lag = angle_table(LAGS, bin_count, out_length, -LH)
    lag_table = jnp.concatenate([cos_lag.T, sin_lag.T], axis=0).astype(jnp.bfloat16)
    group_rows = sum(piece.shape[1] for piece in left_by_window)
    piece_rows, visit_order = chip_gather(white_by_window, "row", row_size)
    visit_count = sum(piece.shape[1] for piece in piece_rows)
    late_first = [(1, index) for index in range(len(piece_rows)) if index > 1 and index % 2 == 1]
    near = [(0, 0), (1, 0), (0, 1), (1, 1)][:2 + min(1, len(left_by_window) - 1) + min(1, len(piece_rows) - 1)]
    fetches = [(1, index) for index in range(len(piece_rows)) if index > 1 and index % 2 == 0]
    far = [(0, index) for index in range(2, len(left_by_window))]
    issue_order = [slot for slot in late_first + near[:2] + near[3:] + fetches[:1] + near[2:3] + fetches[1:] + far[::-1]]
    issue_order = sorted(set(issue_order), key=issue_order.index)[::-1]
    assert len(issue_order) == len(left_by_window) + len(piece_rows)
    piece = block_size
    left_pos = jnp.arange(group_rows, dtype=jnp.int32)
    visit_pos = jnp.arange(visit_count, dtype=jnp.int32)
    if left_order is not None:
        left_pos = left_order[left_pos // piece] * piece + left_pos % piece
    if visit_order is not None:
        visit_pos = visit_order[visit_pos // piece] * piece + visit_pos % piece
    left_perm = (jnp.arange(group_rows)[None, :] == left_pos[:, None]).astype(jnp.bfloat16)
    visit_perm = (jnp.arange(visit_count)[None, :] == visit_pos[:, None]).astype(jnp.bfloat16)
    pair = pair_block(left_by_window, piece_rows, left_perm, visit_perm, lag_table, issue_order)
    pair = jnp.swapaxes(pair.reshape(visit_count, group_rows, LAGS), 0, 1)
    norm_scale = 1.0 / math.sqrt(white.shape[1] * bin_count)
    pair = pair * norm_scale
    lag_offset = jnp.abs(jnp.arange(LAGS, dtype=jnp.int32) - LH)
    keep_mask = lag_offset[None, :] <= lag_limit[:, None]
    tile_stack = jnp.where(keep_mask[:, None, :], pair, 0.0)
    return tile_stack[:, None]


def solution(mesh):
    placed = (P(("row", "col"), None, None), P(), P("row"))
    return jax.shard_map(
        on_device,
        mesh=mesh,
        in_specs=placed,
        out_specs=P("row", "col", None, None),
        check_vma=False,
    )
```

```python
import functools
import math

import jax
import jax.numpy as jnp
from jax import lax
from jax.experimental import pallas as pl
from jax.experimental.pallas import tpu as pltpu
from jax.sharding import PartitionSpec as P

DECIM = 2
LAGS = 128
BAND = 64
LH = 64


def angle_table(row_count, col_count, period, offset):
    row_ids = jnp.arange(row_count, dtype=jnp.int32)[:, None] + offset
    col_ids = jnp.arange(col_count, dtype=jnp.int32)[None, :]
    phase_int = jnp.mod(row_ids * col_ids, period)
    angles = phase_int.astype(jnp.float32) * (2.0 * math.pi / period)
    return (jnp.cos(angles), jnp.sin(angles))


def decimate(records, fir_taps):
    tap_count = fir_taps.shape[0]
    out_block = 128
    in_block = DECIM * out_block
    lead_dims = records.shape[:2]
    block_count = records.shape[2] // in_block
    blocks = records.reshape(lead_dims + (block_count, in_block))
    tails = blocks[:, :, :-1, in_block - tap_count :]
    tails = jnp.concatenate([jnp.zeros(lead_dims + (1, tap_count), records.dtype), tails], axis=2)
    tap_ids = jnp.arange(tap_count, dtype=jnp.int32)[:, None, None]
    in_ids = jnp.arange(in_block + tap_count, dtype=jnp.int32)[None, :, None]
    out_ids = jnp.arange(out_block, dtype=jnp.int32)[None, None, :]
    onehot = (in_ids == DECIM * out_ids + tap_count - tap_ids).astype(jnp.float32)
    band_matrix = jnp.einsum("k,kij->ij", fir_taps, onehot, precision=lax.Precision.HIGH)
    summed = jnp.einsum(
        "swbi,ij->swbj", blocks, band_matrix[tap_count:], precision=lax.Precision.HIGH
    ) + jnp.einsum("swbi,ij->swbj", tails, band_matrix[:tap_count], precision=lax.Precision.HIGH)
    return summed.reshape(lead_dims + (block_count * out_block,))


def spectrum(decimated):
    out_length = decimated.shape[-1]
    first_len = 64
    second_len = out_length // first_len
    lead_dims = decimated.shape[:-1]
    blocks = decimated.reshape(lead_dims + (first_len, second_len))
    cos_one, sin_one = angle_table(first_len, first_len, first_len, 0)
    real_z = jnp.einsum("bwnq,fn->bwfq", blocks, cos_one, precision=lax.Precision.HIGH)
    imag_z = -jnp.einsum("bwnq,fn->bwfq", blocks, sin_one, precision=lax.Precision.HIGH)
    cos_two, sin_two = angle_table(first_len, second_len, out_length, 0)
    real_t = real_z * cos_two + imag_z * sin_two
    imag_t = imag_z * cos_two - real_z * sin_two
    cos_three, sin_three = angle_table(second_len // 2, second_len, second_len, 0)
    real_x = jnp.einsum(
        "bwfq,gq->bwgf", real_t, cos_three, precision=lax.Precision.HIGH
    ) + jnp.einsum("bwfq,gq->bwgf", imag_t, sin_three, precision=lax.Precision.HIGH)
    imag_x = jnp.einsum(
        "bwfq,gq->bwgf", imag_t, cos_three, precision=lax.Precision.HIGH
    ) - jnp.einsum("bwfq,gq->bwgf", real_t, sin_three, precision=lax.Precision.HIGH)
    bin_count = out_length // 2
    return (real_x.reshape(lead_dims + (bin_count,)), imag_x.reshape(lead_dims + (bin_count,)))


def whiten(spec_real, spec_imag):
    lead_dims = spec_real.shape[:-1]
    bin_count = spec_real.shape[-1]
    banded = lead_dims + (bin_count // BAND, BAND)
    squares = (spec_real * spec_real + spec_imag * spec_imag).reshape(banded)
    band_power = jnp.mean(squares, axis=-1, keepdims=True)
    inverse = 1.0 / jnp.sqrt(band_power + 1e-06)
    white_real = (spec_real.reshape(banded) * inverse).reshape(spec_real.shape)
    white_imag = (spec_imag.reshape(banded) * inverse).reshape(spec_imag.shape)
    return jnp.concatenate([white_real, white_imag], axis=-1).astype(jnp.bfloat16)


def cross_kernel(slots, *refs):
    piece_refs = refs[:len(slots)]
    left_perm, visit_perm, table_ref, out_ref, left_f32, visit_f32, cross_ref = refs[len(slots):]
    left_refs = [ref for ref, slot in zip(piece_refs, slots) if slot[0] == 0]
    window_count, piece, width = left_refs[0].shape
    rows_left = left_f32.shape[1]
    bin_count = width // 2
    chunk = 512
    while chunk > 128 and chunk * rows_left > 8192:
        chunk //= 2
    chunks = bin_count // chunk
    group_rows = cross_ref.shape[0]
    group = group_rows // (piece * rows_left)
    visit_count = visit_f32.shape[1] // piece

    for ref, (kind, index) in zip(piece_refs, slots):
        target = left_f32 if kind == 0 else visit_f32
        target[:, index * piece:(index + 1) * piece, :] = ref[...].astype(jnp.float32)
    for window in range(window_count):
        for perm_ref, target in ((left_perm, left_f32), (visit_perm, visit_f32)):
            target[window] = jnp.dot(
                perm_ref[...], target[window].astype(jnp.bfloat16), preferred_element_type=jnp.float32
            )

    for first in range(0, visit_count, group):
        base = first * piece

        def one_chunk(step, carry):
            local = step // chunks
            partner = base + local
            off = pl.multiple_of((step % chunks) * chunk, chunk)
            acc_re = jnp.zeros((rows_left, chunk), jnp.float32)
            acc_im = jnp.zeros((rows_left, chunk), jnp.float32)
            for window in range(window_count):
                left_c = left_f32[window, :, pl.ds(off, chunk)]
                left_d = left_f32[window, :, pl.ds(off + bin_count, chunk)]
                vis_c = visit_f32[window, pl.ds(partner, 1), pl.ds(off, chunk)]
                vis_d = visit_f32[window, pl.ds(partner, 1), pl.ds(off + bin_count, chunk)]
                acc_re = acc_re + (left_c * vis_c + left_d * vis_d)
                acc_im = acc_im + (left_c * vis_d - left_d * vis_c)
            row = pl.multiple_of(local * rows_left, rows_left)
            cross_ref[pl.ds(row, rows_left), pl.ds(off, chunk)] = acc_re.astype(jnp.bfloat16)
            cross_ref[pl.ds(row, rows_left), pl.ds(off + bin_count, chunk)] = acc_im.astype(jnp.bfloat16)
            return carry

        lax.fori_loop(0, group * piece * chunks, one_chunk, 0)
        out_ref[base * rows_left:base * rows_left + group_rows, :] = jnp.dot(
            cross_ref[...], table_ref[...], preferred_element_type=jnp.float32
        )


def pair_block(left_pieces, visit_pieces, left_perm, visit_perm, lag_table, issue_order):
    window_count, piece, width = left_pieces[0].shape
    left_count = len(left_pieces)
    visit_count = len(visit_pieces)
    rows_left = left_count * piece
    visit_rows = visit_count * piece
    lag_count = lag_table.shape[1]
    group = max(1, min(visit_count, 512 // (piece * rows_left)))
    while visit_count % group:
        group -= 1
    flops = visit_rows * rows_left * width * (4 * window_count + 2 * lag_count)
    vmem = pltpu.VMEM
    return pl.pallas_call(
        functools.partial(cross_kernel, tuple(issue_order)),
        out_shape=jax.ShapeDtypeStruct((visit_rows * rows_left, lag_count), jnp.float32),
        in_specs=[pl.BlockSpec(memory_space=vmem)] * (left_count + visit_count + 3),
        out_specs=pl.BlockSpec(memory_space=vmem),
        scratch_shapes=[
            vmem((window_count, rows_left, width), jnp.float32),
            vmem((window_count, visit_rows, width), jnp.float32),
            vmem((group * piece * rows_left, width), jnp.bfloat16),
        ],
        compiler_params=pltpu.CompilerParams(vmem_limit_bytes=60 * 1024 * 1024),
        cost_estimate=pl.CostEstimate(
            flops=flops,
            transcendentals=0,
            bytes_accessed=2 * width * (window_count * (rows_left + visit_rows) + lag_count)
            + 4 * visit_rows * rows_left * lag_count,
        ),
    )(*[(left_pieces, visit_pieces)[kind][index] for kind, index in issue_order], left_perm, visit_perm, lag_table)


def xor_gather(block, axis_name, size):
    if size & (size - 1):
        return [lax.all_gather(block, axis_name, axis=1, tiled=True)], None
    pieces = [block]
    for step in range(1, size):
        pairs = [(source, source ^ step) for source in range(size)]
        pieces.append(lax.ppermute(block, axis_name, pairs))
    order = lax.axis_index(axis_name) ^ jnp.arange(size, dtype=jnp.int32)
    return pieces, order


def chip_gather(block, axis_name, size):
    if size < 4 or size & (size - 1):
        return xor_gather(block, axis_name, size)
    chips = size // 2
    fetched = []
    for step in range(1, chips):
        pairs = [(source, source ^ (2 * step)) for source in range(size)]
        fetched.append(lax.ppermute(block, axis_name, pairs))
    partner = [(source, source ^ 1) for source in range(size)]
    pieces = [block, lax.ppermute(block, axis_name, partner)]
    piece = block.shape[1]
    swapped = lax.ppermute(jnp.concatenate(fetched, axis=1), axis_name, partner)
    for step in range(1, chips):
        pieces.append(fetched[step - 1])
        pieces.append(swapped[:, (step - 1) * piece:step * piece, :])
    order = lax.axis_index(axis_name) ^ jnp.arange(size, dtype=jnp.int32)
    return pieces, order


def on_device(records, fir_taps, lag_limit):
    block_size = records.shape[0]
    decimated = decimate(records, fir_taps)
    out_length = decimated.shape[-1]
    bin_count = out_length // 2
    spec_real, spec_imag = spectrum(decimated)
    white = whiten(spec_real, spec_imag)
    white_by_window = jnp.moveaxis(white, 1, 0)
    col_size = lax.axis_size("col")
    row_size = lax.axis_size("row")
    left_by_window, left_order = xor_gather(white_by_window, "col", col_size)
    cos_lag, sin_lag = angle_table(LAGS, bin_count, out_length, -LH)
    lag_table = jnp.concatenate([cos_lag.T, sin_lag.T], axis=0).astype(jnp.bfloat16)
    group_rows = sum(piece.shape[1] for piece in left_by_window)
    piece_rows, visit_order = chip_gather(white_by_window, "row", row_size)
    visit_count = sum(piece.shape[1] for piece in piece_rows)
    late_first = [(1, index) for index in range(len(piece_rows)) if index > 1 and index % 2 == 1]
    near = [(0, 0), (1, 0), (0, 1), (1, 1)][:2 + min(1, len(left_by_window) - 1) + min(1, len(piece_rows) - 1)]
    fetches = [(1, index) for index in range(len(piece_rows)) if index > 1 and index % 2 == 0]
    far = [(0, index) for index in range(2, len(left_by_window))]
    issue_order = [slot for slot in late_first + near[:2] + near[3:] + fetches[:1] + near[2:3] + fetches[1:] + far[::-1]]
    issue_order = sorted(set(issue_order), key=issue_order.index)
    assert len(issue_order) == len(left_by_window) + len(piece_rows)
    piece = block_size
    left_pos = jnp.arange(group_rows, dtype=jnp.int32)
    visit_pos = jnp.arange(visit_count, dtype=jnp.int32)
    if left_order is not None:
        left_pos = left_order[left_pos // piece] * piece + left_pos % piece
    if visit_order is not None:
        visit_pos = visit_order[visit_pos // piece] * piece + visit_pos % piece
    left_perm = (jnp.arange(group_rows)[None, :] == left_pos[:, None]).astype(jnp.bfloat16)
    visit_perm = (jnp.arange(visit_count)[None, :] == visit_pos[:, None]).astype(jnp.bfloat16)
    pair = pair_block(left_by_window, piece_rows, left_perm, visit_perm, lag_table, issue_order)
    pair = jnp.swapaxes(pair.reshape(visit_count, group_rows, LAGS), 0, 1)
    norm_scale = 1.0 / math.sqrt(white.shape[1] * bin_count)
    pair = pair * norm_scale
    lag_offset = jnp.abs(jnp.arange(LAGS, dtype=jnp.int32) - LH)
    keep_mask = lag_offset[None, :] <= lag_limit[:, None]
    tile_stack = jnp.where(keep_mask[:, None, :], pair, 0.0)
    return tile_stack[:, None]


def solution(mesh):
    placed = (P(("row", "col"), None, None), P(), P("row"))
    return jax.shard_map(
        on_device,
        mesh=mesh,
        in_specs=placed,
        out_specs=P("row", "col", None, None),
        check_vma=False,
    )
```

```python
import functools
import math

import jax
import jax.numpy as jnp
from jax import lax
from jax.experimental import pallas as pl
from jax.experimental.pallas import tpu as pltpu
from jax.sharding import PartitionSpec as P

DECIM = 2
LAGS = 128
BAND = 64
LH = 64


def angle_table(row_count, col_count, period, offset):
    row_ids = jnp.arange(row_count, dtype=jnp.int32)[:, None] + offset
    col_ids = jnp.arange(col_count, dtype=jnp.int32)[None, :]
    phase_int = jnp.mod(row_ids * col_ids, period)
    angles = phase_int.astype(jnp.float32) * (2.0 * math.pi / period)
    return (jnp.cos(angles), jnp.sin(angles))


def decimate(records, fir_taps):
    tap_count = fir_taps.shape[0]
    out_block = 128
    in_block = DECIM * out_block
    lead_dims = records.shape[:2]
    block_count = records.shape[2] // in_block
    blocks = records.reshape(lead_dims + (block_count, in_block))
    tails = blocks[:, :, :-1, in_block - tap_count :]
    tails = jnp.concatenate([jnp.zeros(lead_dims + (1, tap_count), records.dtype), tails], axis=2)
    tap_ids = jnp.arange(tap_count, dtype=jnp.int32)[:, None, None]
    in_ids = jnp.arange(in_block + tap_count, dtype=jnp.int32)[None, :, None]
    out_ids = jnp.arange(out_block, dtype=jnp.int32)[None, None, :]
    onehot = (in_ids == DECIM * out_ids + tap_count - tap_ids).astype(jnp.float32)
    band_matrix = jnp.einsum("k,kij->ij", fir_taps, onehot, precision=lax.Precision.HIGH)
    summed = jnp.einsum(
        "swbi,ij->swbj", blocks, band_matrix[tap_count:], precision=lax.Precision.HIGH
    ) + jnp.einsum("swbi,ij->swbj", tails, band_matrix[:tap_count], precision=lax.Precision.HIGH)
    return summed.reshape(lead_dims + (block_count * out_block,))


def spectrum(decimated):
    out_length = decimated.shape[-1]
    first_len = 64
    second_len = out_length // first_len
    lead_dims = decimated.shape[:-1]
    blocks = decimated.reshape(lead_dims + (first_len, second_len))
    cos_one, sin_one = angle_table(first_len, first_len, first_len, 0)
    real_z = jnp.einsum("bwnq,fn->bwfq", blocks, cos_one, precision=lax.Precision.HIGH)
    imag_z = -jnp.einsum("bwnq,fn->bwfq", blocks, sin_one, precision=lax.Precision.HIGH)
    cos_two, sin_two = angle_table(first_len, second_len, out_length, 0)
    real_t = real_z * cos_two + imag_z * sin_two
    imag_t = imag_z * cos_two - real_z * sin_two
    cos_three, sin_three = angle_table(second_len // 2, second_len, second_len, 0)
    real_x = jnp.einsum(
        "bwfq,gq->bwgf", real_t, cos_three, precision=lax.Precision.HIGH
    ) + jnp.einsum("bwfq,gq->bwgf", imag_t, sin_three, precision=lax.Precision.HIGH)
    imag_x = jnp.einsum(
        "bwfq,gq->bwgf", imag_t, cos_three, precision=lax.Precision.HIGH
    ) - jnp.einsum("bwfq,gq->bwgf", real_t, sin_three, precision=lax.Precision.HIGH)
    bin_count = out_length // 2
    return (real_x.reshape(lead_dims + (bin_count,)), imag_x.reshape(lead_dims + (bin_count,)))


def whiten(spec_real, spec_imag):
    lead_dims = spec_real.shape[:-1]
    bin_count = spec_real.shape[-1]
    banded = lead_dims + (bin_count // BAND, BAND)
    squares = (spec_real * spec_real + spec_imag * spec_imag).reshape(banded)
    band_power = jnp.mean(squares, axis=-1, keepdims=True)
    inverse = 1.0 / jnp.sqrt(band_power + 1e-06)
    white_real = (spec_real.reshape(banded) * inverse).reshape(spec_real.shape)
    white_imag = (spec_imag.reshape(banded) * inverse).reshape(spec_imag.shape)
    return jnp.concatenate([white_real, white_imag], axis=-1).astype(jnp.bfloat16)


def cross_kernel(slots, *refs):
    piece_refs = refs[:len(slots)]
    left_perm, visit_perm, table_ref, out_ref, left_f32, visit_f32, cross_ref = refs[len(slots):]
    left_refs = [ref for ref, slot in zip(piece_refs, slots) if slot[0] == 0]
    window_count, piece, width = left_refs[0].shape
    rows_left = left_f32.shape[1]
    bin_count = width // 2
    chunk = 512
    while chunk > 128 and chunk * rows_left > 8192:
        chunk //= 2
    chunks = bin_count // chunk
    group_rows = cross_ref.shape[0]
    group = group_rows // (piece * rows_left)
    visit_count = visit_f32.shape[1] // piece

    for ref, (kind, index) in zip(piece_refs, slots):
        target = left_f32 if kind == 0 else visit_f32
        target[:, index * piece:(index + 1) * piece, :] = ref[...].astype(jnp.float32)
    for window in range(window_count):
        for perm_ref, target in ((left_perm, left_f32), (visit_perm, visit_f32)):
            target[window] = jnp.dot(
                perm_ref[...], target[window].astype(jnp.bfloat16), preferred_element_type=jnp.float32
            )

    for first in range(0, visit_count, group):
        base = first * piece

        def one_chunk(step, carry):
            local = step // chunks
            partner = base + local
            off = pl.multiple_of((step % chunks) * chunk, chunk)
            acc_re = jnp.zeros((rows_left, chunk), jnp.float32)
            acc_im = jnp.zeros((rows_left, chunk), jnp.float32)
            for window in range(window_count):
                left_c = left_f32[window, :, pl.ds(off, chunk)]
                left_d = left_f32[window, :, pl.ds(off + bin_count, chunk)]
                vis_c = visit_f32[window, pl.ds(partner, 1), pl.ds(off, chunk)]
                vis_d = visit_f32[window, pl.ds(partner, 1), pl.ds(off + bin_count, chunk)]
                acc_re = acc_re + (left_c * vis_c + left_d * vis_d)
                acc_im = acc_im + (left_c * vis_d - left_d * vis_c)
            row = pl.multiple_of(local * rows_left, rows_left)
            cross_ref[pl.ds(row, rows_left), pl.ds(off, chunk)] = acc_re.astype(jnp.bfloat16)
            cross_ref[pl.ds(row, rows_left), pl.ds(off + bin_count, chunk)] = acc_im.astype(jnp.bfloat16)
            return carry

        lax.fori_loop(0, group * piece * chunks, one_chunk, 0)
        out_ref[base * rows_left:base * rows_left + group_rows, :] = jnp.dot(
            cross_ref[...], table_ref[...], preferred_element_type=jnp.float32
        )


def pair_block(left_pieces, visit_pieces, left_perm, visit_perm, lag_table, issue_order):
    window_count, piece, width = left_pieces[0].shape
    left_count = len(left_pieces)
    visit_count = len(visit_pieces)
    rows_left = left_count * piece
    visit_rows = visit_count * piece
    lag_count = lag_table.shape[1]
    group = max(1, min(visit_count, 512 // (piece * rows_left)))
    while visit_count % group:
        group -= 1
    flops = visit_rows * rows_left * width * (4 * window_count + 2 * lag_count)
    vmem = pltpu.VMEM
    return pl.pallas_call(
        functools.partial(cross_kernel, tuple(issue_order)),
        out_shape=jax.ShapeDtypeStruct((visit_rows * rows_left, lag_count), jnp.float32),
        in_specs=[pl.BlockSpec(memory_space=vmem)] * (left_count + visit_count + 3),
        out_specs=pl.BlockSpec(memory_space=vmem),
        scratch_shapes=[
            vmem((window_count, rows_left, width), jnp.float32),
            vmem((window_count, visit_rows, width), jnp.float32),
            vmem((group * piece * rows_left, width), jnp.bfloat16),
        ],
        compiler_params=pltpu.CompilerParams(vmem_limit_bytes=60 * 1024 * 1024),
        cost_estimate=pl.CostEstimate(
            flops=flops,
            transcendentals=0,
            bytes_accessed=2 * width * (window_count * (rows_left + visit_rows) + lag_count)
            + 4 * visit_rows * rows_left * lag_count,
        ),
    )(*[(left_pieces, visit_pieces)[kind][index] for kind, index in issue_order], left_perm, visit_perm, lag_table)


def xor_gather(block, axis_name, size):
    if size & (size - 1):
        return [lax.all_gather(block, axis_name, axis=1, tiled=True)], None
    pieces = [block]
    for step in range(1, size):
        pairs = [(source, source ^ step) for source in range(size)]
        pieces.append(lax.ppermute(block, axis_name, pairs))
    order = lax.axis_index(axis_name) ^ jnp.arange(size, dtype=jnp.int32)
    return pieces, order


def chip_gather(block, axis_name, size):
    if size < 4 or size & (size - 1):
        return xor_gather(block, axis_name, size)
    chips = size // 2
    fetched = []
    for step in range(1, chips):
        pairs = [(source, source ^ (2 * step)) for source in range(size)]
        fetched.append(lax.ppermute(block, axis_name, pairs))
    partner = [(source, source ^ 1) for source in range(size)]
    pieces = [block, lax.ppermute(block, axis_name, partner)]
    piece = block.shape[1]
    swapped = lax.ppermute(jnp.concatenate(fetched, axis=1), axis_name, partner)
    for step in range(1, chips):
        pieces.append(fetched[step - 1])
        pieces.append(swapped[:, (step - 1) * piece:step * piece, :])
    order = lax.axis_index(axis_name) ^ jnp.arange(size, dtype=jnp.int32)
    return pieces, order


def on_device(records, fir_taps, lag_limit):
    block_size = records.shape[0]
    decimated = decimate(records, fir_taps)
    out_length = decimated.shape[-1]
    bin_count = out_length // 2
    spec_real, spec_imag = spectrum(decimated)
    white = whiten(spec_real, spec_imag)
    white_by_window = jnp.moveaxis(white, 1, 0)
    col_size = lax.axis_size("col")
    row_size = lax.axis_size("row")
    left_by_window, left_order = xor_gather(white_by_window, "col", col_size)
    step = out_length // BAND
    cos_hi, sin_hi = angle_table(LAGS, bin_count // BAND, step, -LH)
    cos_lo, sin_lo = angle_table(LAGS, BAND, out_length, -LH)
    cos_lag = (cos_hi[:, :, None] * cos_lo[:, None, :] - sin_hi[:, :, None] * sin_lo[:, None, :]).reshape(LAGS, bin_count)
    sin_lag = (sin_hi[:, :, None] * cos_lo[:, None, :] + cos_hi[:, :, None] * sin_lo[:, None, :]).reshape(LAGS, bin_count)
    lag_table = jnp.concatenate([cos_lag.T, sin_lag.T], axis=0).astype(jnp.bfloat16)
    group_rows = sum(piece.shape[1] for piece in left_by_window)
    piece_rows, visit_order = chip_gather(white_by_window, "row", row_size)
    visit_count = sum(piece.shape[1] for piece in piece_rows)
    late_first = [(1, index) for index in range(len(piece_rows)) if index > 1 and index % 2 == 1]
    near = [(0, 0), (1, 0), (0, 1), (1, 1)][:2 + min(1, len(left_by_window) - 1) + min(1, len(piece_rows) - 1)]
    fetches = [(1, index) for index in range(len(piece_rows)) if index > 1 and index % 2 == 0]
    far = [(0, index) for index in range(2, len(left_by_window))]
    issue_order = [slot for slot in late_first + near[:2] + near[3:] + fetches[:1] + near[2:3] + fetches[1:] + far[::-1]]
    issue_order = sorted(set(issue_order), key=issue_order.index)
    assert len(issue_order) == len(left_by_window) + len(piece_rows)
    piece = block_size
    left_pos = jnp.arange(group_rows, dtype=jnp.int32)
    visit_pos = jnp.arange(visit_count, dtype=jnp.int32)
    if left_order is not None:
        left_pos = left_order[left_pos // piece] * piece + left_pos % piece
    if visit_order is not None:
        visit_pos = visit_order[visit_pos // piece] * piece + visit_pos % piece
    left_perm = (jnp.arange(group_rows)[None, :] == left_pos[:, None]).astype(jnp.bfloat16)
    visit_perm = (jnp.arange(visit_count)[None, :] == visit_pos[:, None]).astype(jnp.bfloat16)
    pair = pair_block(left_by_window, piece_rows, left_perm, visit_perm, lag_table, issue_order)
    pair = jnp.swapaxes(pair.reshape(visit_count, group_rows, LAGS), 0, 1)
    norm_scale = 1.0 / math.sqrt(white.shape[1] * bin_count)
    pair = pair * norm_scale
    lag_offset = jnp.abs(jnp.arange(LAGS, dtype=jnp.int32) - LH)
    keep_mask = lag_offset[None, :] <= lag_limit[:, None]
    tile_stack = jnp.where(keep_mask[:, None, :], pair, 0.0)
    return tile_stack[:, None]


def solution(mesh):
    placed = (P(("row", "col"), None, None), P(), P("row"))
    return jax.shard_map(
        on_device,
        mesh=mesh,
        in_specs=placed,
        out_specs=P("row", "col", None, None),
        check_vma=False,
    )
```
